32 devices in a mesh: dp: 4 (over z), ctx: 2 (over y), head: 4 (over x, core).
Axes of the slice: x: 2, y: 2, z: 4, core: 2. Of those that a mesh axis runs over, the one named last changes fastest.
Arguments:
- hidden_in: bfloat16 [3072, 4096], P(('dp', 'ctx')), may hold values from -6 to 6
- w_query: bfloat16 [4096, 4096], P(('dp', 'ctx'), 'head'), may hold values from -0.09375 to 0.09375
- w_key: bfloat16 [4096, 512], P(('dp', 'ctx'), 'head'), may hold values from -0.09375 to 0.09375
- w_value: bfloat16 [4096, 512], P(('dp', 'ctx'), 'head'), may hold values from -0.09375 to 0.09375
- lengths: int32 [4, 8], P('dp'), may hold values from 1 to 384, 768 in all within a row
- attn_grad: bfloat16 [3072, 4096], P(('dp', 'ctx'), 'head'), may hold values from -6 to 6
Outputs:
- attended: bfloat16 [3072, 4096], P(('dp', 'ctx'), 'head')
- grad_input: bfloat16 [3072, 4096], P(('dp', 'ctx'), 'head')
- grad_query_w: float32 [4096, 4096], P(('dp', 'ctx'), 'head')
- grad_key_w: float32 [4096, 512], P(('dp', 'ctx'), 'head')
- grad_value_w: float32 [4096, 512], P(('dp', 'ctx'), 'head')
The draws below stay inside these ranges and needn't reach their ends.
Inputs may be any that keep to these rules, and one draw needn't show every extreme that they name: `lengths`: each row sums to 768; the longest document of every row has exactly 384 positions.
All inputs are finite; a program needn't handle non-finite values.
Results may differ from the reference program's by a relative error of at most 0.018.
Values may be sent and summed in bfloat16 or wider, within the bound.
No kernel may reach another device: no remote copies, remote signals or barrier semaphores. Data moves between devices by JAX's collectives and lax.ppermute only.
A program may use at most 128 MiB of HBM per device.

```python
import math
import jax
import jax.numpy as jnp
import numpy as np
from jax import lax

D = 4096
HD = 128
KV_HEADS = 4
Q_HEADS = 32
LENGTH = 768
SEQS = 4
TOKENS = 3072
DOCS = 8
MOST = 384


def draw_hidden_in(key, part):
    first_key = jax.random.fold_in(key, 0)
    shape = (SEQS * LENGTH, D)
    return jnp.clip(jax.random.normal(first_key, shape, jnp.float32), -6.0, 6.0).astype(jnp.bfloat16)


def level_of(key, extent, cuts, smallest, top_value):
    def one(dim, shards_of):
        heights = jax.random.uniform(jax.random.fold_in(jax.random.fold_in(key, 6), dim), (shards_of,), jnp.float32, smallest / len(cuts), top_value / len(cuts))
        return jnp.repeat(jnp.exp(heights), extent[dim] // shards_of).reshape((-1,) + (1,) * (len(extent) - dim - 1))

    factor_of = one(*cuts[0])
    for cut in cuts[1:]:
        factor_of = factor_of * one(*cut)
    return factor_of


def split_up(number_of, total, bound, skew):
    portions = [(1 << 20) // math.isqrt(standing ** skew) + 1 for standing in range(2, number_of + 1)]
    rest, counts = total - bound - (number_of - 1), [1] * (number_of - 1)
    while rest > 0:
        movable = [i for i in range(number_of - 1) if counts[i] < bound]
        pool, budget = sum([portions[i] for i in movable]), rest
        for i in movable:
            extra = min(bound - counts[i], max(1, budget * portions[i] // pool), rest)
            counts[i] = counts[i] + extra
            rest = rest - extra
    return np.array([bound] + counts)


def ragged(key, number_of, total, most, slope):
    if number_of == 2:
        one = jax.random.randint(key, (), max(1, total - most), min(most, total - 1) + 1)
        return jnp.stack([one, total - one])
    sizes = jnp.asarray(split_up(number_of, total, most, slope), jnp.int32)
    pairs = (number_of - 1) // 2
    source_of, receiver = sizes[1:1 + 2 * pairs:2], sizes[2:2 + 2 * pairs:2]
    margin = jnp.minimum(source_of - 1, most - receiver)
    shifted = jax.random.randint(jax.random.fold_in(key, 1), (pairs,), 0, 1 << 20) % (margin + 1)
    sizes = sizes.at[1:1 + 2 * pairs:2].set(source_of - shifted).at[2:2 + 2 * pairs:2].set(receiver + shifted)
    return sizes[jax.random.permutation(jax.random.fold_in(key, 2), number_of)]


def centred(stream_key, extent, spread, reach, cuts=(), kind=jnp.bfloat16):
    values = spread * jax.random.normal(stream_key, extent, jnp.float32)
    if cuts:
        values = values * level_of(stream_key, extent, cuts, -0.22, 0.18)
    return jnp.clip(values, -reach, reach).astype(kind)


def setup_inputs(seed: int = 0) -> dict:
    key_of = jax.random.split(jax.random.key(seed), 7)
    hidden_in = draw_hidden_in(jax.random.fold_in(key_of[6], 71), 0)
    w_query = centred(key_of[1], (D, Q_HEADS * HD), D ** -0.5, 0.09375, ((0, 8), (1, 4)))
    w_key = centred(key_of[2], (D, KV_HEADS * HD), D ** -0.5, 0.09375, ((0, 8), (1, 4)))
    w_value = centred(key_of[3], (D, KV_HEADS * HD), D ** -0.5, 0.09375, ((0, 8), (1, 4)))
    lengths = jax.vmap(lambda own: ragged(own, DOCS, LENGTH, MOST, 2))(jax.random.split(key_of[4], SEQS)).reshape((SEQS, DOCS)).astype(jnp.int32)
    attn_grad = centred(key_of[5], (TOKENS, Q_HEADS * HD), 1.0, 6.0, ((0, 8), (1, 4)))
    return {"hidden_in": hidden_in, "w_query": w_query, "w_key": w_key, "w_value": w_value, "lengths": lengths, "attn_grad": attn_grad}


scale_factor = 128.0 ** -0.5
neg_large = -1.0e30


def rope_tables(positions):
    inverse = jnp.power(500000.0, -jnp.arange(64, dtype=jnp.float32) / 64.0)
    angles = positions.astype(jnp.float32)[:, None] * inverse[None, :]
    return jnp.cos(angles)[:, None, :], jnp.sin(angles)[:, None, :]


def rotate(entries, cosine, sine_table):
    first_half = entries[..., :64]
    second_half = entries[..., 64:]
    return jnp.concatenate([first_half * cosine - second_half * sine_table, second_half * cosine + first_half * sine_table], -1)


def unrotate(entries, cosine, sine_table):
    first_half = entries[..., :64]
    second_half = entries[..., 64:]
    return jnp.concatenate([first_half * cosine + second_half * sine_table, second_half * cosine - first_half * sine_table], -1)


def segment_ids(length_row, positions):
    ends = jnp.cumsum(length_row)
    return jnp.sum((positions[:, None] >= ends[None, :]).astype(jnp.int32), 1).astype(jnp.int32)


def pair_attention(operands):
    query_g, key_g, value_g, dout_g, seg_g = operands
    high = lax.Precision.HIGHEST
    positions = jnp.arange(query_g.shape[0], dtype=jnp.int32)
    scores = jnp.einsum("rhd,kd->hrk", query_g.astype(jnp.float32), key_g.astype(jnp.float32), precision=high) * scale_factor
    allowed = ((positions[None, :] <= positions[:, None]) & (seg_g[None, :] == seg_g[:, None]))[None]
    masked = jnp.where(allowed, scores, neg_large)
    top_score = jnp.max(masked, -1)
    total = jnp.sum(jnp.where(allowed, jnp.exp(masked - top_score[..., None]), 0.0), -1)
    log_total = top_score + jnp.log(total)
    prob_rows = jnp.where(allowed, jnp.exp(jnp.where(allowed, scores - log_total[..., None], neg_large)), 0.0)
    prob_b = prob_rows.astype(jnp.bfloat16)
    attended = jnp.einsum("hrk,kd->rhd", prob_b.astype(jnp.float32), value_g.astype(jnp.float32), precision=high).astype(jnp.bfloat16)
    delta_rows = jnp.einsum("rhd,rhd->hr", dout_g.astype(jnp.float32), attended.astype(jnp.float32), precision=high)
    grad_v = jnp.einsum("hrk,rhd->kd", prob_b.astype(jnp.float32), dout_g.astype(jnp.float32), precision=high)
    d_prob = jnp.einsum("rhd,kd->hrk", dout_g.astype(jnp.float32), value_g.astype(jnp.float32), precision=high)
    d_score = (scale_factor * prob_rows * (d_prob - delta_rows[..., None])).astype(jnp.bfloat16)
    grad_q = jnp.einsum("hrk,kd->rhd", d_score.astype(jnp.float32), key_g.astype(jnp.float32), precision=high)
    grad_k = jnp.einsum("hrk,rhd->kd", d_score.astype(jnp.float32), query_g.astype(jnp.float32), precision=high)
    return attended, grad_q, grad_k, grad_v


def reference(hidden_in, w_query, w_key, w_value, lengths, attn_grad):
    heads_all = w_query.shape[1] // 128
    groups = w_key.shape[1] // 128
    per_group = heads_all // groups
    proj_q = jnp.dot(hidden_in, w_query, preferred_element_type=jnp.float32)
    proj_k = jnp.dot(hidden_in, w_key, preferred_element_type=jnp.float32)
    proj_v = jnp.dot(hidden_in, w_value, preferred_element_type=jnp.float32)
    positions = jnp.arange(LENGTH, dtype=jnp.int32)
    cosine, sine_table = rope_tables(positions)
    query_rows = rotate(proj_q.reshape(SEQS, LENGTH, heads_all, 128), cosine, sine_table).astype(jnp.bfloat16)
    key_rows = rotate(proj_k.reshape(SEQS, LENGTH, groups, 128), cosine, sine_table).astype(jnp.bfloat16)
    value_rows = proj_v.astype(jnp.bfloat16).reshape(SEQS, LENGTH, groups, 128)
    dout_rows = attn_grad.reshape(SEQS, LENGTH, heads_all, 128)
    seg_rows = jax.vmap(lambda row: segment_ids(row, positions))(lengths)
    query_p = query_rows.reshape(SEQS, LENGTH, groups, per_group, 128).transpose(0, 2, 1, 3, 4).reshape(SEQS * groups, LENGTH, per_group, 128)
    dout_p = dout_rows.reshape(SEQS, LENGTH, groups, per_group, 128).transpose(0, 2, 1, 3, 4).reshape(SEQS * groups, LENGTH, per_group, 128)
    key_p = key_rows.transpose(0, 2, 1, 3).reshape(SEQS * groups, LENGTH, 128)
    value_p = value_rows.transpose(0, 2, 1, 3).reshape(SEQS * groups, LENGTH, 128)
    seg_p = jnp.repeat(seg_rows, groups, axis=0)
    attended, grad_q, grad_k, grad_v = lax.map(pair_attention, (query_p, key_p, value_p, dout_p, seg_p))
    attended = attended.reshape(SEQS, groups, LENGTH, per_group, 128).transpose(0, 2, 1, 3, 4).reshape(SEQS * LENGTH, heads_all * 128)
    grad_q = grad_q.reshape(SEQS, groups, LENGTH, per_group, 128).transpose(0, 2, 1, 3, 4).reshape(SEQS, LENGTH, heads_all, 128)
    grad_k = grad_k.reshape(SEQS, groups, LENGTH, 128).transpose(0, 2, 1, 3)
    grad_v = grad_v.reshape(SEQS, groups, LENGTH, 128).transpose(0, 2, 1, 3)
    d_query = unrotate(grad_q, cosine, sine_table).astype(jnp.bfloat16).reshape(SEQS * LENGTH, heads_all * 128)
    d_key = unrotate(grad_k, cosine, sine_table).astype(jnp.bfloat16).reshape(SEQS * LENGTH, groups * 128)
    d_value = grad_v.astype(jnp.bfloat16).reshape(SEQS * LENGTH, groups * 128)
    grad_input = jnp.dot(d_query, w_query.T, preferred_element_type=jnp.float32)
    grad_input = grad_input + jnp.dot(d_key, w_key.T, preferred_element_type=jnp.float32)
    grad_input = (grad_input + jnp.dot(d_value, w_value.T, preferred_element_type=jnp.float32)).astype(jnp.bfloat16)
    grad_query_w = jnp.dot(hidden_in.T, d_query, preferred_element_type=jnp.float32)
    grad_key_w = jnp.dot(hidden_in.T, d_key, preferred_element_type=jnp.float32)
    grad_value_w = jnp.dot(hidden_in.T, d_value, preferred_element_type=jnp.float32)
    return attended, grad_input, grad_query_w, grad_key_w, grad_value_w
```

```python
import jax
import jax.numpy as jnp
from jax import lax
from jax.sharding import PartitionSpec as P

scale_factor = 128.0 ** (-0.5)
neg_large = -1e30


def rope_tables(positions):
    inverse = jnp.power(500000.0, -jnp.arange(64, dtype=jnp.float32) / 64.0)
    angles = positions.astype(jnp.float32)[:, None] * inverse[None, :]
    return (jnp.cos(angles)[:, None, :], jnp.sin(angles)[:, None, :])


def rotate(entries, cosine, sine_table):
    first_half = entries[..., :64]
    second_half = entries[..., 64:]
    return jnp.concatenate(
        [
            first_half * cosine - second_half * sine_table,
            second_half * cosine + first_half * sine_table,
        ],
        -1,
    )


def unrotate(entries, cosine, sine_table):
    first_half = entries[..., :64]
    second_half = entries[..., 64:]
    return jnp.concatenate(
        [
            first_half * cosine + second_half * sine_table,
            second_half * cosine - first_half * sine_table,
        ],
        -1,
    )


def segment_ids(length_row, positions):
    ends = jnp.cumsum(length_row)
    return jnp.sum((positions[:, None] >= ends[None, :]).astype(jnp.int32), 1)


def block_scores(query_blk, key_blk, query_pos, key_pos, query_seg, key_seg):
    scores = (
        jnp.einsum("rhd,kd->hrk", query_blk, key_blk, preferred_element_type=jnp.float32)
        * scale_factor
    )
    allowed = (key_pos[None, :] <= query_pos[:, None]) & (key_seg[None, :] == query_seg[:, None])
    return (scores, allowed[None])


def grad_block(
    query_blk,
    dout_blk,
    total_blk,
    delta_blk,
    key_blk,
    value_blk,
    query_pos,
    key_pos,
    query_seg,
    key_seg,
):
    scores, allowed = block_scores(query_blk, key_blk, query_pos, key_pos, query_seg, key_seg)
    prob_rows = jnp.where(
        allowed, jnp.exp(jnp.where(allowed, scores - total_blk[..., None], neg_large)), 0.0
    )
    prob_b = prob_rows.astype(jnp.bfloat16)
    d_prob = jnp.einsum("rhd,kd->hrk", dout_blk, value_blk, preferred_element_type=jnp.float32)
    d_score = (scale_factor * prob_rows * (d_prob - delta_blk[..., None])).astype(jnp.bfloat16)
    return (prob_b, d_score)


def attend_whole(query_rows, key_all, value_all, dout_rows, positions, all_pos, seg_own, seg_all):
    scores, allowed = block_scores(query_rows, key_all, positions, all_pos, seg_own, seg_all)
    masked = jnp.where(allowed, scores, neg_large)
    top_score = jnp.max(masked, -1)
    total = jnp.sum(jnp.where(allowed, jnp.exp(masked - top_score[..., None]), 0.0), -1)
    log_total = top_score + jnp.log(total)
    prob_rows = jnp.where(
        allowed, jnp.exp(jnp.where(allowed, scores - log_total[..., None], neg_large)), 0.0
    )
    prob_b = prob_rows.astype(jnp.bfloat16)
    out_rows = jnp.einsum(
        "hrk,kd->rhd", prob_b, value_all, preferred_element_type=jnp.float32
    ).astype(jnp.bfloat16)
    delta_rows = jnp.einsum("rhd,rhd->hr", dout_rows, out_rows, preferred_element_type=jnp.float32)
    d_prob = jnp.einsum("rhd,kd->hrk", dout_rows, value_all, preferred_element_type=jnp.float32)
    d_score = (scale_factor * prob_rows * (d_prob - delta_rows[..., None])).astype(jnp.bfloat16)
    grad_q = jnp.einsum("hrk,kd->rhd", d_score, key_all, preferred_element_type=jnp.float32)
    part_k = jnp.einsum("hrk,rhd->kd", d_score, query_rows, preferred_element_type=jnp.float32)
    part_v = jnp.einsum("hrk,rhd->kd", prob_b, dout_rows, preferred_element_type=jnp.float32)
    return out_rows, grad_q, part_k, part_v


def attend_blocked(query_rows, key_all, value_all, dout_rows, positions, all_pos, seg_own, seg_all, kblock):
    num_rows, head_count = query_rows.shape[0], query_rows.shape[1]
    seq_len = key_all.shape[0]
    causal_limit = (positions[-1] + kblock) // kblock
    key_first = jnp.int32(0)

    def take_block(block_index):
        first_row = block_index * kblock
        return (
            lax.dynamic_slice_in_dim(key_all, first_row, kblock, 0),
            lax.dynamic_slice_in_dim(value_all, first_row, kblock, 0),
            lax.dynamic_slice_in_dim(all_pos, first_row, kblock, 0),
            lax.dynamic_slice_in_dim(seg_all, first_row, kblock, 0),
        )

    def stats_step(block_index, carried):
        run_max, run_sum = carried
        key_blk, value_blk, key_pos, key_seg = take_block(block_index)
        scores, allowed = block_scores(query_rows, key_blk, positions, key_pos, seg_own, key_seg)
        masked = jnp.where(allowed, scores, neg_large)
        new_max = jnp.maximum(run_max, jnp.max(masked, -1))
        terms = jnp.where(allowed, jnp.exp(masked - new_max[..., None]), 0.0)
        return (new_max, run_sum * jnp.exp(run_max - new_max) + jnp.sum(terms, -1))

    start_stats = (
        jnp.full((head_count, num_rows), neg_large, jnp.float32),
        jnp.zeros((head_count, num_rows), jnp.float32),
    )
    run_max, run_sum = lax.fori_loop(key_first, causal_limit, stats_step, start_stats)
    log_total = run_max + jnp.log(run_sum)

    def output_step(block_index, carried):
        key_blk, value_blk, key_pos, key_seg = take_block(block_index)
        scores, allowed = block_scores(query_rows, key_blk, positions, key_pos, seg_own, key_seg)
        prob_b = jnp.where(
            allowed, jnp.exp(jnp.where(allowed, scores - log_total[..., None], neg_large)), 0.0
        ).astype(jnp.bfloat16)
        return carried + jnp.einsum(
            "hrk,kd->rhd", prob_b, value_blk, preferred_element_type=jnp.float32
        )

    out_sum = lax.fori_loop(
        key_first, causal_limit, output_step, jnp.zeros((num_rows, head_count, 128), jnp.float32)
    )
    out_rows = out_sum.astype(jnp.bfloat16)
    delta_rows = jnp.einsum("rhd,rhd->hr", dout_rows, out_rows, preferred_element_type=jnp.float32)

    def sums_step(block_index, carried):
        grad_q, part_k, part_v = carried
        first_row = block_index * kblock
        key_blk, value_blk, key_pos, key_seg = take_block(block_index)
        prob_b, d_score = grad_block(
            query_rows, dout_rows, log_total, delta_rows, key_blk, value_blk,
            positions, key_pos, seg_own, key_seg,
        )
        grad_q = grad_q + jnp.einsum(
            "hrk,kd->rhd", d_score, key_blk, preferred_element_type=jnp.float32
        )
        block_k = jnp.einsum("hrk,rhd->kd", d_score, query_rows, preferred_element_type=jnp.float32)
        block_v = jnp.einsum("hrk,rhd->kd", prob_b, dout_rows, preferred_element_type=jnp.float32)
        part_k = lax.dynamic_update_slice_in_dim(
            part_k, lax.dynamic_slice_in_dim(part_k, first_row, kblock, 0) + block_k, first_row, 0
        )
        part_v = lax.dynamic_update_slice_in_dim(
            part_v, lax.dynamic_slice_in_dim(part_v, first_row, kblock, 0) + block_v, first_row, 0
        )
        return (grad_q, part_k, part_v)

    start_sums = (
        jnp.zeros((num_rows, head_count, 128), jnp.float32),
        jnp.zeros((seq_len, 128), jnp.float32),
        jnp.zeros((seq_len, 128), jnp.float32),
    )
    grad_q, part_k, part_v = lax.fori_loop(key_first, causal_limit, sums_step, start_sums)
    return out_rows, grad_q, part_k, part_v


def local(hidden_in, w_query, w_key, w_value, lengths, attn_grad):
    num_rows = hidden_in.shape[0]
    head_count = w_query.shape[1] // 128
    query_cols = head_count * 128
    start_row = lax.axis_index("ctx") * num_rows
    seq_len = num_rows * lax.axis_size("ctx")
    positions = start_row + jnp.arange(num_rows, dtype=jnp.int32)
    all_pos = jnp.arange(seq_len, dtype=jnp.int32)
    seg_all = segment_ids(lengths[0], all_pos)
    seg_own = lax.dynamic_slice_in_dim(seg_all, start_row, num_rows)
    cosine, sine_table = rope_tables(positions)
    rows_axes = ("dp", "ctx")
    hidden_cols = lax.all_to_all(hidden_in, rows_axes, 1, 0, tiled=True)
    local_w = jnp.concatenate([w_query, w_key, w_value], 1)
    full_w = lax.all_gather(local_w, rows_axes, axis=0, tiled=True)
    projected = jnp.dot(hidden_in, full_w, preferred_element_type=jnp.float32)
    query_rows = rotate(
        projected[:, :query_cols].reshape(num_rows, head_count, 128), cosine, sine_table
    ).astype(jnp.bfloat16)
    key_rows = rotate(
        projected[:, query_cols : query_cols + 128].reshape(num_rows, 1, 128), cosine, sine_table
    )[:, 0, :].astype(jnp.bfloat16)
    value_rows = projected[:, query_cols + 128 :].astype(jnp.bfloat16)
    key_all, value_all = (
        lax.all_gather(key_rows, "ctx", axis=0, tiled=True),
        lax.all_gather(value_rows, "ctx", axis=0, tiled=True),
    )
    dout_rows = attn_grad.reshape(num_rows, head_count, 128)
    operands = (query_rows, key_all, value_all, dout_rows, positions, all_pos, seg_own, seg_all)
    if head_count * num_rows * seq_len <= (1 << 22):
        out_rows, grad_q, part_k, part_v = attend_whole(*operands)
    else:
        kblock = seq_len
        while head_count * num_rows * kblock > (1 << 22) and kblock % 256 == 0:
            kblock //= 2
        out_rows, grad_q, part_k, part_v = attend_blocked(*operands, kblock)
    attended = out_rows.reshape(num_rows, query_cols)
    grad_k, grad_v = (
        lax.psum_scatter(part_k, "ctx", scatter_dimension=0, tiled=True),
        lax.psum_scatter(part_v, "ctx", scatter_dimension=0, tiled=True),
    )
    d_query = (
        unrotate(grad_q, cosine, sine_table).astype(jnp.bfloat16).reshape(num_rows, query_cols)
    )
    d_key = unrotate(grad_k[:, None, :], cosine, sine_table)[:, 0, :].astype(jnp.bfloat16)
    d_value = grad_v.astype(jnp.bfloat16)
    d_proj = jnp.concatenate([d_query, d_key, d_value], 1)
    input_part = lax.dot_general(
        d_proj, full_w, (((1,), (1,)), ((), ())), preferred_element_type=jnp.float32
    )
    grad_input = lax.psum_scatter(input_part, "head", scatter_dimension=1, tiled=True).astype(
        jnp.bfloat16
    )
    d_proj_all = lax.all_gather(d_proj, rows_axes, axis=0, tiled=True)
    weight_sum = lax.dot_general(
        hidden_cols, d_proj_all, (((0,), (0,)), ((), ())), preferred_element_type=jnp.float32
    )
    return (
        attended,
        grad_input,
        weight_sum[:, :query_cols],
        weight_sum[:, query_cols : query_cols + 128],
        weight_sum[:, query_cols + 128 :],
    )


def solution(mesh):
    placed = (
        P(("dp", "ctx"), None),
        P(("dp", "ctx"), "head"),
        P(("dp", "ctx"), "head"),
        P(("dp", "ctx"), "head"),
        P("dp", None),
        P(("dp", "ctx"), "head"),
    )
    return jax.shard_map(
        local,
        mesh=mesh,
        in_specs=placed,
        out_specs=(
            P(("dp", "ctx"), "head"),
            P(("dp", "ctx"), "head"),
            P(("dp", "ctx"), "head"),
            P(("dp", "ctx"), "head"),
            P(("dp", "ctx"), "head"),
        ),
        check_vma=False,
    )
```

```python
import jax
import jax.numpy as jnp
from jax import lax
from jax.sharding import PartitionSpec as P

scale_factor = 128.0 ** (-0.5)
neg_large = -1e30


def rope_tables(positions):
    inverse = jnp.power(500000.0, -jnp.arange(64, dtype=jnp.float32) / 64.0)
    angles = positions.astype(jnp.float32)[:, None] * inverse[None, :]
    return (jnp.cos(angles)[:, None, :], jnp.sin(angles)[:, None, :])


def rotate(entries, cosine, sine_table):
    first_half = entries[..., :64]
    second_half = entries[..., 64:]
    return jnp.concatenate(
        [
            first_half * cosine - second_half * sine_table,
            second_half * cosine + first_half * sine_table,
        ],
        -1,
    )


def unrotate(entries, cosine, sine_table):
    first_half = entries[..., :64]
    second_half = entries[..., 64:]
    return jnp.concatenate(
        [
            first_half * cosine + second_half * sine_table,
            second_half * cosine - first_half * sine_table,
        ],
        -1,
    )


def segment_ids(length_row, positions):
    ends = jnp.cumsum(length_row)
    return jnp.sum((positions[:, None] >= ends[None, :]).astype(jnp.int32), 1)


def block_scores(query_blk, key_blk, query_pos, key_pos, query_seg, key_seg):
    scores = (
        jnp.einsum("rhd,kd->hrk", query_blk, key_blk, preferred_element_type=jnp.float32)
        * scale_factor
    )
    allowed = (key_pos[None, :] <= query_pos[:, None]) & (key_seg[None, :] == query_seg[:, None])
    return (scores, allowed[None])


def grad_block(
    query_blk,
    dout_blk,
    total_blk,
    delta_blk,
    key_blk,
    value_blk,
    query_pos,
    key_pos,
    query_seg,
    key_seg,
):
    scores, allowed = block_scores(query_blk, key_blk, query_pos, key_pos, query_seg, key_seg)
    prob_rows = jnp.where(
        allowed, jnp.exp(jnp.where(allowed, scores - total_blk[..., None], neg_large)), 0.0
    )
    prob_b = prob_rows.astype(jnp.bfloat16)
    d_prob = jnp.einsum("rhd,kd->hrk", dout_blk, value_blk, preferred_element_type=jnp.float32)
    d_score = (scale_factor * prob_rows * (d_prob - delta_blk[..., None])).astype(jnp.bfloat16)
    return (prob_b, d_score)


def attend_whole(query_rows, key_all, value_all, dout_rows, positions, all_pos, seg_own, seg_all):
    scores, allowed = block_scores(query_rows, key_all, positions, all_pos, seg_own, seg_all)
    masked = jnp.where(allowed, scores, neg_large)
    top_score = jnp.max(masked, -1)
    total = jnp.sum(jnp.where(allowed, jnp.exp(masked - top_score[..., None]), 0.0), -1)
    log_total = top_score + jnp.log(total)
    prob_rows = jnp.where(
        allowed, jnp.exp(jnp.where(allowed, scores - log_total[..., None], neg_large)), 0.0
    )
    prob_b = prob_rows.astype(jnp.bfloat16)
    out_rows = jnp.einsum(
        "hrk,kd->rhd", prob_b, value_all, preferred_element_type=jnp.float32
    ).astype(jnp.bfloat16)
    delta_rows = jnp.einsum("rhd,rhd->hr", dout_rows, out_rows, preferred_element_type=jnp.float32)
    d_prob = jnp.einsum("rhd,kd->hrk", dout_rows, value_all, preferred_element_type=jnp.float32)
    d_score = (scale_factor * prob_rows * (d_prob - delta_rows[..., None])).astype(jnp.bfloat16)
    grad_q = jnp.einsum("hrk,kd->rhd", d_score, key_all, preferred_element_type=jnp.float32)
    part_k = jnp.einsum("hrk,rhd->kd", d_score, query_rows, preferred_element_type=jnp.float32)
    part_v = jnp.einsum("hrk,rhd->kd", prob_b, dout_rows, preferred_element_type=jnp.float32)
    return out_rows, grad_q, part_k, part_v


def attend_blocked(query_rows, key_all, value_all, dout_rows, positions, all_pos, seg_own, seg_all, kblock):
    num_rows, head_count = query_rows.shape[0], query_rows.shape[1]
    seq_len = key_all.shape[0]
    causal_limit = (positions[-1] + kblock) // kblock
    key_first = jnp.int32(0)

    def take_block(block_index):
        first_row = block_index * kblock
        return (
            lax.dynamic_slice_in_dim(key_all, first_row, kblock, 0),
            lax.dynamic_slice_in_dim(value_all, first_row, kblock, 0),
            lax.dynamic_slice_in_dim(all_pos, first_row, kblock, 0),
            lax.dynamic_slice_in_dim(seg_all, first_row, kblock, 0),
        )

    def stats_step(block_index, carried):
        run_max, run_sum = carried
        key_blk, value_blk, key_pos, key_seg = take_block(block_index)
        scores, allowed = block_scores(query_rows, key_blk, positions, key_pos, seg_own, key_seg)
        masked = jnp.where(allowed, scores, neg_large)
        new_max = jnp.maximum(run_max, jnp.max(masked, -1))
        terms = jnp.where(allowed, jnp.exp(masked - new_max[..., None]), 0.0)
        return (new_max, run_sum * jnp.exp(run_max - new_max) + jnp.sum(terms, -1))

    start_stats = (
        jnp.full((head_count, num_rows), neg_large, jnp.float32),
        jnp.zeros((head_count, num_rows), jnp.float32),
    )
    run_max, run_sum = lax.fori_loop(key_first, causal_limit, stats_step, start_stats)
    log_total = run_max + jnp.log(run_sum)

    def output_step(block_index, carried):
        key_blk, value_blk, key_pos, key_seg = take_block(block_index)
        scores, allowed = block_scores(query_rows, key_blk, positions, key_pos, seg_own, key_seg)
        prob_b = jnp.where(
            allowed, jnp.exp(jnp.where(allowed, scores - log_total[..., None], neg_large)), 0.0
        ).astype(jnp.bfloat16)
        return carried + jnp.einsum(
            "hrk,kd->rhd", prob_b, value_blk, preferred_element_type=jnp.float32
        )

    out_sum = lax.fori_loop(
        key_first, causal_limit, output_step, jnp.zeros((num_rows, head_count, 128), jnp.float32)
    )
    out_rows = out_sum.astype(jnp.bfloat16)
    delta_rows = jnp.einsum("rhd,rhd->hr", dout_rows, out_rows, preferred_element_type=jnp.float32)

    def sums_step(block_index, carried):
        grad_q, part_k, part_v = carried
        first_row = block_index * kblock
        key_blk, value_blk, key_pos, key_seg = take_block(block_index)
        prob_b, d_score = grad_block(
            query_rows, dout_rows, log_total, delta_rows, key_blk, value_blk,
            positions, key_pos, seg_own, key_seg,
        )
        grad_q = grad_q + jnp.einsum(
            "hrk,kd->rhd", d_score, key_blk, preferred_element_type=jnp.float32
        )
        block_k = jnp.einsum("hrk,rhd->kd", d_score, query_rows, preferred_element_type=jnp.float32)
        block_v = jnp.einsum("hrk,rhd->kd", prob_b, dout_rows, preferred_element_type=jnp.float32)
        part_k = lax.dynamic_update_slice_in_dim(
            part_k, lax.dynamic_slice_in_dim(part_k, first_row, kblock, 0) + block_k, first_row, 0
        )
        part_v = lax.dynamic_update_slice_in_dim(
            part_v, lax.dynamic_slice_in_dim(part_v, first_row, kblock, 0) + block_v, first_row, 0
        )
        return (grad_q, part_k, part_v)

    start_sums = (
        jnp.zeros((num_rows, head_count, 128), jnp.float32),
        jnp.zeros((seq_len, 128), jnp.float32),
        jnp.zeros((seq_len, 128), jnp.float32),
    )
    grad_q, part_k, part_v = lax.fori_loop(key_first, causal_limit, sums_step, start_sums)
    return out_rows, grad_q, part_k, part_v


def local(hidden_in, w_query, w_key, w_value, lengths, attn_grad):
    num_rows = hidden_in.shape[0]
    head_count = w_query.shape[1] // 128
    query_cols = head_count * 128
    start_row = lax.axis_index("ctx") * num_rows
    seq_len = num_rows * lax.axis_size("ctx")
    positions = start_row + jnp.arange(num_rows, dtype=jnp.int32)
    all_pos = jnp.arange(seq_len, dtype=jnp.int32)
    seg_all = segment_ids(lengths[0], all_pos)
    seg_own = lax.dynamic_slice_in_dim(seg_all, start_row, num_rows)
    cosine, sine_table = rope_tables(positions)
    rows_axes = ("dp", "ctx")
    group_count = lax.axis_size(rows_axes)
    head_groups = lax.axis_size("head")
    if num_rows % head_groups == 0:
        quarter = num_rows // head_groups
        own_rows = lax.dynamic_slice_in_dim(hidden_in, lax.axis_index("head") * quarter, quarter, 0)
        cols_part = lax.all_to_all(own_rows, rows_axes, 1, 0, tiled=True)
    else:
        cols_part = lax.all_to_all(hidden_in, rows_axes, 1, 0, tiled=True)
    local_w = jnp.concatenate([w_query, w_key, w_value], 1)
    full_w = lax.all_gather(local_w, rows_axes, axis=0, tiled=True)
    cols_part, full_w = lax.optimization_barrier((cols_part, full_w))
    if num_rows % head_groups == 0:
        cols_all = lax.all_gather(cols_part, "head", axis=0, tiled=False)
        hidden_cols = (
            cols_all.reshape(head_groups, group_count, quarter, -1)
            .transpose(1, 0, 2, 3)
            .reshape(group_count * num_rows, -1)
        )
    else:
        hidden_cols = cols_part
    projected = jnp.dot(hidden_in, full_w, preferred_element_type=jnp.float32)
    query_rows = rotate(
        projected[:, :query_cols].reshape(num_rows, head_count, 128), cosine, sine_table
    ).astype(jnp.bfloat16)
    key_rows = rotate(
        projected[:, query_cols : query_cols + 128].reshape(num_rows, 1, 128), cosine, sine_table
    )[:, 0, :].astype(jnp.bfloat16)
    value_rows = projected[:, query_cols + 128 :].astype(jnp.bfloat16)
    key_all, value_all = (
        lax.all_gather(key_rows, "ctx", axis=0, tiled=True),
        lax.all_gather(value_rows, "ctx", axis=0, tiled=True),
    )
    hidden_cols, attn_grad = lax.optimization_barrier((hidden_cols, attn_grad))
    dout_rows = attn_grad.reshape(num_rows, head_count, 128)
    operands = (query_rows, key_all, value_all, dout_rows, positions, all_pos, seg_own, seg_all)
    if head_count * num_rows * seq_len <= (1 << 22):
        out_rows, grad_q, part_k, part_v = attend_whole(*operands)
    else:
        kblock = seq_len
        while head_count * num_rows * kblock > (1 << 22) and kblock % 256 == 0:
            kblock //= 2
        out_rows, grad_q, part_k, part_v = attend_blocked(*operands, kblock)
    attended = out_rows.reshape(num_rows, query_cols)
    grad_k, grad_v = (
        lax.psum_scatter(part_k, "ctx", scatter_dimension=0, tiled=True),
        lax.psum_scatter(part_v, "ctx", scatter_dimension=0, tiled=True),
    )
    d_query = (
        unrotate(grad_q, cosine, sine_table).astype(jnp.bfloat16).reshape(num_rows, query_cols)
    )
    d_key = unrotate(grad_k[:, None, :], cosine, sine_table)[:, 0, :].astype(jnp.bfloat16)
    d_value = grad_v.astype(jnp.bfloat16)
    d_proj = jnp.concatenate([d_query, d_key, d_value], 1)
    input_part = lax.dot_general(
        d_proj, full_w, (((1,), (1,)), ((), ())), preferred_element_type=jnp.float32
    )
    grad_input = lax.psum_scatter(input_part, "head", scatter_dimension=1, tiled=True).astype(
        jnp.bfloat16
    )
    d_proj_all = lax.all_gather(d_proj, rows_axes, axis=0, tiled=True)
    weight_sum = lax.dot_general(
        hidden_cols, d_proj_all, (((0,), (0,)), ((), ())), preferred_element_type=jnp.float32
    )
    return (
        attended,
        grad_input,
        weight_sum[:, :query_cols],
        weight_sum[:, query_cols : query_cols + 128],
        weight_sum[:, query_cols + 128 :],
    )


def solution(mesh):
    placed = (
        P(("dp", "ctx"), None),
        P(("dp", "ctx"), "head"),
        P(("dp", "ctx"), "head"),
        P(("dp", "ctx"), "head"),
        P("dp", None),
        P(("dp", "ctx"), "head"),
    )
    return jax.shard_map(
        local,
        mesh=mesh,
        in_specs=placed,
        out_specs=(
            P(("dp", "ctx"), "head"),
            P(("dp", "ctx"), "head"),
            P(("dp", "ctx"), "head"),
            P(("dp", "ctx"), "head"),
            P(("dp", "ctx"), "head"),
        ),
        check_vma=False,
    )
```

```python
import jax
import jax.numpy as jnp
from jax import lax
from jax.sharding import PartitionSpec as P

scale_factor = 128.0 ** (-0.5)
neg_large = -1e30


def rope_tables(positions):
    inverse = jnp.power(500000.0, -jnp.arange(64, dtype=jnp.float32) / 64.0)
    angles = positions.astype(jnp.float32)[:, None] * inverse[None, :]
    return (jnp.cos(angles)[:, None, :], jnp.sin(angles)[:, None, :])


def rotate(entries, cosine, sine_table):
    first_half = entries[..., :64]
    second_half = entries[..., 64:]
    return jnp.concatenate(
        [
            first_half * cosine - second_half * sine_table,
            second_half * cosine + first_half * sine_table,
        ],
        -1,
    )


def unrotate(entries, cosine, sine_table):
    first_half = entries[..., :64]
    second_half = entries[..., 64:]
    return jnp.concatenate(
        [
            first_half * cosine + second_half * sine_table,
            second_half * cosine - first_half * sine_table,
        ],
        -1,
    )


def segment_ids(length_row, positions):
    ends = jnp.cumsum(length_row)
    return jnp.sum((positions[:, None] >= ends[None, :]).astype(jnp.int32), 1)


def block_scores(query_blk, key_blk, query_pos, key_pos, query_seg, key_seg):
    scores = (
        jnp.einsum("rhd,kd->hrk", query_blk, key_blk, preferred_element_type=jnp.float32)
        * scale_factor
    )
    allowed = (key_pos[None, :] <= query_pos[:, None]) & (key_seg[None, :] == query_seg[:, None])
    return (scores, allowed[None])


def grad_block(
    query_blk,
    dout_blk,
    total_blk,
    delta_blk,
    key_blk,
    value_blk,
    query_pos,
    key_pos,
    query_seg,
    key_seg,
):
    scores, allowed = block_scores(query_blk, key_blk, query_pos, key_pos, query_seg, key_seg)
    prob_rows = jnp.where(
        allowed, jnp.exp(jnp.where(allowed, scores - total_blk[..., None], neg_large)), 0.0
    )
    prob_b = prob_rows.astype(jnp.bfloat16)
    d_prob = jnp.einsum("rhd,kd->hrk", dout_blk, value_blk, preferred_element_type=jnp.float32)
    d_score = (scale_factor * prob_rows * (d_prob - delta_blk[..., None])).astype(jnp.bfloat16)
    return (prob_b, d_score)


def attend_whole(query_rows, key_all, value_all, dout_rows, positions, all_pos, seg_own, seg_all):
    scores, allowed = block_scores(query_rows, key_all, positions, all_pos, seg_own, seg_all)
    masked = jnp.where(allowed, scores, neg_large)
    top_score = jnp.max(masked, -1)
    total = jnp.sum(jnp.where(allowed, jnp.exp(masked - top_score[..., None]), 0.0), -1)
    log_total = top_score + jnp.log(total)
    prob_rows = jnp.where(
        allowed, jnp.exp(jnp.where(allowed, scores - log_total[..., None], neg_large)), 0.0
    )
    prob_b = prob_rows.astype(jnp.bfloat16)
    out_rows = jnp.einsum(
        "hrk,kd->rhd", prob_b, value_all, preferred_element_type=jnp.float32
    ).astype(jnp.bfloat16)
    delta_rows = jnp.einsum("rhd,rhd->hr", dout_rows, out_rows, preferred_element_type=jnp.float32)
    d_prob = jnp.einsum("rhd,kd->hrk", dout_rows, value_all, preferred_element_type=jnp.float32)
    d_score = (scale_factor * prob_rows * (d_prob - delta_rows[..., None])).astype(jnp.bfloat16)
    grad_q = jnp.einsum("hrk,kd->rhd", d_score, key_all, preferred_element_type=jnp.float32)
    part_k = jnp.einsum("hrk,rhd->kd", d_score, query_rows, preferred_element_type=jnp.float32)
    part_v = jnp.einsum("hrk,rhd->kd", prob_b, dout_rows, preferred_element_type=jnp.float32)
    return out_rows, grad_q, part_k, part_v


def attend_blocked(query_rows, key_all, value_all, dout_rows, positions, all_pos, seg_own, seg_all, kblock):
    num_rows, head_count = query_rows.shape[0], query_rows.shape[1]
    seq_len = key_all.shape[0]
    causal_limit = (positions[-1] + kblock) // kblock
    key_first = jnp.int32(0)

    def take_block(block_index):
        first_row = block_index * kblock
        return (
            lax.dynamic_slice_in_dim(key_all, first_row, kblock, 0),
            lax.dynamic_slice_in_dim(value_all, first_row, kblock, 0),
            lax.dynamic_slice_in_dim(all_pos, first_row, kblock, 0),
            lax.dynamic_slice_in_dim(seg_all, first_row, kblock, 0),
        )

    def stats_step(block_index, carried):
        run_max, run_sum = carried
        key_blk, value_blk, key_pos, key_seg = take_block(block_index)
        scores, allowed = block_scores(query_rows, key_blk, positions, key_pos, seg_own, key_seg)
        masked = jnp.where(allowed, scores, neg_large)
        new_max = jnp.maximum(run_max, jnp.max(masked, -1))
        terms = jnp.where(allowed, jnp.exp(masked - new_max[..., None]), 0.0)
        return (new_max, run_sum * jnp.exp(run_max - new_max) + jnp.sum(terms, -1))

    start_stats = (
        jnp.full((head_count, num_rows), neg_large, jnp.float32),
        jnp.zeros((head_count, num_rows), jnp.float32),
    )
    run_max, run_sum = lax.fori_loop(key_first, causal_limit, stats_step, start_stats)
    log_total = run_max + jnp.log(run_sum)

    def output_step(block_index, carried):
        key_blk, value_blk, key_pos, key_seg = take_block(block_index)
        scores, allowed = block_scores(query_rows, key_blk, positions, key_pos, seg_own, key_seg)
        prob_b = jnp.where(
            allowed, jnp.exp(jnp.where(allowed, scores - log_total[..., None], neg_large)), 0.0
        ).astype(jnp.bfloat16)
        return carried + jnp.einsum(
            "hrk,kd->rhd", prob_b, value_blk, preferred_element_type=jnp.float32
        )

    out_sum = lax.fori_loop(
        key_first, causal_limit, output_step, jnp.zeros((num_rows, head_count, 128), jnp.float32)
    )
    out_rows = out_sum.astype(jnp.bfloat16)
    delta_rows = jnp.einsum("rhd,rhd->hr", dout_rows, out_rows, preferred_element_type=jnp.float32)

    def sums_step(block_index, carried):
        grad_q, part_k, part_v = carried
        first_row = block_index * kblock
        key_blk, value_blk, key_pos, key_seg = take_block(block_index)
        prob_b, d_score = grad_block(
            query_rows, dout_rows, log_total, delta_rows, key_blk, value_blk,
            positions, key_pos, seg_own, key_seg,
        )
        grad_q = grad_q + jnp.einsum(
            "hrk,kd->rhd", d_score, key_blk, preferred_element_type=jnp.float32
        )
        block_k = jnp.einsum("hrk,rhd->kd", d_score, query_rows, preferred_element_type=jnp.float32)
        block_v = jnp.einsum("hrk,rhd->kd", prob_b, dout_rows, preferred_element_type=jnp.float32)
        part_k = lax.dynamic_update_slice_in_dim(
            part_k, lax.dynamic_slice_in_dim(part_k, first_row, kblock, 0) + block_k, first_row, 0
        )
        part_v = lax.dynamic_update_slice_in_dim(
            part_v, lax.dynamic_slice_in_dim(part_v, first_row, kblock, 0) + block_v, first_row, 0
        )
        return (grad_q, part_k, part_v)

    start_sums = (
        jnp.zeros((num_rows, head_count, 128), jnp.float32),
        jnp.zeros((seq_len, 128), jnp.float32),
        jnp.zeros((seq_len, 128), jnp.float32),
    )
    grad_q, part_k, part_v = lax.fori_loop(key_first, causal_limit, sums_step, start_sums)
    return out_rows, grad_q, part_k, part_v


def local(hidden_in, w_query, w_key, w_value, lengths, attn_grad):
    num_rows = hidden_in.shape[0]
    head_count = w_query.shape[1] // 128
    query_cols = head_count * 128
    start_row = lax.axis_index("ctx") * num_rows
    seq_len = num_rows * lax.axis_size("ctx")
    positions = start_row + jnp.arange(num_rows, dtype=jnp.int32)
    all_pos = jnp.arange(seq_len, dtype=jnp.int32)
    seg_all = segment_ids(lengths[0], all_pos)
    seg_own = lax.dynamic_slice_in_dim(seg_all, start_row, num_rows)
    cosine, sine_table = rope_tables(positions)
    rows_axes = ("dp", "ctx")
    group_count = lax.axis_size(rows_axes)
    head_groups = lax.axis_size("head")
    if num_rows % head_groups == 0:
        quarter = num_rows // head_groups
        own_rows = lax.dynamic_slice_in_dim(hidden_in, lax.axis_index("head") * quarter, quarter, 0)
        cols_part = lax.all_to_all(own_rows, rows_axes, 1, 0, tiled=True)
    else:
        cols_part = lax.all_to_all(hidden_in, rows_axes, 1, 0, tiled=True)
    local_w = jnp.concatenate([w_query, w_key, w_value], 1)
    full_w = lax.all_gather(local_w, rows_axes, axis=0, tiled=True)
    cols_part, full_w = lax.optimization_barrier((cols_part, full_w))
    if num_rows % head_groups == 0:
        cols_all = lax.all_gather(cols_part, "head", axis=0, tiled=False)
        hidden_cols = (
            cols_all.reshape(head_groups, group_count, quarter, -1)
            .transpose(1, 0, 2, 3)
            .reshape(group_count * num_rows, -1)
        )
    else:
        hidden_cols = cols_part
    projected = jnp.dot(hidden_in, full_w, preferred_element_type=jnp.float32)
    query_rows = rotate(
        projected[:, :query_cols].reshape(num_rows, head_count, 128), cosine, sine_table
    ).astype(jnp.bfloat16)
    key_rows = rotate(
        projected[:, query_cols : query_cols + 128].reshape(num_rows, 1, 128), cosine, sine_table
    )[:, 0, :].astype(jnp.bfloat16)
    value_rows = projected[:, query_cols + 128 :].astype(jnp.bfloat16)
    key_all, value_all = (
        lax.all_gather(key_rows, "ctx", axis=0, tiled=True),
        lax.all_gather(value_rows, "ctx", axis=0, tiled=True),
    )
    hidden_cols, attn_grad = lax.optimization_barrier((hidden_cols, attn_grad))
    dout_rows = attn_grad.reshape(num_rows, head_count, 128)
    operands = (query_rows, key_all, value_all, dout_rows, positions, all_pos, seg_own, seg_all)
    if head_count * num_rows * seq_len <= (1 << 22):
        out_rows, grad_q, part_k, part_v = attend_whole(*operands)
    else:
        kblock = seq_len
        while head_count * num_rows * kblock > (1 << 22) and kblock % 256 == 0:
            kblock //= 2
        out_rows, grad_q, part_k, part_v = attend_blocked(*operands, kblock)
    attended = out_rows.reshape(num_rows, query_cols)
    grad_k, grad_v = (
        lax.psum_scatter(part_k, "ctx", scatter_dimension=0, tiled=True),
        lax.psum_scatter(part_v, "ctx", scatter_dimension=0, tiled=True),
    )
    d_query = (
        unrotate(grad_q, cosine, sine_table).astype(jnp.bfloat16).reshape(num_rows, query_cols)
    )
    d_key = unrotate(grad_k[:, None, :], cosine, sine_table)[:, 0, :].astype(jnp.bfloat16)
    d_value = grad_v.astype(jnp.bfloat16)
    d_proj = jnp.concatenate([d_query, d_key, d_value], 1)
    input_part = lax.dot_general(
        d_proj, full_w, (((1,), (1,)), ((), ())), preferred_element_type=jnp.float32
    )
    input_cols = input_part.shape[1] // head_groups
    input_split = lax.all_to_all(
        input_part.reshape(num_rows, head_groups, input_cols), "head", 1, 1, tiled=False
    )
    grad_input = jnp.sum(input_split, axis=1).astype(jnp.bfloat16)
    d_proj_all = lax.all_gather(d_proj, rows_axes, axis=0, tiled=True)
    weight_sum = lax.dot_general(
        hidden_cols, d_proj_all, (((0,), (0,)), ((), ())), preferred_element_type=jnp.float32
    )
    return (
        attended,
        grad_input,
        weight_sum[:, :query_cols],
        weight_sum[:, query_cols : query_cols + 128],
        weight_sum[:, query_cols + 128 :],
    )


def solution(mesh):
    placed = (
        P(("dp", "ctx"), None),
        P(("dp", "ctx"), "head"),
        P(("dp", "ctx"), "head"),
        P(("dp", "ctx"), "head"),
        P("dp", None),
        P(("dp", "ctx"), "head"),
    )
    return jax.shard_map(
        local,
        mesh=mesh,
        in_specs=placed,
        out_specs=(
            P(("dp", "ctx"), "head"),
            P(("dp", "ctx"), "head"),
            P(("dp", "ctx"), "head"),
            P(("dp", "ctx"), "head"),
            P(("dp", "ctx"), "head"),
        ),
        check_vma=False,
    )
```

```python
import jax
import jax.numpy as jnp
from jax import lax
from jax.sharding import PartitionSpec as P

scale_factor = 128.0 ** (-0.5)
neg_large = -1e30


def rope_tables(positions):
    inverse = jnp.power(500000.0, -jnp.arange(64, dtype=jnp.float32) / 64.0)
    angles = positions.astype(jnp.float32)[:, None] * inverse[None, :]
    return (jnp.cos(angles)[:, None, :], jnp.sin(angles)[:, None, :])


def rotate(entries, cosine, sine_table):
    first_half = entries[..., :64]
    second_half = entries[..., 64:]
    return jnp.concatenate(
        [
            first_half * cosine - second_half * sine_table,
            second_half * cosine + first_half * sine_table,
        ],
        -1,
    )


def unrotate(entries, cosine, sine_table):
    first_half = entries[..., :64]
    second_half = entries[..., 64:]
    return jnp.concatenate(
        [
            first_half * cosine + second_half * sine_table,
            second_half * cosine - first_half * sine_table,
        ],
        -1,
    )


def segment_ids(length_row, positions):
    ends = jnp.cumsum(length_row)
    return jnp.sum((positions[:, None] >= ends[None, :]).astype(jnp.int32), 1)


def block_scores(query_blk, key_blk, query_pos, key_pos, query_seg, key_seg):
    scores = (
        jnp.einsum("rhd,kd->hrk", query_blk, key_blk, preferred_element_type=jnp.float32)
        * scale_factor
    )
    allowed = (key_pos[None, :] <= query_pos[:, None]) & (key_seg[None, :] == query_seg[:, None])
    return (scores, allowed[None])


def grad_block(
    query_blk,
    dout_blk,
    total_blk,
    delta_blk,
    key_blk,
    value_blk,
    query_pos,
    key_pos,
    query_seg,
    key_seg,
):
    scores, allowed = block_scores(query_blk, key_blk, query_pos, key_pos, query_seg, key_seg)
    prob_rows = jnp.where(
        allowed, jnp.exp(jnp.where(allowed, scores - total_blk[..., None], neg_large)), 0.0
    )
    prob_b = prob_rows.astype(jnp.bfloat16)
    d_prob = jnp.einsum("rhd,kd->hrk", dout_blk, value_blk, preferred_element_type=jnp.float32)
    d_score = (scale_factor * prob_rows * (d_prob - delta_blk[..., None])).astype(jnp.bfloat16)
    return (prob_b, d_score)


def attend_whole(query_rows, key_all, value_all, dout_rows, positions, all_pos, seg_own, seg_all):
    scores, allowed = block_scores(query_rows, key_all, positions, all_pos, seg_own, seg_all)
    masked = jnp.where(allowed, scores, neg_large)
    top_score = jnp.max(masked, -1)
    total = jnp.sum(jnp.where(allowed, jnp.exp(masked - top_score[..., None]), 0.0), -1)
    log_total = top_score + jnp.log(total)
    prob_rows = jnp.where(
        allowed, jnp.exp(jnp.where(allowed, scores - log_total[..., None], neg_large)), 0.0
    )
    prob_b = prob_rows.astype(jnp.bfloat16)
    out_rows = jnp.einsum(
        "hrk,kd->rhd", prob_b, value_all, preferred_element_type=jnp.float32
    ).astype(jnp.bfloat16)
    delta_rows = jnp.einsum("rhd,rhd->hr", dout_rows, out_rows, preferred_element_type=jnp.float32)
    d_prob = jnp.einsum("rhd,kd->hrk", dout_rows, value_all, preferred_element_type=jnp.float32)
    d_score = (scale_factor * prob_rows * (d_prob - delta_rows[..., None])).astype(jnp.bfloat16)
    grad_q = jnp.einsum("hrk,kd->rhd", d_score, key_all, preferred_element_type=jnp.float32)
    part_k = jnp.einsum("hrk,rhd->kd", d_score, query_rows, preferred_element_type=jnp.float32)
    part_v = jnp.einsum("hrk,rhd->kd", prob_b, dout_rows, preferred_element_type=jnp.float32)
    return out_rows, grad_q, part_k, part_v


def attend_blocked(query_rows, key_all, value_all, dout_rows, positions, all_pos, seg_own, seg_all, kblock):
    num_rows, head_count = query_rows.shape[0], query_rows.shape[1]
    seq_len = key_all.shape[0]
    causal_limit = (positions[-1] + kblock) // kblock
    key_first = jnp.int32(0)

    def take_block(block_index):
        first_row = block_index * kblock
        return (
            lax.dynamic_slice_in_dim(key_all, first_row, kblock, 0),
            lax.dynamic_slice_in_dim(value_all, first_row, kblock, 0),
            lax.dynamic_slice_in_dim(all_pos, first_row, kblock, 0),
            lax.dynamic_slice_in_dim(seg_all, first_row, kblock, 0),
        )

    def stats_step(block_index, carried):
        run_max, run_sum = carried
        key_blk, value_blk, key_pos, key_seg = take_block(block_index)
        scores, allowed = block_scores(query_rows, key_blk, positions, key_pos, seg_own, key_seg)
        masked = jnp.where(allowed, scores, neg_large)
        new_max = jnp.maximum(run_max, jnp.max(masked, -1))
        terms = jnp.where(allowed, jnp.exp(masked - new_max[..., None]), 0.0)
        return (new_max, run_sum * jnp.exp(run_max - new_max) + jnp.sum(terms, -1))

    start_stats = (
        jnp.full((head_count, num_rows), neg_large, jnp.float32),
        jnp.zeros((head_count, num_rows), jnp.float32),
    )
    run_max, run_sum = lax.fori_loop(key_first, causal_limit, stats_step, start_stats)
    log_total = run_max + jnp.log(run_sum)

    def output_step(block_index, carried):
        key_blk, value_blk, key_pos, key_seg = take_block(block_index)
        scores, allowed = block_scores(query_rows, key_blk, positions, key_pos, seg_own, key_seg)
        prob_b = jnp.where(
            allowed, jnp.exp(jnp.where(allowed, scores - log_total[..., None], neg_large)), 0.0
        ).astype(jnp.bfloat16)
        return carried + jnp.einsum(
            "hrk,kd->rhd", prob_b, value_blk, preferred_element_type=jnp.float32
        )

    out_sum = lax.fori_loop(
        key_first, causal_limit, output_step, jnp.zeros((num_rows, head_count, 128), jnp.float32)
    )
    out_rows = out_sum.astype(jnp.bfloat16)
    delta_rows = jnp.einsum("rhd,rhd->hr", dout_rows, out_rows, preferred_element_type=jnp.float32)

    def sums_step(block_index, carried):
        grad_q, part_k, part_v = carried
        first_row = block_index * kblock
        key_blk, value_blk, key_pos, key_seg = take_block(block_index)
        prob_b, d_score = grad_block(
            query_rows, dout_rows, log_total, delta_rows, key_blk, value_blk,
            positions, key_pos, seg_own, key_seg,
        )
        grad_q = grad_q + jnp.einsum(
            "hrk,kd->rhd", d_score, key_blk, preferred_element_type=jnp.float32
        )
        block_k = jnp.einsum("hrk,rhd->kd", d_score, query_rows, preferred_element_type=jnp.float32)
        block_v = jnp.einsum("hrk,rhd->kd", prob_b, dout_rows, preferred_element_type=jnp.float32)
        part_k = lax.dynamic_update_slice_in_dim(
            part_k, lax.dynamic_slice_in_dim(part_k, first_row, kblock, 0) + block_k, first_row, 0
        )
        part_v = lax.dynamic_update_slice_in_dim(
            part_v, lax.dynamic_slice_in_dim(part_v, first_row, kblock, 0) + block_v, first_row, 0
        )
        return (grad_q, part_k, part_v)

    start_sums = (
        jnp.zeros((num_rows, head_count, 128), jnp.float32),
        jnp.zeros((seq_len, 128), jnp.float32),
        jnp.zeros((seq_len, 128), jnp.float32),
    )
    grad_q, part_k, part_v = lax.fori_loop(key_first, causal_limit, sums_step, start_sums)
    return out_rows, grad_q, part_k, part_v


def attend(query_rows, key_all, value_all, dout_rows, positions, all_pos, seg_own, seg_all):
    head_count, num_rows, seq_len = query_rows.shape[1], query_rows.shape[0], key_all.shape[0]
    operands = (query_rows, key_all, value_all, dout_rows, positions, all_pos, seg_own, seg_all)
    if head_count * num_rows * seq_len <= (1 << 22):
        return attend_whole(*operands)
    kblock = seq_len
    while head_count * num_rows * kblock > (1 << 21) and kblock % 256 == 0:
        kblock //= 2
    return attend_blocked(*operands, kblock)


def local(hidden_in, w_query, w_key, w_value, lengths, attn_grad):
    num_rows = hidden_in.shape[0]
    head_count = w_query.shape[1] // 128
    first_heads = head_count // 2 if head_count % 2 == 0 else head_count
    first_cols = first_heads * 128
    query_cols = head_count * 128
    start_row = lax.axis_index("ctx") * num_rows
    seq_len = num_rows * lax.axis_size("ctx")
    positions = start_row + jnp.arange(num_rows, dtype=jnp.int32)
    all_pos = jnp.arange(seq_len, dtype=jnp.int32)
    seg_all = segment_ids(lengths[0], all_pos)
    seg_own = lax.dynamic_slice_in_dim(seg_all, start_row, num_rows)
    cosine, sine_table = rope_tables(positions)
    rows_axes = ("dp", "ctx")
    group_count = lax.axis_size(rows_axes)
    head_groups = lax.axis_size("head")
    if num_rows % head_groups == 0:
        quarter = num_rows // head_groups
        own_rows = lax.dynamic_slice_in_dim(hidden_in, lax.axis_index("head") * quarter, quarter, 0)
        cols_part = lax.all_to_all(own_rows, rows_axes, 1, 0, tiled=True)
    else:
        cols_part = lax.all_to_all(hidden_in, rows_axes, 1, 0, tiled=True)
    local_a = jnp.concatenate([w_query[:, :first_cols], w_key, w_value], 1)
    full_a = lax.all_gather(local_a, rows_axes, axis=0, tiled=True)
    cols_part, full_a, w_query = lax.optimization_barrier((cols_part, full_a, w_query))
    if num_rows % head_groups == 0:
        cols_all = lax.all_gather(cols_part, "head", axis=0, tiled=False)
        hidden_cols = (
            cols_all.reshape(head_groups, group_count, quarter, -1)
            .transpose(1, 0, 2, 3)
            .reshape(group_count * num_rows, -1)
        )
    else:
        hidden_cols = cols_part
    proj_a = jnp.dot(hidden_in, full_a, preferred_element_type=jnp.float32)
    query_a = rotate(
        proj_a[:, :first_cols].reshape(num_rows, first_heads, 128), cosine, sine_table
    ).astype(jnp.bfloat16)
    key_rows = rotate(
        proj_a[:, first_cols : first_cols + 128].reshape(num_rows, 1, 128), cosine, sine_table
    )[:, 0, :].astype(jnp.bfloat16)
    value_rows = proj_a[:, first_cols + 128 :].astype(jnp.bfloat16)
    key_all, value_all = (
        lax.all_gather(key_rows, "ctx", axis=0, tiled=True),
        lax.all_gather(value_rows, "ctx", axis=0, tiled=True),
    )
    dout_rows = attn_grad.reshape(num_rows, head_count, 128)
    shared = (key_all, value_all)
    masks = (positions, all_pos, seg_own, seg_all)
    out_a, grad_qa, part_k, part_v = attend(query_a, *shared, dout_rows[:, :first_heads], *masks)
    d_query_a = unrotate(grad_qa, cosine, sine_table).astype(jnp.bfloat16).reshape(num_rows, -1)
    out_parts, d_query_parts = [out_a], [d_query_a]
    if first_heads < head_count:
        w_rest = w_query[:, first_cols:]
        full_b = lax.all_gather(w_rest, rows_axes, axis=0, tiled=True)
        d_query_a, full_b = lax.optimization_barrier((d_query_a, full_b))
        early_all = lax.all_gather(d_query_a, rows_axes, axis=0, tiled=True)
        proj_b = jnp.dot(hidden_in, full_b, preferred_element_type=jnp.float32)
        query_b = rotate(
            proj_b.reshape(num_rows, head_count - first_heads, 128), cosine, sine_table
        ).astype(jnp.bfloat16)
        out_b, grad_qb, part_kb, part_vb = attend(
            query_b, *shared, dout_rows[:, first_heads:], *masks
        )
        early_all, hidden_cols, part_kb, part_vb = lax.optimization_barrier(
            (early_all, hidden_cols, part_kb, part_vb)
        )
        part_k, part_v = part_k + part_kb, part_v + part_vb
        out_parts.append(out_b)
        d_query_b = unrotate(grad_qb, cosine, sine_table).astype(jnp.bfloat16).reshape(num_rows, -1)
        d_query_parts.append(d_query_b)
    attended = jnp.concatenate(out_parts, 1).reshape(num_rows, query_cols)
    grad_k, grad_v = (
        lax.psum_scatter(part_k, "ctx", scatter_dimension=0, tiled=True),
        lax.psum_scatter(part_v, "ctx", scatter_dimension=0, tiled=True),
    )
    d_key = unrotate(grad_k[:, None, :], cosine, sine_table)[:, 0, :].astype(jnp.bfloat16)
    d_value = grad_v.astype(jnp.bfloat16)
    d_proj_a = jnp.concatenate([d_query_a, d_key, d_value], 1)
    input_part = lax.dot_general(
        d_proj_a, full_a, (((1,), (1,)), ((), ())), preferred_element_type=jnp.float32
    )
    if first_heads < head_count:
        input_part = input_part + lax.dot_general(
            d_query_b, full_b, (((1,), (1,)), ((), ())), preferred_element_type=jnp.float32
        )
        late_proj = jnp.concatenate([d_query_b, d_key, d_value], 1)
        early_sum = lax.dot_general(
            hidden_cols, early_all, (((0,), (0,)), ((), ())), preferred_element_type=jnp.float32
        )
    else:
        late_proj = jnp.concatenate([d_key, d_value], 1)
        early_all = lax.all_gather(d_query_a, rows_axes, axis=0, tiled=True)
        early_sum = lax.dot_general(
            hidden_cols, early_all, (((0,), (0,)), ((), ())), preferred_element_type=jnp.float32
        )
    input_cols = input_part.shape[1] // head_groups
    input_split = lax.all_to_all(
        input_part.reshape(num_rows, head_groups, input_cols), "head", 1, 1, tiled=False
    )
    grad_input = jnp.sum(input_split, axis=1).astype(jnp.bfloat16)
    late_all = lax.all_gather(late_proj, rows_axes, axis=0, tiled=True)
    late_sum = lax.dot_general(
        hidden_cols, late_all, (((0,), (0,)), ((), ())), preferred_element_type=jnp.float32
    )
    query_w = jnp.concatenate([early_sum, late_sum[:, : query_cols - first_cols]], 1)
    rest = late_sum[:, query_cols - first_cols :]
    return (attended, grad_input, query_w, rest[:, :128], rest[:, 128:])


def solution(mesh):
    placed = (
        P(("dp", "ctx"), None),
        P(("dp", "ctx"), "head"),
        P(("dp", "ctx"), "head"),
        P(("dp", "ctx"), "head"),
        P("dp", None),
        P(("dp", "ctx"), "head"),
    )
    return jax.shard_map(
        local,
        mesh=mesh,
        in_specs=placed,
        out_specs=(
            P(("dp", "ctx"), "head"),
            P(("dp", "ctx"), "head"),
            P(("dp", "ctx"), "head"),
            P(("dp", "ctx"), "head"),
            P(("dp", "ctx"), "head"),
        ),
        check_vma=False,
    )
```

```python
import jax
import jax.numpy as jnp
from jax import lax
from jax.sharding import PartitionSpec as P

scale_factor = 128.0 ** (-0.5)
neg_large = -1e30


def rope_tables(positions):
    inverse = jnp.power(500000.0, -jnp.arange(64, dtype=jnp.float32) / 64.0)
    angles = positions.astype(jnp.float32)[:, None] * inverse[None, :]
    return (jnp.cos(angles)[:, None, :], jnp.sin(angles)[:, None, :])


def rotate(entries, cosine, sine_table):
    first_half = entries[..., :64]
    second_half = entries[..., 64:]
    return jnp.concatenate(
        [
            first_half * cosine - second_half * sine_table,
            second_half * cosine + first_half * sine_table,
        ],
        -1,
    )


def unrotate(entries, cosine, sine_table):
    first_half = entries[..., :64]
    second_half = entries[..., 64:]
    return jnp.concatenate(
        [
            first_half * cosine + second_half * sine_table,
            second_half * cosine - first_half * sine_table,
        ],
        -1,
    )


def segment_ids(length_row, positions):
    ends = jnp.cumsum(length_row)
    return jnp.sum((positions[:, None] >= ends[None, :]).astype(jnp.int32), 1)


def block_scores(query_blk, key_blk, query_pos, key_pos, query_seg, key_seg):
    scores = (
        jnp.einsum("rhd,kd->hrk", query_blk, key_blk, preferred_element_type=jnp.float32)
        * scale_factor
    )
    allowed = (key_pos[None, :] <= query_pos[:, None]) & (key_seg[None, :] == query_seg[:, None])
    return (scores, allowed[None])


def grad_block(
    query_blk,
    dout_blk,
    total_blk,
    delta_blk,
    key_blk,
    value_blk,
    query_pos,
    key_pos,
    query_seg,
    key_seg,
):
    scores, allowed = block_scores(query_blk, key_blk, query_pos, key_pos, query_seg, key_seg)
    prob_rows = jnp.where(
        allowed, jnp.exp(jnp.where(allowed, scores - total_blk[..., None], neg_large)), 0.0
    )
    prob_b = prob_rows.astype(jnp.bfloat16)
    d_prob = jnp.einsum("rhd,kd->hrk", dout_blk, value_blk, preferred_element_type=jnp.float32)
    d_score = (scale_factor * prob_rows * (d_prob - delta_blk[..., None])).astype(jnp.bfloat16)
    return (prob_b, d_score)


def attend_whole(query_rows, key_all, value_all, dout_rows, positions, all_pos, seg_own, seg_all):
    scores, allowed = block_scores(query_rows, key_all, positions, all_pos, seg_own, seg_all)
    masked = jnp.where(allowed, scores, neg_large)
    top_score = jnp.max(masked, -1)
    total = jnp.sum(jnp.where(allowed, jnp.exp(masked - top_score[..., None]), 0.0), -1)
    log_total = top_score + jnp.log(total)
    prob_rows = jnp.where(
        allowed, jnp.exp(jnp.where(allowed, scores - log_total[..., None], neg_large)), 0.0
    )
    prob_b = prob_rows.astype(jnp.bfloat16)
    out_rows = jnp.einsum(
        "hrk,kd->rhd", prob_b, value_all, preferred_element_type=jnp.float32
    ).astype(jnp.bfloat16)
    delta_rows = jnp.einsum("rhd,rhd->hr", dout_rows, out_rows, preferred_element_type=jnp.float32)
    d_prob = jnp.einsum("rhd,kd->hrk", dout_rows, value_all, preferred_element_type=jnp.float32)
    d_score = (scale_factor * prob_rows * (d_prob - delta_rows[..., None])).astype(jnp.bfloat16)
    grad_q = jnp.einsum("hrk,kd->rhd", d_score, key_all, preferred_element_type=jnp.float32)
    part_k = jnp.einsum("hrk,rhd->kd", d_score, query_rows, preferred_element_type=jnp.float32)
    part_v = jnp.einsum("hrk,rhd->kd", prob_b, dout_rows, preferred_element_type=jnp.float32)
    return out_rows, grad_q, part_k, part_v


def attend_blocked(query_rows, key_all, value_all, dout_rows, positions, all_pos, seg_own, seg_all, kblock):
    num_rows, head_count = query_rows.shape[0], query_rows.shape[1]
    seq_len = key_all.shape[0]
    causal_limit = (positions[-1] + kblock) // kblock
    key_first = jnp.int32(0)

    def take_block(block_index):
        first_row = block_index * kblock
        return (
            lax.dynamic_slice_in_dim(key_all, first_row, kblock, 0),
            lax.dynamic_slice_in_dim(value_all, first_row, kblock, 0),
            lax.dynamic_slice_in_dim(all_pos, first_row, kblock, 0),
            lax.dynamic_slice_in_dim(seg_all, first_row, kblock, 0),
        )

    def stats_step(block_index, carried):
        run_max, run_sum = carried
        key_blk, value_blk, key_pos, key_seg = take_block(block_index)
        scores, allowed = block_scores(query_rows, key_blk, positions, key_pos, seg_own, key_seg)
        masked = jnp.where(allowed, scores, neg_large)
        new_max = jnp.maximum(run_max, jnp.max(masked, -1))
        terms = jnp.where(allowed, jnp.exp(masked - new_max[..., None]), 0.0)
        return (new_max, run_sum * jnp.exp(run_max - new_max) + jnp.sum(terms, -1))

    start_stats = (
        jnp.full((head_count, num_rows), neg_large, jnp.float32),
        jnp.zeros((head_count, num_rows), jnp.float32),
    )
    run_max, run_sum = lax.fori_loop(key_first, causal_limit, stats_step, start_stats)
    log_total = run_max + jnp.log(run_sum)

    def output_step(block_index, carried):
        key_blk, value_blk, key_pos, key_seg = take_block(block_index)
        scores, allowed = block_scores(query_rows, key_blk, positions, key_pos, seg_own, key_seg)
        prob_b = jnp.where(
            allowed, jnp.exp(jnp.where(allowed, scores - log_total[..., None], neg_large)), 0.0
        ).astype(jnp.bfloat16)
        return carried + jnp.einsum(
            "hrk,kd->rhd", prob_b, value_blk, preferred_element_type=jnp.float32
        )

    out_sum = lax.fori_loop(
        key_first, causal_limit, output_step, jnp.zeros((num_rows, head_count, 128), jnp.float32)
    )
    out_rows = out_sum.astype(jnp.bfloat16)
    delta_rows = jnp.einsum("rhd,rhd->hr", dout_rows, out_rows, preferred_element_type=jnp.float32)

    def sums_step(block_index, carried):
        grad_q, part_k, part_v = carried
        first_row = block_index * kblock
        key_blk, value_blk, key_pos, key_seg = take_block(block_index)
        prob_b, d_score = grad_block(
            query_rows, dout_rows, log_total, delta_rows, key_blk, value_blk,
            positions, key_pos, seg_own, key_seg,
        )
        grad_q = grad_q + jnp.einsum(
            "hrk,kd->rhd", d_score, key_blk, preferred_element_type=jnp.float32
        )
        block_k = jnp.einsum("hrk,rhd->kd", d_score, query_rows, preferred_element_type=jnp.float32)
        block_v = jnp.einsum("hrk,rhd->kd", prob_b, dout_rows, preferred_element_type=jnp.float32)
        part_k = lax.dynamic_update_slice_in_dim(
            part_k, lax.dynamic_slice_in_dim(part_k, first_row, kblock, 0) + block_k, first_row, 0
        )
        part_v = lax.dynamic_update_slice_in_dim(
            part_v, lax.dynamic_slice_in_dim(part_v, first_row, kblock, 0) + block_v, first_row, 0
        )
        return (grad_q, part_k, part_v)

    start_sums = (
        jnp.zeros((num_rows, head_count, 128), jnp.float32),
        jnp.zeros((seq_len, 128), jnp.float32),
        jnp.zeros((seq_len, 128), jnp.float32),
    )
    grad_q, part_k, part_v = lax.fori_loop(key_first, causal_limit, sums_step, start_sums)
    return out_rows, grad_q, part_k, part_v


def attend(query_rows, key_all, value_all, dout_rows, positions, all_pos, seg_own, seg_all):
    head_count, num_rows, seq_len = query_rows.shape[1], query_rows.shape[0], key_all.shape[0]
    operands = (query_rows, key_all, value_all, dout_rows, positions, all_pos, seg_own, seg_all)
    if head_count * num_rows * seq_len <= (1 << 22):
        return attend_whole(*operands)
    kblock = seq_len
    while head_count * num_rows * kblock > (1 << 21) and kblock % 256 == 0:
        kblock //= 2
    return attend_blocked(*operands, kblock)


def local(hidden_in, w_query, w_key, w_value, lengths, attn_grad):
    num_rows = hidden_in.shape[0]
    head_count = w_query.shape[1] // 128
    first_heads = head_count // 2 if head_count % 2 == 0 else head_count
    first_cols = first_heads * 128
    query_cols = head_count * 128
    start_row = lax.axis_index("ctx") * num_rows
    seq_len = num_rows * lax.axis_size("ctx")
    positions = start_row + jnp.arange(num_rows, dtype=jnp.int32)
    all_pos = jnp.arange(seq_len, dtype=jnp.int32)
    seg_all = segment_ids(lengths[0], all_pos)
    seg_own = lax.dynamic_slice_in_dim(seg_all, start_row, num_rows)
    cosine, sine_table = rope_tables(positions)
    rows_axes = ("dp", "ctx")
    group_count = lax.axis_size(rows_axes)
    head_groups = lax.axis_size("head")
    local_a = jnp.concatenate([w_query[:, :first_cols], w_key, w_value], 1)
    full_a = lax.all_gather(local_a, rows_axes, axis=0, tiled=True)
    full_a, w_query, hidden_in = lax.optimization_barrier((full_a, w_query, hidden_in))
    split_rows = num_rows % head_groups == 0
    if split_rows:
        quarter = num_rows // head_groups
        own_rows = lax.dynamic_slice_in_dim(hidden_in, lax.axis_index("head") * quarter, quarter, 0)
        cols_part = lax.all_to_all(own_rows, rows_axes, 1, 0, tiled=True)
    else:
        cols_part = lax.all_to_all(hidden_in, rows_axes, 1, 0, tiled=True)
    proj_a = jnp.dot(hidden_in, full_a, preferred_element_type=jnp.float32)
    query_a = rotate(
        proj_a[:, :first_cols].reshape(num_rows, first_heads, 128), cosine, sine_table
    ).astype(jnp.bfloat16)
    key_rows = rotate(
        proj_a[:, first_cols : first_cols + 128].reshape(num_rows, 1, 128), cosine, sine_table
    )[:, 0, :].astype(jnp.bfloat16)
    value_rows = proj_a[:, first_cols + 128 :].astype(jnp.bfloat16)
    key_all, value_all = (
        lax.all_gather(key_rows, "ctx", axis=0, tiled=True),
        lax.all_gather(value_rows, "ctx", axis=0, tiled=True),
    )
    dout_rows = attn_grad.reshape(num_rows, head_count, 128)
    shared = (key_all, value_all)
    masks = (positions, all_pos, seg_own, seg_all)
    out_a, grad_qa, part_k, part_v = attend(query_a, *shared, dout_rows[:, :first_heads], *masks)
    d_query_a = unrotate(grad_qa, cosine, sine_table).astype(jnp.bfloat16).reshape(num_rows, -1)
    out_parts, d_query_parts = [out_a], [d_query_a]
    if first_heads < head_count:
        w_rest = w_query[:, first_cols:]
        full_b = lax.all_gather(w_rest, rows_axes, axis=0, tiled=True)
        d_query_a, full_b, cols_part = lax.optimization_barrier((d_query_a, full_b, cols_part))
        early_all = lax.all_gather(d_query_a, rows_axes, axis=0, tiled=True)
        proj_b = jnp.dot(hidden_in, full_b, preferred_element_type=jnp.float32)
        query_b = rotate(
            proj_b.reshape(num_rows, head_count - first_heads, 128), cosine, sine_table
        ).astype(jnp.bfloat16)
        out_b, grad_qb, part_kb, part_vb = attend(
            query_b, *shared, dout_rows[:, first_heads:], *masks
        )
        if split_rows:
            spread = jnp.broadcast_to(cols_part[None], (head_groups,) + cols_part.shape)
            cols_all = lax.all_to_all(spread, "head", 0, 0, tiled=False)
            hidden_cols = (
                cols_all.reshape(head_groups, group_count, quarter, -1)
                .transpose(1, 0, 2, 3)
                .reshape(group_count * num_rows, -1)
            )
        else:
            hidden_cols = cols_part
        early_all, hidden_cols, part_kb, part_vb = lax.optimization_barrier(
            (early_all, hidden_cols, part_kb, part_vb)
        )
        part_k, part_v = part_k + part_kb, part_v + part_vb
        out_parts.append(out_b)
        d_query_b = unrotate(grad_qb, cosine, sine_table).astype(jnp.bfloat16).reshape(num_rows, -1)
        d_query_parts.append(d_query_b)
    attended = jnp.concatenate(out_parts, 1).reshape(num_rows, query_cols)
    grad_k, grad_v = (
        lax.psum_scatter(part_k, "ctx", scatter_dimension=0, tiled=True),
        lax.psum_scatter(part_v, "ctx", scatter_dimension=0, tiled=True),
    )
    d_key = unrotate(grad_k[:, None, :], cosine, sine_table)[:, 0, :].astype(jnp.bfloat16)
    d_value = grad_v.astype(jnp.bfloat16)
    d_proj_a = jnp.concatenate([d_query_a, d_key, d_value], 1)
    input_part = lax.dot_general(
        d_proj_a, full_a, (((1,), (1,)), ((), ())), preferred_element_type=jnp.float32
    )
    if first_heads < head_count:
        input_part = input_part + lax.dot_general(
            d_query_b, full_b, (((1,), (1,)), ((), ())), preferred_element_type=jnp.float32
        )
        late_proj = jnp.concatenate([d_query_b, d_key, d_value], 1)
        early_sum = lax.dot_general(
            hidden_cols, early_all, (((0,), (0,)), ((), ())), preferred_element_type=jnp.float32
        )
    else:
        hidden_cols = cols_part
        if split_rows:
            cols_all = lax.all_gather(cols_part, "head", axis=0, tiled=False)
            hidden_cols = (
                cols_all.reshape(head_groups, group_count, quarter, -1)
                .transpose(1, 0, 2, 3)
                .reshape(group_count * num_rows, -1)
            )
        late_proj = jnp.concatenate([d_key, d_value], 1)
        early_all = lax.all_gather(d_query_a, rows_axes, axis=0, tiled=True)
        early_sum = lax.dot_general(
            hidden_cols, early_all, (((0,), (0,)), ((), ())), preferred_element_type=jnp.float32
        )
    input_cols = input_part.shape[1] // head_groups
    input_split = lax.all_to_all(
        input_part.reshape(num_rows, head_groups, input_cols), "head", 1, 1, tiled=False
    )
    grad_input = jnp.sum(input_split, axis=1).astype(jnp.bfloat16)
    late_all = lax.all_gather(late_proj, rows_axes, axis=0, tiled=True)
    late_sum = lax.dot_general(
        hidden_cols, late_all, (((0,), (0,)), ((), ())), preferred_element_type=jnp.float32
    )
    query_w = jnp.concatenate([early_sum, late_sum[:, : query_cols - first_cols]], 1)
    rest = late_sum[:, query_cols - first_cols :]
    return (attended, grad_input, query_w, rest[:, :128], rest[:, 128:])


def solution(mesh):
    placed = (
        P(("dp", "ctx"), None),
        P(("dp", "ctx"), "head"),
        P(("dp", "ctx"), "head"),
        P(("dp", "ctx"), "head"),
        P("dp", None),
        P(("dp", "ctx"), "head"),
    )
    return jax.shard_map(
        local,
        mesh=mesh,
        in_specs=placed,
        out_specs=(
            P(("dp", "ctx"), "head"),
            P(("dp", "ctx"), "head"),
            P(("dp", "ctx"), "head"),
            P(("dp", "ctx"), "head"),
            P(("dp", "ctx"), "head"),
        ),
        check_vma=False,
    )
```

```python
import jax
import jax.numpy as jnp
from jax import lax
from jax.sharding import PartitionSpec as P

scale_factor = 128.0 ** (-0.5)
neg_large = -1e30


def rope_tables(positions):
    inverse = jnp.power(500000.0, -jnp.arange(64, dtype=jnp.float32) / 64.0)
    angles = positions.astype(jnp.float32)[:, None] * inverse[None, :]
    return (jnp.cos(angles)[:, None, :], jnp.sin(angles)[:, None, :])


def rotate(entries, cosine, sine_table):
    first_half = entries[..., :64]
    second_half = entries[..., 64:]
    return jnp.concatenate(
        [
            first_half * cosine - second_half * sine_table,
            second_half * cosine + first_half * sine_table,
        ],
        -1,
    )


def unrotate(entries, cosine, sine_table):
    first_half = entries[..., :64]
    second_half = entries[..., 64:]
    return jnp.concatenate(
        [
            first_half * cosine + second_half * sine_table,
            second_half * cosine - first_half * sine_table,
        ],
        -1,
    )


def segment_ids(length_row, positions):
    ends = jnp.cumsum(length_row)
    return jnp.sum((positions[:, None] >= ends[None, :]).astype(jnp.int32), 1)


def block_scores(query_blk, key_blk, query_pos, key_pos, query_seg, key_seg):
    scores = (
        jnp.einsum("rhd,kd->hrk", query_blk, key_blk, preferred_element_type=jnp.float32)
        * scale_factor
    )
    allowed = (key_pos[None, :] <= query_pos[:, None]) & (key_seg[None, :] == query_seg[:, None])
    return (scores, allowed[None])


def grad_block(
    query_blk,
    dout_blk,
    total_blk,
    delta_blk,
    key_blk,
    value_blk,
    query_pos,
    key_pos,
    query_seg,
    key_seg,
):
    scores, allowed = block_scores(query_blk, key_blk, query_pos, key_pos, query_seg, key_seg)
    prob_rows = jnp.where(
        allowed, jnp.exp(jnp.where(allowed, scores - total_blk[..., None], neg_large)), 0.0
    )
    prob_b = prob_rows.astype(jnp.bfloat16)
    d_prob = jnp.einsum("rhd,kd->hrk", dout_blk, value_blk, preferred_element_type=jnp.float32)
    d_score = (scale_factor * prob_rows * (d_prob - delta_blk[..., None])).astype(jnp.bfloat16)
    return (prob_b, d_score)


def attend_whole(query_rows, key_all, value_all, dout_rows, positions, all_pos, seg_own, seg_all):
    scores, allowed = block_scores(query_rows, key_all, positions, all_pos, seg_own, seg_all)
    masked = jnp.where(allowed, scores, neg_large)
    top_score = jnp.max(masked, -1)
    total = jnp.sum(jnp.where(allowed, jnp.exp(masked - top_score[..., None]), 0.0), -1)
    log_total = top_score + jnp.log(total)
    prob_rows = jnp.where(
        allowed, jnp.exp(jnp.where(allowed, scores - log_total[..., None], neg_large)), 0.0
    )
    prob_b = prob_rows.astype(jnp.bfloat16)
    out_rows = jnp.einsum(
        "hrk,kd->rhd", prob_b, value_all, preferred_element_type=jnp.float32
    ).astype(jnp.bfloat16)
    delta_rows = jnp.einsum("rhd,rhd->hr", dout_rows, out_rows, preferred_element_type=jnp.float32)
    d_prob = jnp.einsum("rhd,kd->hrk", dout_rows, value_all, preferred_element_type=jnp.float32)
    d_score = (scale_factor * prob_rows * (d_prob - delta_rows[..., None])).astype(jnp.bfloat16)
    grad_q = jnp.einsum("hrk,kd->rhd", d_score, key_all, preferred_element_type=jnp.float32)
    part_k = jnp.einsum("hrk,rhd->kd", d_score, query_rows, preferred_element_type=jnp.float32)
    part_v = jnp.einsum("hrk,rhd->kd", prob_b, dout_rows, preferred_element_type=jnp.float32)
    return out_rows, grad_q, part_k, part_v


def attend_blocked(query_rows, key_all, value_all, dout_rows, positions, all_pos, seg_own, seg_all, kblock):
    num_rows, head_count = query_rows.shape[0], query_rows.shape[1]
    seq_len = key_all.shape[0]
    causal_limit = (positions[-1] + kblock) // kblock
    key_first = jnp.int32(0)

    def take_block(block_index):
        first_row = block_index * kblock
        return (
            lax.dynamic_slice_in_dim(key_all, first_row, kblock, 0),
            lax.dynamic_slice_in_dim(value_all, first_row, kblock, 0),
            lax.dynamic_slice_in_dim(all_pos, first_row, kblock, 0),
            lax.dynamic_slice_in_dim(seg_all, first_row, kblock, 0),
        )

    def stats_step(block_index, carried):
        run_max, run_sum = carried
        key_blk, value_blk, key_pos, key_seg = take_block(block_index)
        scores, allowed = block_scores(query_rows, key_blk, positions, key_pos, seg_own, key_seg)
        masked = jnp.where(allowed, scores, neg_large)
        new_max = jnp.maximum(run_max, jnp.max(masked, -1))
        terms = jnp.where(allowed, jnp.exp(masked - new_max[..., None]), 0.0)
        return (new_max, run_sum * jnp.exp(run_max - new_max) + jnp.sum(terms, -1))

    start_stats = (
        jnp.full((head_count, num_rows), neg_large, jnp.float32),
        jnp.zeros((head_count, num_rows), jnp.float32),
    )
    run_max, run_sum = lax.fori_loop(key_first, causal_limit, stats_step, start_stats)
    log_total = run_max + jnp.log(run_sum)

    def output_step(block_index, carried):
        key_blk, value_blk, key_pos, key_seg = take_block(block_index)
        scores, allowed = block_scores(query_rows, key_blk, positions, key_pos, seg_own, key_seg)
        prob_b = jnp.where(
            allowed, jnp.exp(jnp.where(allowed, scores - log_total[..., None], neg_large)), 0.0
        ).astype(jnp.bfloat16)
        return carried + jnp.einsum(
            "hrk,kd->rhd", prob_b, value_blk, preferred_element_type=jnp.float32
        )

    out_sum = lax.fori_loop(
        key_first, causal_limit, output_step, jnp.zeros((num_rows, head_count, 128), jnp.float32)
    )
    out_rows = out_sum.astype(jnp.bfloat16)
    delta_rows = jnp.einsum("rhd,rhd->hr", dout_rows, out_rows, preferred_element_type=jnp.float32)

    def sums_step(block_index, carried):
        grad_q, part_k, part_v = carried
        first_row = block_index * kblock
        key_blk, value_blk, key_pos, key_seg = take_block(block_index)
        prob_b, d_score = grad_block(
            query_rows, dout_rows, log_total, delta_rows, key_blk, value_blk,
            positions, key_pos, seg_own, key_seg,
        )
        grad_q = grad_q + jnp.einsum(
            "hrk,kd->rhd", d_score, key_blk, preferred_element_type=jnp.float32
        )
        block_k = jnp.einsum("hrk,rhd->kd", d_score, query_rows, preferred_element_type=jnp.float32)
        block_v = jnp.einsum("hrk,rhd->kd", prob_b, dout_rows, preferred_element_type=jnp.float32)
        part_k = lax.dynamic_update_slice_in_dim(
            part_k, lax.dynamic_slice_in_dim(part_k, first_row, kblock, 0) + block_k, first_row, 0
        )
        part_v = lax.dynamic_update_slice_in_dim(
            part_v, lax.dynamic_slice_in_dim(part_v, first_row, kblock, 0) + block_v, first_row, 0
        )
        return (grad_q, part_k, part_v)

    start_sums = (
        jnp.zeros((num_rows, head_count, 128), jnp.float32),
        jnp.zeros((seq_len, 128), jnp.float32),
        jnp.zeros((seq_len, 128), jnp.float32),
    )
    grad_q, part_k, part_v = lax.fori_loop(key_first, causal_limit, sums_step, start_sums)
    return out_rows, grad_q, part_k, part_v


def attend(query_rows, key_all, value_all, dout_rows, positions, all_pos, seg_own, seg_all):
    head_count, num_rows, seq_len = query_rows.shape[1], query_rows.shape[0], key_all.shape[0]
    operands = (query_rows, key_all, value_all, dout_rows, positions, all_pos, seg_own, seg_all)
    if head_count * num_rows * seq_len <= (1 << 22):
        return attend_whole(*operands)
    kblock = seq_len
    while head_count * num_rows * kblock > (1 << 21) and kblock % 256 == 0:
        kblock //= 2
    return attend_blocked(*operands, kblock)


def local(hidden_in, w_query, w_key, w_value, lengths, attn_grad):
    num_rows = hidden_in.shape[0]
    head_count = w_query.shape[1] // 128
    first_heads = head_count // 2 if head_count % 2 == 0 else head_count
    first_cols = first_heads * 128
    query_cols = head_count * 128
    start_row = lax.axis_index("ctx") * num_rows
    seq_len = num_rows * lax.axis_size("ctx")
    positions = start_row + jnp.arange(num_rows, dtype=jnp.int32)
    all_pos = jnp.arange(seq_len, dtype=jnp.int32)
    seg_all = segment_ids(lengths[0], all_pos)
    seg_own = lax.dynamic_slice_in_dim(seg_all, start_row, num_rows)
    cosine, sine_table = rope_tables(positions)
    rows_axes = ("dp", "ctx")
    group_count = lax.axis_size(rows_axes)
    head_groups = lax.axis_size("head")
    local_a = jnp.concatenate([w_query[:, :first_cols], w_key, w_value], 1)
    full_a = lax.all_gather(local_a, rows_axes, axis=0, tiled=True)
    full_a, w_query, hidden_in = lax.optimization_barrier((full_a, w_query, hidden_in))
    split_rows = num_rows % head_groups == 0
    if split_rows:
        quarter = num_rows // head_groups
        own_rows = lax.dynamic_slice_in_dim(hidden_in, lax.axis_index("head") * quarter, quarter, 0)
        cols_part = lax.all_to_all(own_rows, rows_axes, 1, 0, tiled=True)
    else:
        cols_part = lax.all_to_all(hidden_in, rows_axes, 1, 0, tiled=True)
    proj_a = jnp.dot(hidden_in, full_a, preferred_element_type=jnp.float32)
    query_a = rotate(
        proj_a[:, :first_cols].reshape(num_rows, first_heads, 128), cosine, sine_table
    ).astype(jnp.bfloat16)
    key_rows = rotate(
        proj_a[:, first_cols : first_cols + 128].reshape(num_rows, 1, 128), cosine, sine_table
    )[:, 0, :].astype(jnp.bfloat16)
    value_rows = proj_a[:, first_cols + 128 :].astype(jnp.bfloat16)
    key_all, value_all = (
        lax.all_gather(key_rows, "ctx", axis=0, tiled=True),
        lax.all_gather(value_rows, "ctx", axis=0, tiled=True),
    )
    dout_rows = attn_grad.reshape(num_rows, head_count, 128)
    shared = (key_all, value_all)
    masks = (positions, all_pos, seg_own, seg_all)
    out_a, grad_qa, part_k, part_v = attend(query_a, *shared, dout_rows[:, :first_heads], *masks)
    d_query_a = unrotate(grad_qa, cosine, sine_table).astype(jnp.bfloat16).reshape(num_rows, -1)
    out_parts, d_query_parts = [out_a], [d_query_a]
    if first_heads < head_count:
        w_rest = w_query[:, first_cols:]
        full_b = lax.all_gather(w_rest, rows_axes, axis=0, tiled=True)
        d_query_a, full_b = lax.optimization_barrier((d_query_a, full_b))
        early_all = lax.all_gather(d_query_a, rows_axes, axis=0, tiled=True)
        proj_b = jnp.dot(hidden_in, full_b, preferred_element_type=jnp.float32)
        query_b = rotate(
            proj_b.reshape(num_rows, head_count - first_heads, 128), cosine, sine_table
        ).astype(jnp.bfloat16)
        out_b, grad_qb, part_kb, part_vb = attend(
            query_b, *shared, dout_rows[:, first_heads:], *masks
        )
        early_all, cols_part, part_kb, part_vb = lax.optimization_barrier(
            (early_all, cols_part, part_kb, part_vb)
        )
        hidden_cols = cols_part
        if split_rows:
            spread = jnp.broadcast_to(cols_part[None], (head_groups,) + cols_part.shape)
            cols_all = lax.all_to_all(spread, "head", 0, 0, tiled=False)
            hidden_cols = (
                cols_all.reshape(head_groups, group_count, quarter, -1)
                .transpose(1, 0, 2, 3)
                .reshape(group_count * num_rows, -1)
            )
        part_k, part_v = part_k + part_kb, part_v + part_vb
        out_parts.append(out_b)
        d_query_b = unrotate(grad_qb, cosine, sine_table).astype(jnp.bfloat16).reshape(num_rows, -1)
        d_query_parts.append(d_query_b)
    attended = jnp.concatenate(out_parts, 1).reshape(num_rows, query_cols)
    grad_k, grad_v = (
        lax.psum_scatter(part_k, "ctx", scatter_dimension=0, tiled=True),
        lax.psum_scatter(part_v, "ctx", scatter_dimension=0, tiled=True),
    )
    d_key = unrotate(grad_k[:, None, :], cosine, sine_table)[:, 0, :].astype(jnp.bfloat16)
    d_value = grad_v.astype(jnp.bfloat16)
    d_proj_a = jnp.concatenate([d_query_a, d_key, d_value], 1)
    input_part = lax.dot_general(
        d_proj_a, full_a, (((1,), (1,)), ((), ())), preferred_element_type=jnp.float32
    )
    if first_heads < head_count:
        input_part = input_part + lax.dot_general(
            d_query_b, full_b, (((1,), (1,)), ((), ())), preferred_element_type=jnp.float32
        )
        late_proj = jnp.concatenate([d_query_b, d_key, d_value], 1)
        early_sum = lax.dot_general(
            hidden_cols, early_all, (((0,), (0,)), ((), ())), preferred_element_type=jnp.float32
        )
    else:
        hidden_cols = cols_part
        if split_rows:
            cols_all = lax.all_gather(cols_part, "head", axis=0, tiled=False)
            hidden_cols = (
                cols_all.reshape(head_groups, group_count, quarter, -1)
                .transpose(1, 0, 2, 3)
                .reshape(group_count * num_rows, -1)
            )
        late_proj = jnp.concatenate([d_key, d_value], 1)
        early_all = lax.all_gather(d_query_a, rows_axes, axis=0, tiled=True)
        early_sum = lax.dot_general(
            hidden_cols, early_all, (((0,), (0,)), ((), ())), preferred_element_type=jnp.float32
        )
    input_cols = input_part.shape[1] // head_groups
    input_split = lax.all_to_all(
        input_part.astype(jnp.bfloat16).reshape(num_rows, head_groups, input_cols),
        "head", 1, 1, tiled=False,
    )
    grad_input = jnp.sum(input_split.astype(jnp.float32), axis=1).astype(jnp.bfloat16)
    late_all = lax.all_gather(late_proj, rows_axes, axis=0, tiled=True)
    late_sum = lax.dot_general(
        hidden_cols, late_all, (((0,), (0,)), ((), ())), preferred_element_type=jnp.float32
    )
    query_w = jnp.concatenate([early_sum, late_sum[:, : query_cols - first_cols]], 1)
    rest = late_sum[:, query_cols - first_cols :]
    return (attended, grad_input, query_w, rest[:, :128], rest[:, 128:])


def solution(mesh):
    placed = (
        P(("dp", "ctx"), None),
        P(("dp", "ctx"), "head"),
        P(("dp", "ctx"), "head"),
        P(("dp", "ctx"), "head"),
        P("dp", None),
        P(("dp", "ctx"), "head"),
    )
    return jax.shard_map(
        local,
        mesh=mesh,
        in_specs=placed,
        out_specs=(
            P(("dp", "ctx"), "head"),
            P(("dp", "ctx"), "head"),
            P(("dp", "ctx"), "head"),
            P(("dp", "ctx"), "head"),
            P(("dp", "ctx"), "head"),
        ),
        check_vma=False,
    )
```

```python
import jax
import jax.numpy as jnp
from jax import lax
from jax.sharding import PartitionSpec as P

scale_factor = 128.0 ** (-0.5)
neg_large = -1e30


def rope_tables(positions):
    inverse = jnp.power(500000.0, -jnp.arange(64, dtype=jnp.float32) / 64.0)
    angles = positions.astype(jnp.float32)[:, None] * inverse[None, :]
    return (jnp.cos(angles)[:, None, :], jnp.sin(angles)[:, None, :])


def rotate(entries, cosine, sine_table):
    first_half = entries[..., :64]
    second_half = entries[..., 64:]
    return jnp.concatenate(
        [
            first_half * cosine - second_half * sine_table,
            second_half * cosine + first_half * sine_table,
        ],
        -1,
    )


def unrotate(entries, cosine, sine_table):
    first_half = entries[..., :64]
    second_half = entries[..., 64:]
    return jnp.concatenate(
        [
            first_half * cosine + second_half * sine_table,
            second_half * cosine - first_half * sine_table,
        ],
        -1,
    )


def segment_ids(length_row, positions):
    ends = jnp.cumsum(length_row)
    return jnp.sum((positions[:, None] >= ends[None, :]).astype(jnp.int32), 1)


def block_scores(query_blk, key_blk, query_pos, key_pos, query_seg, key_seg):
    scores = (
        jnp.einsum("rhd,kd->hrk", query_blk, key_blk, preferred_element_type=jnp.float32)
        * scale_factor
    )
    allowed = (key_pos[None, :] <= query_pos[:, None]) & (key_seg[None, :] == query_seg[:, None])
    return (scores, allowed[None])


def grad_block(
    query_blk,
    dout_blk,
    total_blk,
    delta_blk,
    key_blk,
    value_blk,
    query_pos,
    key_pos,
    query_seg,
    key_seg,
):
    scores, allowed = block_scores(query_blk, key_blk, query_pos, key_pos, query_seg, key_seg)
    prob_rows = jnp.where(
        allowed, jnp.exp(jnp.where(allowed, scores - total_blk[..., None], neg_large)), 0.0
    )
    prob_b = prob_rows.astype(jnp.bfloat16)
    d_prob = jnp.einsum("rhd,kd->hrk", dout_blk, value_blk, preferred_element_type=jnp.float32)
    d_score = (scale_factor * prob_rows * (d_prob - delta_blk[..., None])).astype(jnp.bfloat16)
    return (prob_b, d_score)


def attend_whole(query_rows, key_all, value_all, dout_rows, positions, all_pos, seg_own, seg_all):
    scores, allowed = block_scores(query_rows, key_all, positions, all_pos, seg_own, seg_all)
    masked = jnp.where(allowed, scores, neg_large)
    top_score = jnp.max(masked, -1)
    total = jnp.sum(jnp.where(allowed, jnp.exp(masked - top_score[..., None]), 0.0), -1)
    log_total = top_score + jnp.log(total)
    prob_rows = jnp.where(
        allowed, jnp.exp(jnp.where(allowed, scores - log_total[..., None], neg_large)), 0.0
    )
    prob_b = prob_rows.astype(jnp.bfloat16)
    out_rows = jnp.einsum(
        "hrk,kd->rhd", prob_b, value_all, preferred_element_type=jnp.float32
    ).astype(jnp.bfloat16)
    delta_rows = jnp.einsum("rhd,rhd->hr", dout_rows, out_rows, preferred_element_type=jnp.float32)
    d_prob = jnp.einsum("rhd,kd->hrk", dout_rows, value_all, preferred_element_type=jnp.float32)
    d_score = (scale_factor * prob_rows * (d_prob - delta_rows[..., None])).astype(jnp.bfloat16)
    grad_q = jnp.einsum("hrk,kd->rhd", d_score, key_all, preferred_element_type=jnp.float32)
    part_k = jnp.einsum("hrk,rhd->kd", d_score, query_rows, preferred_element_type=jnp.float32)
    part_v = jnp.einsum("hrk,rhd->kd", prob_b, dout_rows, preferred_element_type=jnp.float32)
    return out_rows, grad_q, part_k, part_v


def attend_blocked(query_rows, key_all, value_all, dout_rows, positions, all_pos, seg_own, seg_all, kblock):
    num_rows, head_count = query_rows.shape[0], query_rows.shape[1]
    seq_len = key_all.shape[0]
    causal_limit = (positions[-1] + kblock) // kblock
    key_first = jnp.int32(0)

    def take_block(block_index):
        first_row = block_index * kblock
        return (
            lax.dynamic_slice_in_dim(key_all, first_row, kblock, 0),
            lax.dynamic_slice_in_dim(value_all, first_row, kblock, 0),
            lax.dynamic_slice_in_dim(all_pos, first_row, kblock, 0),
            lax.dynamic_slice_in_dim(seg_all, first_row, kblock, 0),
        )

    def stats_step(block_index, carried):
        run_max, run_sum = carried
        key_blk, value_blk, key_pos, key_seg = take_block(block_index)
        scores, allowed = block_scores(query_rows, key_blk, positions, key_pos, seg_own, key_seg)
        masked = jnp.where(allowed, scores, neg_large)
        new_max = jnp.maximum(run_max, jnp.max(masked, -1))
        terms = jnp.where(allowed, jnp.exp(masked - new_max[..., None]), 0.0)
        return (new_max, run_sum * jnp.exp(run_max - new_max) + jnp.sum(terms, -1))

    start_stats = (
        jnp.full((head_count, num_rows), neg_large, jnp.float32),
        jnp.zeros((head_count, num_rows), jnp.float32),
    )
    run_max, run_sum = lax.fori_loop(key_first, causal_limit, stats_step, start_stats)
    log_total = run_max + jnp.log(run_sum)

    def output_step(block_index, carried):
        key_blk, value_blk, key_pos, key_seg = take_block(block_index)
        scores, allowed = block_scores(query_rows, key_blk, positions, key_pos, seg_own, key_seg)
        prob_b = jnp.where(
            allowed, jnp.exp(jnp.where(allowed, scores - log_total[..., None], neg_large)), 0.0
        ).astype(jnp.bfloat16)
        return carried + jnp.einsum(
            "hrk,kd->rhd", prob_b, value_blk, preferred_element_type=jnp.float32
        )

    out_sum = lax.fori_loop(
        key_first, causal_limit, output_step, jnp.zeros((num_rows, head_count, 128), jnp.float32)
    )
    out_rows = out_sum.astype(jnp.bfloat16)
    delta_rows = jnp.einsum("rhd,rhd->hr", dout_rows, out_rows, preferred_element_type=jnp.float32)

    def sums_step(block_index, carried):
        grad_q, part_k, part_v = carried
        first_row = block_index * kblock
        key_blk, value_blk, key_pos, key_seg = take_block(block_index)
        prob_b, d_score = grad_block(
            query_rows, dout_rows, log_total, delta_rows, key_blk, value_blk,
            positions, key_pos, seg_own, key_seg,
        )
        grad_q = grad_q + jnp.einsum(
            "hrk,kd->rhd", d_score, key_blk, preferred_element_type=jnp.float32
        )
        block_k = jnp.einsum("hrk,rhd->kd", d_score, query_rows, preferred_element_type=jnp.float32)
        block_v = jnp.einsum("hrk,rhd->kd", prob_b, dout_rows, preferred_element_type=jnp.float32)
        part_k = lax.dynamic_update_slice_in_dim(
            part_k, lax.dynamic_slice_in_dim(part_k, first_row, kblock, 0) + block_k, first_row, 0
        )
        part_v = lax.dynamic_update_slice_in_dim(
            part_v, lax.dynamic_slice_in_dim(part_v, first_row, kblock, 0) + block_v, first_row, 0
        )
        return (grad_q, part_k, part_v)

    start_sums = (
        jnp.zeros((num_rows, head_count, 128), jnp.float32),
        jnp.zeros((seq_len, 128), jnp.float32),
        jnp.zeros((seq_len, 128), jnp.float32),
    )
    grad_q, part_k, part_v = lax.fori_loop(key_first, causal_limit, sums_step, start_sums)
    return out_rows, grad_q, part_k, part_v


def attend(query_rows, key_all, value_all, dout_rows, positions, all_pos, seg_own, seg_all):
    head_count, num_rows, seq_len = query_rows.shape[1], query_rows.shape[0], key_all.shape[0]
    operands = (query_rows, key_all, value_all, dout_rows, positions, all_pos, seg_own, seg_all)
    if head_count * num_rows * seq_len <= (1 << 22):
        return attend_whole(*operands)
    kblock = seq_len
    while head_count * num_rows * kblock > (1 << 21) and kblock % 256 == 0:
        kblock //= 2
    return attend_blocked(*operands, kblock)


def local(hidden_in, w_query, w_key, w_value, lengths, attn_grad):
    num_rows = hidden_in.shape[0]
    head_count = w_query.shape[1] // 128
    first_heads = head_count // 2 if head_count % 2 == 0 else head_count
    first_cols = first_heads * 128
    query_cols = head_count * 128
    start_row = lax.axis_index("ctx") * num_rows
    seq_len = num_rows * lax.axis_size("ctx")
    positions = start_row + jnp.arange(num_rows, dtype=jnp.int32)
    all_pos = jnp.arange(seq_len, dtype=jnp.int32)
    seg_all = segment_ids(lengths[0], all_pos)
    seg_own = lax.dynamic_slice_in_dim(seg_all, start_row, num_rows)
    cosine, sine_table = rope_tables(positions)
    rows_axes = ("dp", "ctx")
    group_count = lax.axis_size(rows_axes)
    head_groups = lax.axis_size("head")
    local_a = jnp.concatenate([w_query[:, :first_cols], w_key, w_value], 1)
    full_a = lax.all_gather(local_a, rows_axes, axis=0, tiled=True)
    split_rows = num_rows % head_groups == 0
    if split_rows:
        quarter = num_rows // head_groups
        own_rows = lax.dynamic_slice_in_dim(hidden_in, lax.axis_index("head") * quarter, quarter, 0)
        cols_part = lax.all_to_all(own_rows, rows_axes, 1, 0, tiled=True)
        spread = jnp.broadcast_to(cols_part[None], (head_groups,) + cols_part.shape)
        cols_all = lax.all_to_all(spread, "head", 0, 0, tiled=False)
        hidden_cols = (
            cols_all.reshape(head_groups, group_count, quarter, -1)
            .transpose(1, 0, 2, 3)
            .reshape(group_count * num_rows, -1)
        )
    else:
        hidden_cols = lax.all_to_all(hidden_in, rows_axes, 1, 0, tiled=True)
    full_a, w_query, hidden_cols = lax.optimization_barrier((full_a, w_query, hidden_cols))
    proj_a = jnp.dot(hidden_in, full_a, preferred_element_type=jnp.float32)
    query_a = rotate(
        proj_a[:, :first_cols].reshape(num_rows, first_heads, 128), cosine, sine_table
    ).astype(jnp.bfloat16)
    key_rows = rotate(
        proj_a[:, first_cols : first_cols + 128].reshape(num_rows, 1, 128), cosine, sine_table
    )[:, 0, :].astype(jnp.bfloat16)
    value_rows = proj_a[:, first_cols + 128 :].astype(jnp.bfloat16)
    key_all, value_all = (
        lax.all_gather(key_rows, "ctx", axis=0, tiled=True),
        lax.all_gather(value_rows, "ctx", axis=0, tiled=True),
    )
    dout_rows = attn_grad.reshape(num_rows, head_count, 128)
    shared = (key_all, value_all)
    masks = (positions, all_pos, seg_own, seg_all)
    out_a, grad_qa, part_k, part_v = attend(query_a, *shared, dout_rows[:, :first_heads], *masks)
    d_query_a = unrotate(grad_qa, cosine, sine_table).astype(jnp.bfloat16).reshape(num_rows, -1)
    out_parts, d_query_parts = [out_a], [d_query_a]
    if first_heads < head_count:
        w_rest = w_query[:, first_cols:]
        full_b = lax.all_gather(w_rest, rows_axes, axis=0, tiled=True)
        d_query_a, full_b = lax.optimization_barrier((d_query_a, full_b))
        early_all = lax.all_gather(d_query_a, rows_axes, axis=0, tiled=True)
        proj_b = jnp.dot(hidden_in, full_b, preferred_element_type=jnp.float32)
        query_b = rotate(
            proj_b.reshape(num_rows, head_count - first_heads, 128), cosine, sine_table
        ).astype(jnp.bfloat16)
        out_b, grad_qb, part_kb, part_vb = attend(
            query_b, *shared, dout_rows[:, first_heads:], *masks
        )
        early_all, part_kb, part_vb = lax.optimization_barrier((early_all, part_kb, part_vb))
        part_k, part_v = part_k + part_kb, part_v + part_vb
        out_parts.append(out_b)
        d_query_b = unrotate(grad_qb, cosine, sine_table).astype(jnp.bfloat16).reshape(num_rows, -1)
        d_query_parts.append(d_query_b)
    attended = jnp.concatenate(out_parts, 1).reshape(num_rows, query_cols)
    grad_k, grad_v = (
        lax.psum_scatter(part_k, "ctx", scatter_dimension=0, tiled=True),
        lax.psum_scatter(part_v, "ctx", scatter_dimension=0, tiled=True),
    )
    d_key = unrotate(grad_k[:, None, :], cosine, sine_table)[:, 0, :].astype(jnp.bfloat16)
    d_value = grad_v.astype(jnp.bfloat16)
    d_proj_a = jnp.concatenate([d_query_a, d_key, d_value], 1)
    input_part = lax.dot_general(
        d_proj_a, full_a, (((1,), (1,)), ((), ())), preferred_element_type=jnp.float32
    )
    if first_heads < head_count:
        input_part = input_part + lax.dot_general(
            d_query_b, full_b, (((1,), (1,)), ((), ())), preferred_element_type=jnp.float32
        )
        late_proj = jnp.concatenate([d_query_b, d_key, d_value], 1)
        early_sum = lax.dot_general(
            hidden_cols, early_all, (((0,), (0,)), ((), ())), preferred_element_type=jnp.float32
        )
    else:
        late_proj = jnp.concatenate([d_key, d_value], 1)
        early_all = lax.all_gather(d_query_a, rows_axes, axis=0, tiled=True)
        early_sum = lax.dot_general(
            hidden_cols, early_all, (((0,), (0,)), ((), ())), preferred_element_type=jnp.float32
        )
    input_cols = input_part.shape[1] // head_groups
    input_split = lax.all_to_all(
        input_part.astype(jnp.bfloat16).reshape(num_rows, head_groups, input_cols),
        "head", 1, 1, tiled=False,
    )
    grad_input = jnp.sum(input_split.astype(jnp.float32), axis=1).astype(jnp.bfloat16)
    late_all = lax.all_gather(late_proj, rows_axes, axis=0, tiled=True)
    late_sum = lax.dot_general(
        hidden_cols, late_all, (((0,), (0,)), ((), ())), preferred_element_type=jnp.float32
    )
    query_w = jnp.concatenate([early_sum, late_sum[:, : query_cols - first_cols]], 1)
    rest = late_sum[:, query_cols - first_cols :]
    return (attended, grad_input, query_w, rest[:, :128], rest[:, 128:])


def solution(mesh):
    placed = (
        P(("dp", "ctx"), None),
        P(("dp", "ctx"), "head"),
        P(("dp", "ctx"), "head"),
        P(("dp", "ctx"), "head"),
        P("dp", None),
        P(("dp", "ctx"), "head"),
    )
    return jax.shard_map(
        local,
        mesh=mesh,
        in_specs=placed,
        out_specs=(
            P(("dp", "ctx"), "head"),
            P(("dp", "ctx"), "head"),
            P(("dp", "ctx"), "head"),
            P(("dp", "ctx"), "head"),
            P(("dp", "ctx"), "head"),
        ),
        check_vma=False,
    )
```

```python
import jax
import jax.numpy as jnp
from jax import lax
from jax.sharding import PartitionSpec as P

scale_factor = 128.0 ** (-0.5)
neg_large = -1e30


def rope_tables(positions):
    inverse = jnp.power(500000.0, -jnp.arange(64, dtype=jnp.float32) / 64.0)
    angles = positions.astype(jnp.float32)[:, None] * inverse[None, :]
    return (jnp.cos(angles)[:, None, :], jnp.sin(angles)[:, None, :])


def rotate(entries, cosine, sine_table):
    first_half = entries[..., :64]
    second_half = entries[..., 64:]
    return jnp.concatenate(
        [
            first_half * cosine - second_half * sine_table,
            second_half * cosine + first_half * sine_table,
        ],
        -1,
    )


def unrotate(entries, cosine, sine_table):
    first_half = entries[..., :64]
    second_half = entries[..., 64:]
    return jnp.concatenate(
        [
            first_half * cosine + second_half * sine_table,
            second_half * cosine - first_half * sine_table,
        ],
        -1,
    )


def segment_ids(length_row, positions):
    ends = jnp.cumsum(length_row)
    return jnp.sum((positions[:, None] >= ends[None, :]).astype(jnp.int32), 1)


def block_scores(query_blk, key_blk, query_pos, key_pos, query_seg, key_seg):
    scores = (
        jnp.einsum("rhd,kd->hrk", query_blk, key_blk, preferred_element_type=jnp.float32)
        * scale_factor
    )
    allowed = (key_pos[None, :] <= query_pos[:, None]) & (key_seg[None, :] == query_seg[:, None])
    return (scores, allowed[None])


def grad_block(
    query_blk,
    dout_blk,
    total_blk,
    delta_blk,
    key_blk,
    value_blk,
    query_pos,
    key_pos,
    query_seg,
    key_seg,
):
    scores, allowed = block_scores(query_blk, key_blk, query_pos, key_pos, query_seg, key_seg)
    prob_rows = jnp.where(
        allowed, jnp.exp(jnp.where(allowed, scores - total_blk[..., None], neg_large)), 0.0
    )
    prob_b = prob_rows.astype(jnp.bfloat16)
    d_prob = jnp.einsum("rhd,kd->hrk", dout_blk, value_blk, preferred_element_type=jnp.float32)
    d_score = (scale_factor * prob_rows * (d_prob - delta_blk[..., None])).astype(jnp.bfloat16)
    return (prob_b, d_score)


def attend_whole(query_rows, key_all, value_all, dout_rows, positions, all_pos, seg_own, seg_all):
    scores, allowed = block_scores(query_rows, key_all, positions, all_pos, seg_own, seg_all)
    masked = jnp.where(allowed, scores, neg_large)
    top_score = jnp.max(masked, -1)
    total = jnp.sum(jnp.where(allowed, jnp.exp(masked - top_score[..., None]), 0.0), -1)
    log_total = top_score + jnp.log(total)
    prob_rows = jnp.where(
        allowed, jnp.exp(jnp.where(allowed, scores - log_total[..., None], neg_large)), 0.0
    )
    prob_b = prob_rows.astype(jnp.bfloat16)
    out_rows = jnp.einsum(
        "hrk,kd->rhd", prob_b, value_all, preferred_element_type=jnp.float32
    ).astype(jnp.bfloat16)
    delta_rows = jnp.einsum("rhd,rhd->hr", dout_rows, out_rows, preferred_element_type=jnp.float32)
    d_prob = jnp.einsum("rhd,kd->hrk", dout_rows, value_all, preferred_element_type=jnp.float32)
    d_score = (scale_factor * prob_rows * (d_prob - delta_rows[..., None])).astype(jnp.bfloat16)
    grad_q = jnp.einsum("hrk,kd->rhd", d_score, key_all, preferred_element_type=jnp.float32)
    part_k = jnp.einsum("hrk,rhd->kd", d_score, query_rows, preferred_element_type=jnp.float32)
    part_v = jnp.einsum("hrk,rhd->kd", prob_b, dout_rows, preferred_element_type=jnp.float32)
    return out_rows, grad_q, part_k, part_v


def attend_blocked(query_rows, key_all, value_all, dout_rows, positions, all_pos, seg_own, seg_all, kblock):
    num_rows, head_count = query_rows.shape[0], query_rows.shape[1]
    seq_len = key_all.shape[0]
    causal_limit = (positions[-1] + kblock) // kblock
    key_first = jnp.int32(0)

    def take_block(block_index):
        first_row = block_index * kblock
        return (
            lax.dynamic_slice_in_dim(key_all, first_row, kblock, 0),
            lax.dynamic_slice_in_dim(value_all, first_row, kblock, 0),
            lax.dynamic_slice_in_dim(all_pos, first_row, kblock, 0),
            lax.dynamic_slice_in_dim(seg_all, first_row, kblock, 0),
        )

    def stats_step(block_index, carried):
        run_max, run_sum = carried
        key_blk, value_blk, key_pos, key_seg = take_block(block_index)
        scores, allowed = block_scores(query_rows, key_blk, positions, key_pos, seg_own, key_seg)
        masked = jnp.where(allowed, scores, neg_large)
        new_max = jnp.maximum(run_max, jnp.max(masked, -1))
        terms = jnp.where(allowed, jnp.exp(masked - new_max[..., None]), 0.0)
        return (new_max, run_sum * jnp.exp(run_max - new_max) + jnp.sum(terms, -1))

    start_stats = (
        jnp.full((head_count, num_rows), neg_large, jnp.float32),
        jnp.zeros((head_count, num_rows), jnp.float32),
    )
    run_max, run_sum = lax.fori_loop(key_first, causal_limit, stats_step, start_stats)
    log_total = run_max + jnp.log(run_sum)

    def output_step(block_index, carried):
        key_blk, value_blk, key_pos, key_seg = take_block(block_index)
        scores, allowed = block_scores(query_rows, key_blk, positions, key_pos, seg_own, key_seg)
        prob_b = jnp.where(
            allowed, jnp.exp(jnp.where(allowed, scores - log_total[..., None], neg_large)), 0.0
        ).astype(jnp.bfloat16)
        return carried + jnp.einsum(
            "hrk,kd->rhd", prob_b, value_blk, preferred_element_type=jnp.float32
        )

    out_sum = lax.fori_loop(
        key_first, causal_limit, output_step, jnp.zeros((num_rows, head_count, 128), jnp.float32)
    )
    out_rows = out_sum.astype(jnp.bfloat16)
    delta_rows = jnp.einsum("rhd,rhd->hr", dout_rows, out_rows, preferred_element_type=jnp.float32)

    def sums_step(block_index, carried):
        grad_q, part_k, part_v = carried
        first_row = block_index * kblock
        key_blk, value_blk, key_pos, key_seg = take_block(block_index)
        prob_b, d_score = grad_block(
            query_rows, dout_rows, log_total, delta_rows, key_blk, value_blk,
            positions, key_pos, seg_own, key_seg,
        )
        grad_q = grad_q + jnp.einsum(
            "hrk,kd->rhd", d_score, key_blk, preferred_element_type=jnp.float32
        )
        block_k = jnp.einsum("hrk,rhd->kd", d_score, query_rows, preferred_element_type=jnp.float32)
        block_v = jnp.einsum("hrk,rhd->kd", prob_b, dout_rows, preferred_element_type=jnp.float32)
        part_k = lax.dynamic_update_slice_in_dim(
            part_k, lax.dynamic_slice_in_dim(part_k, first_row, kblock, 0) + block_k, first_row, 0
        )
        part_v = lax.dynamic_update_slice_in_dim(
            part_v, lax.dynamic_slice_in_dim(part_v, first_row, kblock, 0) + block_v, first_row, 0
        )
        return (grad_q, part_k, part_v)

    start_sums = (
        jnp.zeros((num_rows, head_count, 128), jnp.float32),
        jnp.zeros((seq_len, 128), jnp.float32),
        jnp.zeros((seq_len, 128), jnp.float32),
    )
    grad_q, part_k, part_v = lax.fori_loop(key_first, causal_limit, sums_step, start_sums)
    return out_rows, grad_q, part_k, part_v


def attend(query_rows, key_all, value_all, dout_rows, positions, all_pos, seg_own, seg_all):
    head_count, num_rows, seq_len = query_rows.shape[1], query_rows.shape[0], key_all.shape[0]
    operands = (query_rows, key_all, value_all, dout_rows, positions, all_pos, seg_own, seg_all)
    if head_count * num_rows * seq_len <= (1 << 22):
        return attend_whole(*operands)
    kblock = seq_len
    while head_count * num_rows * kblock > (1 << 21) and kblock % 256 == 0:
        kblock //= 2
    return attend_blocked(*operands, kblock)


def local(hidden_in, w_query, w_key, w_value, lengths, attn_grad):
    num_rows = hidden_in.shape[0]
    head_count = w_query.shape[1] // 128
    first_heads = head_count // 2 if head_count % 2 == 0 else head_count
    first_cols = first_heads * 128
    query_cols = head_count * 128
    start_row = lax.axis_index("ctx") * num_rows
    seq_len = num_rows * lax.axis_size("ctx")
    positions = start_row + jnp.arange(num_rows, dtype=jnp.int32)
    all_pos = jnp.arange(seq_len, dtype=jnp.int32)
    seg_all = segment_ids(lengths[0], all_pos)
    seg_own = lax.dynamic_slice_in_dim(seg_all, start_row, num_rows)
    cosine, sine_table = rope_tables(positions)
    rows_axes = ("dp", "ctx")
    group_count = lax.axis_size(rows_axes)
    head_groups = lax.axis_size("head")
    local_a = jnp.concatenate([w_query[:, :first_cols], w_key, w_value], 1)
    full_a = lax.all_gather(local_a, rows_axes, axis=0, tiled=True)
    split_rows = num_rows % head_groups == 0
    if split_rows:
        quarter = num_rows // head_groups
        own_rows = lax.dynamic_slice_in_dim(hidden_in, lax.axis_index("head") * quarter, quarter, 0)
        cols_part = lax.all_to_all(own_rows, rows_axes, 1, 0, tiled=True)
        spread = jnp.broadcast_to(cols_part[None], (head_groups,) + cols_part.shape)
        cols_all = lax.all_to_all(spread, "head", 0, 0, tiled=False)
        hidden_cols = (
            cols_all.reshape(head_groups, group_count, quarter, -1)
            .transpose(1, 0, 2, 3)
            .reshape(group_count * num_rows, -1)
        )
    else:
        hidden_cols = lax.all_to_all(hidden_in, rows_axes, 1, 0, tiled=True)
    full_a, w_query, hidden_cols = lax.optimization_barrier((full_a, w_query, hidden_cols))
    proj_a = jnp.dot(hidden_in, full_a, preferred_element_type=jnp.float32)
    query_a = rotate(
        proj_a[:, :first_cols].reshape(num_rows, first_heads, 128), cosine, sine_table
    ).astype(jnp.bfloat16)
    key_rows = rotate(
        proj_a[:, first_cols : first_cols + 128].reshape(num_rows, 1, 128), cosine, sine_table
    )[:, 0, :].astype(jnp.bfloat16)
    value_rows = proj_a[:, first_cols + 128 :].astype(jnp.bfloat16)
    ctx_index, ctx_count = lax.axis_index("ctx"), lax.axis_size("ctx")
    kv_rows = jnp.concatenate([key_rows, value_rows], 1)
    if ctx_count == 2:
        kv_other = lax.ppermute(kv_rows, "ctx", [(0, 1), (1, 0)])
        kv_all = jnp.where(
            ctx_index == 0,
            jnp.concatenate([kv_rows, kv_other], 0),
            jnp.concatenate([kv_other, kv_rows], 0),
        )
    else:
        kv_all = lax.all_gather(kv_rows, "ctx", axis=0, tiled=True)
    key_all, value_all = kv_all[:, :128], kv_all[:, 128:]
    dout_rows = attn_grad.reshape(num_rows, head_count, 128)
    shared = (key_all, value_all)
    masks = (positions, all_pos, seg_own, seg_all)
    out_a, grad_qa, part_k, part_v = attend(query_a, *shared, dout_rows[:, :first_heads], *masks)
    d_query_a = unrotate(grad_qa, cosine, sine_table).astype(jnp.bfloat16).reshape(num_rows, -1)
    out_parts, d_query_parts = [out_a], [d_query_a]
    if first_heads < head_count:
        w_rest = w_query[:, first_cols:]
        full_b = lax.all_gather(w_rest, rows_axes, axis=0, tiled=True)
        d_query_a, full_b = lax.optimization_barrier((d_query_a, full_b))
        early_all = lax.all_gather(d_query_a, rows_axes, axis=0, tiled=True)
        proj_b = jnp.dot(hidden_in, full_b, preferred_element_type=jnp.float32)
        query_b = rotate(
            proj_b.reshape(num_rows, head_count - first_heads, 128), cosine, sine_table
        ).astype(jnp.bfloat16)
        out_b, grad_qb, part_kb, part_vb = attend(
            query_b, *shared, dout_rows[:, first_heads:], *masks
        )
        early_all, part_kb, part_vb = lax.optimization_barrier((early_all, part_kb, part_vb))
        part_k, part_v = part_k + part_kb, part_v + part_vb
        out_parts.append(out_b)
        d_query_b = unrotate(grad_qb, cosine, sine_table).astype(jnp.bfloat16).reshape(num_rows, -1)
        d_query_parts.append(d_query_b)
    attended = jnp.concatenate(out_parts, 1).reshape(num_rows, query_cols)
    parts_kv = jnp.concatenate([part_k, part_v], 1)
    if ctx_count == 2:
        own_part = lax.dynamic_slice_in_dim(parts_kv, ctx_index * num_rows, num_rows, 0)
        away_part = lax.dynamic_slice_in_dim(parts_kv, (1 - ctx_index) * num_rows, num_rows, 0)
        grad_kv = own_part + lax.ppermute(away_part, "ctx", [(0, 1), (1, 0)])
    else:
        grad_kv = lax.psum_scatter(parts_kv, "ctx", scatter_dimension=0, tiled=True)
    grad_k, grad_v = grad_kv[:, :128], grad_kv[:, 128:]
    d_key = unrotate(grad_k[:, None, :], cosine, sine_table)[:, 0, :].astype(jnp.bfloat16)
    d_value = grad_v.astype(jnp.bfloat16)
    d_proj_a = jnp.concatenate([d_query_a, d_key, d_value], 1)
    input_part = lax.dot_general(
        d_proj_a, full_a, (((1,), (1,)), ((), ())), preferred_element_type=jnp.float32
    )
    if first_heads < head_count:
        input_part = input_part + lax.dot_general(
            d_query_b, full_b, (((1,), (1,)), ((), ())), preferred_element_type=jnp.float32
        )
        late_proj = jnp.concatenate([d_query_b, d_key, d_value], 1)
        early_sum = lax.dot_general(
            hidden_cols, early_all, (((0,), (0,)), ((), ())), preferred_element_type=jnp.float32
        )
    else:
        late_proj = jnp.concatenate([d_key, d_value], 1)
        early_all = lax.all_gather(d_query_a, rows_axes, axis=0, tiled=True)
        early_sum = lax.dot_general(
            hidden_cols, early_all, (((0,), (0,)), ((), ())), preferred_element_type=jnp.float32
        )
    input_cols = input_part.shape[1] // head_groups
    input_split = lax.all_to_all(
        input_part.astype(jnp.bfloat16).reshape(num_rows, head_groups, input_cols),
        "head", 1, 1, tiled=False,
    )
    grad_input = jnp.sum(input_split.astype(jnp.float32), axis=1).astype(jnp.bfloat16)
    late_all = lax.all_gather(late_proj, rows_axes, axis=0, tiled=True)
    late_sum = lax.dot_general(
        hidden_cols, late_all, (((0,), (0,)), ((), ())), preferred_element_type=jnp.float32
    )
    query_w = jnp.concatenate([early_sum, late_sum[:, : query_cols - first_cols]], 1)
    rest = late_sum[:, query_cols - first_cols :]
    return (attended, grad_input, query_w, rest[:, :128], rest[:, 128:])


def solution(mesh):
    placed = (
        P(("dp", "ctx"), None),
        P(("dp", "ctx"), "head"),
        P(("dp", "ctx"), "head"),
        P(("dp", "ctx"), "head"),
        P("dp", None),
        P(("dp", "ctx"), "head"),
    )
    return jax.shard_map(
        local,
        mesh=mesh,
        in_specs=placed,
        out_specs=(
            P(("dp", "ctx"), "head"),
            P(("dp", "ctx"), "head"),
            P(("dp", "ctx"), "head"),
            P(("dp", "ctx"), "head"),
            P(("dp", "ctx"), "head"),
        ),
        check_vma=False,
    )
```

```python
import jax
import jax.numpy as jnp
from jax import lax
from jax.sharding import PartitionSpec as P

scale_factor = 128.0 ** (-0.5)
neg_large = -1e30


def rope_tables(positions):
    inverse = jnp.power(500000.0, -jnp.arange(64, dtype=jnp.float32) / 64.0)
    angles = positions.astype(jnp.float32)[:, None] * inverse[None, :]
    return (jnp.cos(angles)[:, None, :], jnp.sin(angles)[:, None, :])


def rotate(entries, cosine, sine_table):
    first_half = entries[..., :64]
    second_half = entries[..., 64:]
    return jnp.concatenate(
        [
            first_half * cosine - second_half * sine_table,
            second_half * cosine + first_half * sine_table,
        ],
        -1,
    )


def unrotate(entries, cosine, sine_table):
    first_half = entries[..., :64]
    second_half = entries[..., 64:]
    return jnp.concatenate(
        [
            first_half * cosine + second_half * sine_table,
            second_half * cosine - first_half * sine_table,
        ],
        -1,
    )


def segment_ids(length_row, positions):
    ends = jnp.cumsum(length_row)
    return jnp.sum((positions[:, None] >= ends[None, :]).astype(jnp.int32), 1)


def block_scores(query_blk, key_blk, query_pos, key_pos, query_seg, key_seg):
    scores = (
        jnp.einsum("rhd,kd->hrk", query_blk, key_blk, preferred_element_type=jnp.float32)
        * scale_factor
    )
    allowed = (key_pos[None, :] <= query_pos[:, None]) & (key_seg[None, :] == query_seg[:, None])
    return (scores, allowed[None])


def grad_block(
    query_blk,
    dout_blk,
    total_blk,
    delta_blk,
    key_blk,
    value_blk,
    query_pos,
    key_pos,
    query_seg,
    key_seg,
):
    scores, allowed = block_scores(query_blk, key_blk, query_pos, key_pos, query_seg, key_seg)
    prob_rows = jnp.where(
        allowed, jnp.exp(jnp.where(allowed, scores - total_blk[..., None], neg_large)), 0.0
    )
    prob_b = prob_rows.astype(jnp.bfloat16)
    d_prob = jnp.einsum("rhd,kd->hrk", dout_blk, value_blk, preferred_element_type=jnp.float32)
    d_score = (scale_factor * prob_rows * (d_prob - delta_blk[..., None])).astype(jnp.bfloat16)
    return (prob_b, d_score)


def attend_whole(query_rows, key_all, value_all, dout_rows, positions, all_pos, seg_own, seg_all):
    scores, allowed = block_scores(query_rows, key_all, positions, all_pos, seg_own, seg_all)
    masked = jnp.where(allowed, scores, neg_large)
    top_score = jnp.max(masked, -1)
    total = jnp.sum(jnp.where(allowed, jnp.exp(masked - top_score[..., None]), 0.0), -1)
    log_total = top_score + jnp.log(total)
    prob_rows = jnp.where(
        allowed, jnp.exp(jnp.where(allowed, scores - log_total[..., None], neg_large)), 0.0
    )
    prob_b = prob_rows.astype(jnp.bfloat16)
    out_rows = jnp.einsum(
        "hrk,kd->rhd", prob_b, value_all, preferred_element_type=jnp.float32
    ).astype(jnp.bfloat16)
    delta_rows = jnp.einsum("rhd,rhd->hr", dout_rows, out_rows, preferred_element_type=jnp.float32)
    d_prob = jnp.einsum("rhd,kd->hrk", dout_rows, value_all, preferred_element_type=jnp.float32)
    d_score = (scale_factor * prob_rows * (d_prob - delta_rows[..., None])).astype(jnp.bfloat16)
    grad_q = jnp.einsum("hrk,kd->rhd", d_score, key_all, preferred_element_type=jnp.float32)
    part_k = jnp.einsum("hrk,rhd->kd", d_score, query_rows, preferred_element_type=jnp.float32)
    part_v = jnp.einsum("hrk,rhd->kd", prob_b, dout_rows, preferred_element_type=jnp.float32)
    return out_rows, grad_q, part_k, part_v


def attend_blocked(query_rows, key_all, value_all, dout_rows, positions, all_pos, seg_own, seg_all, kblock):
    num_rows, head_count = query_rows.shape[0], query_rows.shape[1]
    seq_len = key_all.shape[0]
    causal_limit = (positions[-1] + kblock) // kblock
    key_first = jnp.int32(0)

    def take_block(block_index):
        first_row = block_index * kblock
        return (
            lax.dynamic_slice_in_dim(key_all, first_row, kblock, 0),
            lax.dynamic_slice_in_dim(value_all, first_row, kblock, 0),
            lax.dynamic_slice_in_dim(all_pos, first_row, kblock, 0),
            lax.dynamic_slice_in_dim(seg_all, first_row, kblock, 0),
        )

    def stats_step(block_index, carried):
        run_max, run_sum = carried
        key_blk, value_blk, key_pos, key_seg = take_block(block_index)
        scores, allowed = block_scores(query_rows, key_blk, positions, key_pos, seg_own, key_seg)
        masked = jnp.where(allowed, scores, neg_large)
        new_max = jnp.maximum(run_max, jnp.max(masked, -1))
        terms = jnp.where(allowed, jnp.exp(masked - new_max[..., None]), 0.0)
        return (new_max, run_sum * jnp.exp(run_max - new_max) + jnp.sum(terms, -1))

    start_stats = (
        jnp.full((head_count, num_rows), neg_large, jnp.float32),
        jnp.zeros((head_count, num_rows), jnp.float32),
    )
    run_max, run_sum = lax.fori_loop(key_first, causal_limit, stats_step, start_stats)
    log_total = run_max + jnp.log(run_sum)

    def output_step(block_index, carried):
        key_blk, value_blk, key_pos, key_seg = take_block(block_index)
        scores, allowed = block_scores(query_rows, key_blk, positions, key_pos, seg_own, key_seg)
        prob_b = jnp.where(
            allowed, jnp.exp(jnp.where(allowed, scores - log_total[..., None], neg_large)), 0.0
        ).astype(jnp.bfloat16)
        return carried + jnp.einsum(
            "hrk,kd->rhd", prob_b, value_blk, preferred_element_type=jnp.float32
        )

    out_sum = lax.fori_loop(
        key_first, causal_limit, output_step, jnp.zeros((num_rows, head_count, 128), jnp.float32)
    )
    out_rows = out_sum.astype(jnp.bfloat16)
    delta_rows = jnp.einsum("rhd,rhd->hr", dout_rows, out_rows, preferred_element_type=jnp.float32)

    def sums_step(block_index, carried):
        grad_q, part_k, part_v = carried
        first_row = block_index * kblock
        key_blk, value_blk, key_pos, key_seg = take_block(block_index)
        prob_b, d_score = grad_block(
            query_rows, dout_rows, log_total, delta_rows, key_blk, value_blk,
            positions, key_pos, seg_own, key_seg,
        )
        grad_q = grad_q + jnp.einsum(
            "hrk,kd->rhd", d_score, key_blk, preferred_element_type=jnp.float32
        )
        block_k = jnp.einsum("hrk,rhd->kd", d_score, query_rows, preferred_element_type=jnp.float32)
        block_v = jnp.einsum("hrk,rhd->kd", prob_b, dout_rows, preferred_element_type=jnp.float32)
        part_k = lax.dynamic_update_slice_in_dim(
            part_k, lax.dynamic_slice_in_dim(part_k, first_row, kblock, 0) + block_k, first_row, 0
        )
        part_v = lax.dynamic_update_slice_in_dim(
            part_v, lax.dynamic_slice_in_dim(part_v, first_row, kblock, 0) + block_v, first_row, 0
        )
        return (grad_q, part_k, part_v)

    start_sums = (
        jnp.zeros((num_rows, head_count, 128), jnp.float32),
        jnp.zeros((seq_len, 128), jnp.float32),
        jnp.zeros((seq_len, 128), jnp.float32),
    )
    grad_q, part_k, part_v = lax.fori_loop(key_first, causal_limit, sums_step, start_sums)
    return out_rows, grad_q, part_k, part_v


def attend(query_rows, key_all, value_all, dout_rows, positions, all_pos, seg_own, seg_all):
    head_count, num_rows, seq_len = query_rows.shape[1], query_rows.shape[0], key_all.shape[0]
    operands = (query_rows, key_all, value_all, dout_rows, positions, all_pos, seg_own, seg_all)
    if head_count * num_rows * seq_len <= (1 << 22):
        return attend_whole(*operands)
    kblock = seq_len
    while head_count * num_rows * kblock > (1 << 21) and kblock % 256 == 0:
        kblock //= 2
    return attend_blocked(*operands, kblock)


def local(hidden_in, w_query, w_key, w_value, lengths, attn_grad):
    num_rows = hidden_in.shape[0]
    head_count = w_query.shape[1] // 128
    first_heads = head_count // 2 if head_count % 2 == 0 else head_count
    first_cols = first_heads * 128
    query_cols = head_count * 128
    start_row = lax.axis_index("ctx") * num_rows
    seq_len = num_rows * lax.axis_size("ctx")
    positions = start_row + jnp.arange(num_rows, dtype=jnp.int32)
    all_pos = jnp.arange(seq_len, dtype=jnp.int32)
    seg_all = segment_ids(lengths[0], all_pos)
    seg_own = lax.dynamic_slice_in_dim(seg_all, start_row, num_rows)
    cosine, sine_table = rope_tables(positions)
    rows_axes = ("dp", "ctx")
    group_count = lax.axis_size(rows_axes)
    head_groups = lax.axis_size("head")
    local_a = jnp.concatenate([w_query[:, :first_cols], w_key, w_value], 1)
    full_a = lax.all_gather(local_a, rows_axes, axis=0, tiled=True)
    split_rows = num_rows % head_groups == 0
    if split_rows:
        quarter = num_rows // head_groups
        own_rows = lax.dynamic_slice_in_dim(hidden_in, lax.axis_index("head") * quarter, quarter, 0)
        cols_part = lax.all_to_all(own_rows, rows_axes, 1, 0, tiled=True)
    else:
        cols_part = lax.all_to_all(hidden_in, rows_axes, 1, 0, tiled=True)
    full_a, w_query, cols_part = lax.optimization_barrier((full_a, w_query, cols_part))
    hidden_cols = cols_part
    if split_rows:
        spread = jnp.broadcast_to(cols_part[None], (head_groups,) + cols_part.shape)
        cols_all = lax.all_to_all(spread, "head", 0, 0, tiled=False)
        hidden_cols = (
            cols_all.reshape(head_groups, group_count, quarter, -1)
            .transpose(1, 0, 2, 3)
            .reshape(group_count * num_rows, -1)
        )
    proj_a = jnp.dot(hidden_in, full_a, preferred_element_type=jnp.float32)
    query_a = rotate(
        proj_a[:, :first_cols].reshape(num_rows, first_heads, 128), cosine, sine_table
    ).astype(jnp.bfloat16)
    key_rows = rotate(
        proj_a[:, first_cols : first_cols + 128].reshape(num_rows, 1, 128), cosine, sine_table
    )[:, 0, :].astype(jnp.bfloat16)
    value_rows = proj_a[:, first_cols + 128 :].astype(jnp.bfloat16)
    ctx_index, ctx_count = lax.axis_index("ctx"), lax.axis_size("ctx")
    kv_rows = jnp.concatenate([key_rows, value_rows], 1)
    if ctx_count == 2:
        kv_other = lax.ppermute(kv_rows, "ctx", [(0, 1), (1, 0)])
        kv_all = jnp.where(
            ctx_index == 0,
            jnp.concatenate([kv_rows, kv_other], 0),
            jnp.concatenate([kv_other, kv_rows], 0),
        )
    else:
        kv_all = lax.all_gather(kv_rows, "ctx", axis=0, tiled=True)
    key_all, value_all = kv_all[:, :128], kv_all[:, 128:]
    dout_rows = attn_grad.reshape(num_rows, head_count, 128)
    shared = (key_all, value_all)
    masks = (positions, all_pos, seg_own, seg_all)
    out_a, grad_qa, part_k, part_v = attend(query_a, *shared, dout_rows[:, :first_heads], *masks)
    d_query_a = unrotate(grad_qa, cosine, sine_table).astype(jnp.bfloat16).reshape(num_rows, -1)
    out_parts, d_query_parts = [out_a], [d_query_a]
    if first_heads < head_count:
        w_rest = w_query[:, first_cols:]
        full_b = lax.all_gather(w_rest, rows_axes, axis=0, tiled=True)
        d_query_a, full_b, hidden_cols = lax.optimization_barrier((d_query_a, full_b, hidden_cols))
        early_all = lax.all_gather(d_query_a, rows_axes, axis=0, tiled=True)
        proj_b = jnp.dot(hidden_in, full_b, preferred_element_type=jnp.float32)
        query_b = rotate(
            proj_b.reshape(num_rows, head_count - first_heads, 128), cosine, sine_table
        ).astype(jnp.bfloat16)
        out_b, grad_qb, part_kb, part_vb = attend(
            query_b, *shared, dout_rows[:, first_heads:], *masks
        )
        d_query_b = unrotate(grad_qb, cosine, sine_table).astype(jnp.bfloat16).reshape(num_rows, -1)
        early_all, d_query_b = lax.optimization_barrier((early_all, d_query_b))
        mid_all = lax.all_gather(d_query_b, rows_axes, axis=0, tiled=True)
        part_k, part_v = part_k + part_kb, part_v + part_vb
        out_parts.append(out_b)
    attended = jnp.concatenate(out_parts, 1).reshape(num_rows, query_cols)
    parts_kv = jnp.concatenate([part_k, part_v], 1)
    if ctx_count == 2:
        own_part = lax.dynamic_slice_in_dim(parts_kv, ctx_index * num_rows, num_rows, 0)
        away_part = lax.dynamic_slice_in_dim(parts_kv, (1 - ctx_index) * num_rows, num_rows, 0)
        grad_kv = own_part + lax.ppermute(away_part, "ctx", [(0, 1), (1, 0)])
    else:
        grad_kv = lax.psum_scatter(parts_kv, "ctx", scatter_dimension=0, tiled=True)
    grad_k, grad_v = grad_kv[:, :128], grad_kv[:, 128:]
    d_key = unrotate(grad_k[:, None, :], cosine, sine_table)[:, 0, :].astype(jnp.bfloat16)
    d_value = grad_v.astype(jnp.bfloat16)
    d_proj_a = jnp.concatenate([d_query_a, d_key, d_value], 1)
    input_part = lax.dot_general(
        d_proj_a, full_a, (((1,), (1,)), ((), ())), preferred_element_type=jnp.float32
    )
    if first_heads < head_count:
        input_part = input_part + lax.dot_general(
            d_query_b, full_b, (((1,), (1,)), ((), ())), preferred_element_type=jnp.float32
        )
        late_proj = jnp.concatenate([d_key, d_value], 1)
        early_sum = lax.dot_general(
            hidden_cols,
            jnp.concatenate([early_all, mid_all], 1),
            (((0,), (0,)), ((), ())),
            preferred_element_type=jnp.float32,
        )
    else:
        late_proj = jnp.concatenate([d_key, d_value], 1)
        early_all = lax.all_gather(d_query_a, rows_axes, axis=0, tiled=True)
        early_sum = lax.dot_general(
            hidden_cols, early_all, (((0,), (0,)), ((), ())), preferred_element_type=jnp.float32
        )
    input_cols = input_part.shape[1] // head_groups
    input_split = lax.all_to_all(
        input_part.astype(jnp.bfloat16).reshape(num_rows, head_groups, input_cols),
        "head", 1, 1, tiled=False,
    )
    grad_input = jnp.sum(input_split.astype(jnp.float32), axis=1).astype(jnp.bfloat16)
    late_spread = jnp.broadcast_to(late_proj[None], (group_count,) + late_proj.shape)
    late_all = lax.all_to_all(late_spread, rows_axes, 0, 0, tiled=False).reshape(
        group_count * num_rows, -1
    )
    late_sum = lax.dot_general(
        hidden_cols, late_all, (((0,), (0,)), ((), ())), preferred_element_type=jnp.float32
    )
    query_w = early_sum
    rest = late_sum
    return (attended, grad_input, query_w, rest[:, :128], rest[:, 128:])


def solution(mesh):
    placed = (
        P(("dp", "ctx"), None),
        P(("dp", "ctx"), "head"),
        P(("dp", "ctx"), "head"),
        P(("dp", "ctx"), "head"),
        P("dp", None),
        P(("dp", "ctx"), "head"),
    )
    return jax.shard_map(
        local,
        mesh=mesh,
        in_specs=placed,
        out_specs=(
            P(("dp", "ctx"), "head"),
            P(("dp", "ctx"), "head"),
            P(("dp", "ctx"), "head"),
            P(("dp", "ctx"), "head"),
            P(("dp", "ctx"), "head"),
        ),
        check_vma=False,
    )
```

```python
import jax
import jax.numpy as jnp
from jax import lax
from jax.sharding import PartitionSpec as P

scale_factor = 128.0 ** (-0.5)
neg_large = -1e30


def rope_tables(positions):
    inverse = jnp.power(500000.0, -jnp.arange(64, dtype=jnp.float32) / 64.0)
    angles = positions.astype(jnp.float32)[:, None] * inverse[None, :]
    return (jnp.cos(angles)[:, None, :], jnp.sin(angles)[:, None, :])


def rotate(entries, cosine, sine_table):
    first_half = entries[..., :64]
    second_half = entries[..., 64:]
    return jnp.concatenate(
        [
            first_half * cosine - second_half * sine_table,
            second_half * cosine + first_half * sine_table,
        ],
        -1,
    )


def unrotate(entries, cosine, sine_table):
    first_half = entries[..., :64]
    second_half = entries[..., 64:]
    return jnp.concatenate(
        [
            first_half * cosine + second_half * sine_table,
            second_half * cosine - first_half * sine_table,
        ],
        -1,
    )


def segment_ids(length_row, positions):
    ends = jnp.cumsum(length_row)
    return jnp.sum((positions[:, None] >= ends[None, :]).astype(jnp.int32), 1)


def block_scores(query_blk, key_blk, query_pos, key_pos, query_seg, key_seg):
    scores = (
        jnp.einsum("rhd,kd->hrk", query_blk, key_blk, preferred_element_type=jnp.float32)
        * scale_factor
    )
    allowed = (key_pos[None, :] <= query_pos[:, None]) & (key_seg[None, :] == query_seg[:, None])
    return (scores, allowed[None])


def grad_block(
    query_blk,
    dout_blk,
    total_blk,
    delta_blk,
    key_blk,
    value_blk,
    query_pos,
    key_pos,
    query_seg,
    key_seg,
):
    scores, allowed = block_scores(query_blk, key_blk, query_pos, key_pos, query_seg, key_seg)
    prob_rows = jnp.where(
        allowed, jnp.exp(jnp.where(allowed, scores - total_blk[..., None], neg_large)), 0.0
    )
    prob_b = prob_rows.astype(jnp.bfloat16)
    d_prob = jnp.einsum("rhd,kd->hrk", dout_blk, value_blk, preferred_element_type=jnp.float32)
    d_score = (scale_factor * prob_rows * (d_prob - delta_blk[..., None])).astype(jnp.bfloat16)
    return (prob_b, d_score)


def attend_whole(query_rows, key_all, value_all, dout_rows, positions, all_pos, seg_own, seg_all):
    scores, allowed = block_scores(query_rows, key_all, positions, all_pos, seg_own, seg_all)
    masked = jnp.where(allowed, scores, neg_large)
    top_score = jnp.max(masked, -1)
    total = jnp.sum(jnp.where(allowed, jnp.exp(masked - top_score[..., None]), 0.0), -1)
    log_total = top_score + jnp.log(total)
    prob_rows = jnp.where(
        allowed, jnp.exp(jnp.where(allowed, scores - log_total[..., None], neg_large)), 0.0
    )
    prob_b = prob_rows.astype(jnp.bfloat16)
    out_rows = jnp.einsum(
        "hrk,kd->rhd", prob_b, value_all, preferred_element_type=jnp.float32
    ).astype(jnp.bfloat16)
    delta_rows = jnp.einsum("rhd,rhd->hr", dout_rows, out_rows, preferred_element_type=jnp.float32)
    d_prob = jnp.einsum("rhd,kd->hrk", dout_rows, value_all, preferred_element_type=jnp.float32)
    d_score = (scale_factor * prob_rows * (d_prob - delta_rows[..., None])).astype(jnp.bfloat16)
    grad_q = jnp.einsum("hrk,kd->rhd", d_score, key_all, preferred_element_type=jnp.float32)
    part_k = jnp.einsum("hrk,rhd->kd", d_score, query_rows, preferred_element_type=jnp.float32)
    part_v = jnp.einsum("hrk,rhd->kd", prob_b, dout_rows, preferred_element_type=jnp.float32)
    return out_rows, grad_q, part_k, part_v


def attend_blocked(query_rows, key_all, value_all, dout_rows, positions, all_pos, seg_own, seg_all, kblock):
    num_rows, head_count = query_rows.shape[0], query_rows.shape[1]
    seq_len = key_all.shape[0]
    causal_limit = (positions[-1] + kblock) // kblock
    key_first = jnp.int32(0)

    def take_block(block_index):
        first_row = block_index * kblock
        return (
            lax.dynamic_slice_in_dim(key_all, first_row, kblock, 0),
            lax.dynamic_slice_in_dim(value_all, first_row, kblock, 0),
            lax.dynamic_slice_in_dim(all_pos, first_row, kblock, 0),
            lax.dynamic_slice_in_dim(seg_all, first_row, kblock, 0),
        )

    def stats_step(block_index, carried):
        run_max, run_sum = carried
        key_blk, value_blk, key_pos, key_seg = take_block(block_index)
        scores, allowed = block_scores(query_rows, key_blk, positions, key_pos, seg_own, key_seg)
        masked = jnp.where(allowed, scores, neg_large)
        new_max = jnp.maximum(run_max, jnp.max(masked, -1))
        terms = jnp.where(allowed, jnp.exp(masked - new_max[..., None]), 0.0)
        return (new_max, run_sum * jnp.exp(run_max - new_max) + jnp.sum(terms, -1))

    start_stats = (
        jnp.full((head_count, num_rows), neg_large, jnp.float32),
        jnp.zeros((head_count, num_rows), jnp.float32),
    )
    run_max, run_sum = lax.fori_loop(key_first, causal_limit, stats_step, start_stats)
    log_total = run_max + jnp.log(run_sum)

    def output_step(block_index, carried):
        key_blk, value_blk, key_pos, key_seg = take_block(block_index)
        scores, allowed = block_scores(query_rows, key_blk, positions, key_pos, seg_own, key_seg)
        prob_b = jnp.where(
            allowed, jnp.exp(jnp.where(allowed, scores - log_total[..., None], neg_large)), 0.0
        ).astype(jnp.bfloat16)
        return carried + jnp.einsum(
            "hrk,kd->rhd", prob_b, value_blk, preferred_element_type=jnp.float32
        )

    out_sum = lax.fori_loop(
        key_first, causal_limit, output_step, jnp.zeros((num_rows, head_count, 128), jnp.float32)
    )
    out_rows = out_sum.astype(jnp.bfloat16)
    delta_rows = jnp.einsum("rhd,rhd->hr", dout_rows, out_rows, preferred_element_type=jnp.float32)

    def sums_step(block_index, carried):
        grad_q, part_k, part_v = carried
        first_row = block_index * kblock
        key_blk, value_blk, key_pos, key_seg = take_block(block_index)
        prob_b, d_score = grad_block(
            query_rows, dout_rows, log_total, delta_rows, key_blk, value_blk,
            positions, key_pos, seg_own, key_seg,
        )
        grad_q = grad_q + jnp.einsum(
            "hrk,kd->rhd", d_score, key_blk, preferred_element_type=jnp.float32
        )
        block_k = jnp.einsum("hrk,rhd->kd", d_score, query_rows, preferred_element_type=jnp.float32)
        block_v = jnp.einsum("hrk,rhd->kd", prob_b, dout_rows, preferred_element_type=jnp.float32)
        part_k = lax.dynamic_update_slice_in_dim(
            part_k, lax.dynamic_slice_in_dim(part_k, first_row, kblock, 0) + block_k, first_row, 0
        )
        part_v = lax.dynamic_update_slice_in_dim(
            part_v, lax.dynamic_slice_in_dim(part_v, first_row, kblock, 0) + block_v, first_row, 0
        )
        return (grad_q, part_k, part_v)

    start_sums = (
        jnp.zeros((num_rows, head_count, 128), jnp.float32),
        jnp.zeros((seq_len, 128), jnp.float32),
        jnp.zeros((seq_len, 128), jnp.float32),
    )
    grad_q, part_k, part_v = lax.fori_loop(key_first, causal_limit, sums_step, start_sums)
    return out_rows, grad_q, part_k, part_v


def attend(query_rows, key_all, value_all, dout_rows, positions, all_pos, seg_own, seg_all):
    head_count, num_rows, seq_len = query_rows.shape[1], query_rows.shape[0], key_all.shape[0]
    operands = (query_rows, key_all, value_all, dout_rows, positions, all_pos, seg_own, seg_all)
    if head_count * num_rows * seq_len <= (1 << 22):
        return attend_whole(*operands)
    kblock = seq_len
    while head_count * num_rows * kblock > (1 << 21) and kblock % 256 == 0:
        kblock //= 2
    return attend_blocked(*operands, kblock)


def local(hidden_in, w_query, w_key, w_value, lengths, attn_grad):
    num_rows = hidden_in.shape[0]
    head_count = w_query.shape[1] // 128
    first_heads = head_count // 2 if head_count % 2 == 0 else head_count
    first_cols = first_heads * 128
    query_cols = head_count * 128
    start_row = lax.axis_index("ctx") * num_rows
    seq_len = num_rows * lax.axis_size("ctx")
    positions = start_row + jnp.arange(num_rows, dtype=jnp.int32)
    all_pos = jnp.arange(seq_len, dtype=jnp.int32)
    seg_all = segment_ids(lengths[0], all_pos)
    seg_own = lax.dynamic_slice_in_dim(seg_all, start_row, num_rows)
    cosine, sine_table = rope_tables(positions)
    rows_axes = ("dp", "ctx")
    group_count = lax.axis_size(rows_axes)
    head_groups = lax.axis_size("head")
    local_a = jnp.concatenate([w_query[:, :first_cols], w_key, w_value], 1)
    full_a = lax.all_gather(local_a, rows_axes, axis=0, tiled=True)
    split_rows = num_rows % head_groups == 0
    if split_rows:
        quarter = num_rows // head_groups
        own_rows = lax.dynamic_slice_in_dim(hidden_in, lax.axis_index("head") * quarter, quarter, 0)
        cols_part = lax.all_to_all(own_rows, rows_axes, 1, 0, tiled=True)
    else:
        cols_part = lax.all_to_all(hidden_in, rows_axes, 1, 0, tiled=True)
    full_a, w_query, cols_part = lax.optimization_barrier((full_a, w_query, cols_part))
    hidden_cols = cols_part
    if split_rows:
        spread = jnp.broadcast_to(cols_part[None], (head_groups,) + cols_part.shape)
        cols_all = lax.all_to_all(spread, "head", 0, 0, tiled=False)
        hidden_cols = (
            cols_all.reshape(head_groups, group_count, quarter, -1)
            .transpose(1, 0, 2, 3)
            .reshape(group_count * num_rows, -1)
        )
    proj_a = jnp.dot(hidden_in, full_a, preferred_element_type=jnp.float32)
    query_a = rotate(
        proj_a[:, :first_cols].reshape(num_rows, first_heads, 128), cosine, sine_table
    ).astype(jnp.bfloat16)
    key_rows = rotate(
        proj_a[:, first_cols : first_cols + 128].reshape(num_rows, 1, 128), cosine, sine_table
    )[:, 0, :].astype(jnp.bfloat16)
    value_rows = proj_a[:, first_cols + 128 :].astype(jnp.bfloat16)
    ctx_index, ctx_count = lax.axis_index("ctx"), lax.axis_size("ctx")
    kv_rows = jnp.concatenate([key_rows, value_rows], 1)
    if ctx_count == 2:
        kv_other = lax.ppermute(kv_rows, "ctx", [(0, 1), (1, 0)])
        kv_all = jnp.where(
            ctx_index == 0,
            jnp.concatenate([kv_rows, kv_other], 0),
            jnp.concatenate([kv_other, kv_rows], 0),
        )
    else:
        kv_all = lax.all_gather(kv_rows, "ctx", axis=0, tiled=True)
    key_all, value_all = kv_all[:, :128], kv_all[:, 128:]
    dout_rows = attn_grad.reshape(num_rows, head_count, 128)
    shared = (key_all, value_all)
    masks = (positions, all_pos, seg_own, seg_all)
    out_a, grad_qa, part_k, part_v = attend(query_a, *shared, dout_rows[:, :first_heads], *masks)
    d_query_a = unrotate(grad_qa, cosine, sine_table).astype(jnp.bfloat16).reshape(num_rows, -1)
    out_parts, d_query_parts = [out_a], [d_query_a]
    if first_heads < head_count:
        w_rest = w_query[:, first_cols:]
        full_b = lax.all_gather(w_rest, rows_axes, axis=0, tiled=True)
        d_query_a, full_b, hidden_cols = lax.optimization_barrier((d_query_a, full_b, hidden_cols))
        early_all = lax.all_gather(d_query_a, rows_axes, axis=0, tiled=True)
        proj_b = jnp.dot(hidden_in, full_b, preferred_element_type=jnp.float32)
        query_b = rotate(
            proj_b.reshape(num_rows, head_count - first_heads, 128), cosine, sine_table
        ).astype(jnp.bfloat16)
        out_b, grad_qb, part_kb, part_vb = attend(
            query_b, *shared, dout_rows[:, first_heads:], *masks
        )
        d_query_b = unrotate(grad_qb, cosine, sine_table).astype(jnp.bfloat16).reshape(num_rows, -1)
        early_all, d_query_b = lax.optimization_barrier((early_all, d_query_b))
        mid_all = lax.all_gather(d_query_b, rows_axes, axis=0, tiled=True)
        part_k, part_v = part_k + part_kb, part_v + part_vb
        out_parts.append(out_b)
    attended = jnp.concatenate(out_parts, 1).reshape(num_rows, query_cols)
    parts_kv = jnp.concatenate([part_k, part_v], 1)
    if ctx_count == 2:
        own_part = lax.dynamic_slice_in_dim(parts_kv, ctx_index * num_rows, num_rows, 0)
        away_part = lax.dynamic_slice_in_dim(parts_kv, (1 - ctx_index) * num_rows, num_rows, 0)
        grad_kv = own_part + lax.ppermute(away_part, "ctx", [(0, 1), (1, 0)])
    else:
        grad_kv = lax.psum_scatter(parts_kv, "ctx", scatter_dimension=0, tiled=True)
    grad_k, grad_v = grad_kv[:, :128], grad_kv[:, 128:]
    d_key = unrotate(grad_k[:, None, :], cosine, sine_table)[:, 0, :].astype(jnp.bfloat16)
    d_value = grad_v.astype(jnp.bfloat16)
    d_proj_a = jnp.concatenate([d_query_a, d_key, d_value], 1)
    input_part = lax.dot_general(
        d_proj_a, full_a, (((1,), (1,)), ((), ())), preferred_element_type=jnp.float32
    )
    if first_heads < head_count:
        input_part = input_part + lax.dot_general(
            d_query_b, full_b, (((1,), (1,)), ((), ())), preferred_element_type=jnp.float32
        )
        late_proj = jnp.concatenate([d_key, d_value], 1)
        early_sum = lax.dot_general(
            hidden_cols,
            jnp.concatenate([early_all, mid_all], 1),
            (((0,), (0,)), ((), ())),
            preferred_element_type=jnp.float32,
        )
    else:
        late_proj = jnp.concatenate([d_key, d_value], 1)
        early_all = lax.all_gather(d_query_a, rows_axes, axis=0, tiled=True)
        early_sum = lax.dot_general(
            hidden_cols, early_all, (((0,), (0,)), ((), ())), preferred_element_type=jnp.float32
        )
    input_cols = input_part.shape[1] // head_groups
    input_split = lax.all_to_all(
        input_part.astype(jnp.bfloat16).reshape(num_rows, head_groups, input_cols),
        "head", 1, 1, tiled=False,
    )
    input_split, late_proj = lax.optimization_barrier((input_split, late_proj))
    grad_input = jnp.sum(input_split.astype(jnp.float32), axis=1).astype(jnp.bfloat16)
    late_spread = jnp.broadcast_to(late_proj[None], (group_count,) + late_proj.shape)
    late_all = lax.all_to_all(late_spread, rows_axes, 0, 0, tiled=False).reshape(
        group_count * num_rows, -1
    )
    late_sum = lax.dot_general(
        hidden_cols, late_all, (((0,), (0,)), ((), ())), preferred_element_type=jnp.float32
    )
    query_w = early_sum
    rest = late_sum
    return (attended, grad_input, query_w, rest[:, :128], rest[:, 128:])


def solution(mesh):
    placed = (
        P(("dp", "ctx"), None),
        P(("dp", "ctx"), "head"),
        P(("dp", "ctx"), "head"),
        P(("dp", "ctx"), "head"),
        P("dp", None),
        P(("dp", "ctx"), "head"),
    )
    return jax.shard_map(
        local,
        mesh=mesh,
        in_specs=placed,
        out_specs=(
            P(("dp", "ctx"), "head"),
            P(("dp", "ctx"), "head"),
            P(("dp", "ctx"), "head"),
            P(("dp", "ctx"), "head"),
            P(("dp", "ctx"), "head"),
        ),
        check_vma=False,
    )
```

```python
import jax
import jax.numpy as jnp
from jax import lax
from jax.sharding import PartitionSpec as P

scale_factor = 128.0 ** (-0.5)
neg_large = -1e30


def rope_tables(positions):
    inverse = jnp.power(500000.0, -jnp.arange(64, dtype=jnp.float32) / 64.0)
    angles = positions.astype(jnp.float32)[:, None] * inverse[None, :]
    return (jnp.cos(angles)[:, None, :], jnp.sin(angles)[:, None, :])


def rotate(entries, cosine, sine_table):
    first_half = entries[..., :64]
    second_half = entries[..., 64:]
    return jnp.concatenate(
        [
            first_half * cosine - second_half * sine_table,
            second_half * cosine + first_half * sine_table,
        ],
        -1,
    )


def unrotate(entries, cosine, sine_table):
    first_half = entries[..., :64]
    second_half = entries[..., 64:]
    return jnp.concatenate(
        [
            first_half * cosine + second_half * sine_table,
            second_half * cosine - first_half * sine_table,
        ],
        -1,
    )


def segment_ids(length_row, positions):
    ends = jnp.cumsum(length_row)
    return jnp.sum((positions[:, None] >= ends[None, :]).astype(jnp.int32), 1)


def block_scores(query_blk, key_blk, query_pos, key_pos, query_seg, key_seg):
    scores = (
        jnp.einsum("rhd,kd->hrk", query_blk, key_blk, preferred_element_type=jnp.float32)
        * scale_factor
    )
    allowed = (key_pos[None, :] <= query_pos[:, None]) & (key_seg[None, :] == query_seg[:, None])
    return (scores, allowed[None])


def grad_block(
    query_blk,
    dout_blk,
    total_blk,
    delta_blk,
    key_blk,
    value_blk,
    query_pos,
    key_pos,
    query_seg,
    key_seg,
):
    scores, allowed = block_scores(query_blk, key_blk, query_pos, key_pos, query_seg, key_seg)
    prob_rows = jnp.where(
        allowed, jnp.exp(jnp.where(allowed, scores - total_blk[..., None], neg_large)), 0.0
    )
    prob_b = prob_rows.astype(jnp.bfloat16)
    d_prob = jnp.einsum("rhd,kd->hrk", dout_blk, value_blk, preferred_element_type=jnp.float32)
    d_score = (scale_factor * prob_rows * (d_prob - delta_blk[..., None])).astype(jnp.bfloat16)
    return (prob_b, d_score)


def attend_whole(query_rows, key_all, value_all, dout_rows, positions, all_pos, seg_own, seg_all):
    scores, allowed = block_scores(query_rows, key_all, positions, all_pos, seg_own, seg_all)
    masked = jnp.where(allowed, scores, neg_large)
    top_score = jnp.max(masked, -1)
    total = jnp.sum(jnp.where(allowed, jnp.exp(masked - top_score[..., None]), 0.0), -1)
    log_total = top_score + jnp.log(total)
    prob_rows = jnp.where(
        allowed, jnp.exp(jnp.where(allowed, scores - log_total[..., None], neg_large)), 0.0
    )
    prob_b = prob_rows.astype(jnp.bfloat16)
    out_rows = jnp.einsum(
        "hrk,kd->rhd", prob_b, value_all, preferred_element_type=jnp.float32
    ).astype(jnp.bfloat16)
    delta_rows = jnp.einsum("rhd,rhd->hr", dout_rows, out_rows, preferred_element_type=jnp.float32)
    d_prob = jnp.einsum("rhd,kd->hrk", dout_rows, value_all, preferred_element_type=jnp.float32)
    d_score = (scale_factor * prob_rows * (d_prob - delta_rows[..., None])).astype(jnp.bfloat16)
    grad_q = jnp.einsum("hrk,kd->rhd", d_score, key_all, preferred_element_type=jnp.float32)
    part_k = jnp.einsum("hrk,rhd->kd", d_score, query_rows, preferred_element_type=jnp.float32)
    part_v = jnp.einsum("hrk,rhd->kd", prob_b, dout_rows, preferred_element_type=jnp.float32)
    return out_rows, grad_q, part_k, part_v


def attend_blocked(query_rows, key_all, value_all, dout_rows, positions, all_pos, seg_own, seg_all, kblock):
    num_rows, head_count = query_rows.shape[0], query_rows.shape[1]
    seq_len = key_all.shape[0]
    causal_limit = (positions[-1] + kblock) // kblock
    key_first = jnp.int32(0)

    def take_block(block_index):
        first_row = block_index * kblock
        return (
            lax.dynamic_slice_in_dim(key_all, first_row, kblock, 0),
            lax.dynamic_slice_in_dim(value_all, first_row, kblock, 0),
            lax.dynamic_slice_in_dim(all_pos, first_row, kblock, 0),
            lax.dynamic_slice_in_dim(seg_all, first_row, kblock, 0),
        )

    def stats_step(block_index, carried):
        run_max, run_sum = carried
        key_blk, value_blk, key_pos, key_seg = take_block(block_index)
        scores, allowed = block_scores(query_rows, key_blk, positions, key_pos, seg_own, key_seg)
        masked = jnp.where(allowed, scores, neg_large)
        new_max = jnp.maximum(run_max, jnp.max(masked, -1))
        terms = jnp.where(allowed, jnp.exp(masked - new_max[..., None]), 0.0)
        return (new_max, run_sum * jnp.exp(run_max - new_max) + jnp.sum(terms, -1))

    start_stats = (
        jnp.full((head_count, num_rows), neg_large, jnp.float32),
        jnp.zeros((head_count, num_rows), jnp.float32),
    )
    run_max, run_sum = lax.fori_loop(key_first, causal_limit, stats_step, start_stats)
    log_total = run_max + jnp.log(run_sum)

    def output_step(block_index, carried):
        key_blk, value_blk, key_pos, key_seg = take_block(block_index)
        scores, allowed = block_scores(query_rows, key_blk, positions, key_pos, seg_own, key_seg)
        prob_b = jnp.where(
            allowed, jnp.exp(jnp.where(allowed, scores - log_total[..., None], neg_large)), 0.0
        ).astype(jnp.bfloat16)
        return carried + jnp.einsum(
            "hrk,kd->rhd", prob_b, value_blk, preferred_element_type=jnp.float32
        )

    out_sum = lax.fori_loop(
        key_first, causal_limit, output_step, jnp.zeros((num_rows, head_count, 128), jnp.float32)
    )
    out_rows = out_sum.astype(jnp.bfloat16)
    delta_rows = jnp.einsum("rhd,rhd->hr", dout_rows, out_rows, preferred_element_type=jnp.float32)

    def sums_step(block_index, carried):
        grad_q, part_k, part_v = carried
        first_row = block_index * kblock
        key_blk, value_blk, key_pos, key_seg = take_block(block_index)
        prob_b, d_score = grad_block(
            query_rows, dout_rows, log_total, delta_rows, key_blk, value_blk,
            positions, key_pos, seg_own, key_seg,
        )
        grad_q = grad_q + jnp.einsum(
            "hrk,kd->rhd", d_score, key_blk, preferred_element_type=jnp.float32
        )
        block_k = jnp.einsum("hrk,rhd->kd", d_score, query_rows, preferred_element_type=jnp.float32)
        block_v = jnp.einsum("hrk,rhd->kd", prob_b, dout_rows, preferred_element_type=jnp.float32)
        part_k = lax.dynamic_update_slice_in_dim(
            part_k, lax.dynamic_slice_in_dim(part_k, first_row, kblock, 0) + block_k, first_row, 0
        )
        part_v = lax.dynamic_update_slice_in_dim(
            part_v, lax.dynamic_slice_in_dim(part_v, first_row, kblock, 0) + block_v, first_row, 0
        )
        return (grad_q, part_k, part_v)

    start_sums = (
        jnp.zeros((num_rows, head_count, 128), jnp.float32),
        jnp.zeros((seq_len, 128), jnp.float32),
        jnp.zeros((seq_len, 128), jnp.float32),
    )
    grad_q, part_k, part_v = lax.fori_loop(key_first, causal_limit, sums_step, start_sums)
    return out_rows, grad_q, part_k, part_v


def attend(query_rows, key_all, value_all, dout_rows, positions, all_pos, seg_own, seg_all):
    head_count, num_rows, seq_len = query_rows.shape[1], query_rows.shape[0], key_all.shape[0]
    operands = (query_rows, key_all, value_all, dout_rows, positions, all_pos, seg_own, seg_all)
    if head_count * num_rows * seq_len <= (1 << 22):
        return attend_whole(*operands)
    kblock = seq_len
    while head_count * num_rows * kblock > (1 << 21) and kblock % 256 == 0:
        kblock //= 2
    return attend_blocked(*operands, kblock)


def local(hidden_in, w_query, w_key, w_value, lengths, attn_grad):
    num_rows = hidden_in.shape[0]
    head_count = w_query.shape[1] // 128
    first_heads = head_count // 2 if head_count % 2 == 0 else head_count
    first_cols = first_heads * 128
    query_cols = head_count * 128
    start_row = lax.axis_index("ctx") * num_rows
    seq_len = num_rows * lax.axis_size("ctx")
    positions = start_row + jnp.arange(num_rows, dtype=jnp.int32)
    all_pos = jnp.arange(seq_len, dtype=jnp.int32)
    seg_all = segment_ids(lengths[0], all_pos)
    seg_own = lax.dynamic_slice_in_dim(seg_all, start_row, num_rows)
    cosine, sine_table = rope_tables(positions)
    rows_axes = ("dp", "ctx")
    group_count = lax.axis_size(rows_axes)
    head_groups = lax.axis_size("head")
    local_a = jnp.concatenate([w_query[:, :first_cols], w_key, w_value], 1)
    full_a = lax.all_gather(local_a, rows_axes, axis=0, tiled=True)
    split_rows = num_rows % head_groups == 0
    if split_rows:
        quarter = num_rows // head_groups
        own_rows = lax.dynamic_slice_in_dim(hidden_in, lax.axis_index("head") * quarter, quarter, 0)
        cols_part = lax.all_to_all(own_rows, rows_axes, 1, 0, tiled=True)
    else:
        cols_part = lax.all_to_all(hidden_in, rows_axes, 1, 0, tiled=True)
    full_a, w_query, cols_part = lax.optimization_barrier((full_a, w_query, cols_part))
    hidden_cols = cols_part
    if split_rows:
        spread = jnp.broadcast_to(cols_part[None], (head_groups,) + cols_part.shape)
        cols_all = lax.all_to_all(spread, "head", 0, 0, tiled=False)
        hidden_cols = (
            cols_all.reshape(head_groups, group_count, quarter, -1)
            .transpose(1, 0, 2, 3)
            .reshape(group_count * num_rows, -1)
        )
    proj_a = jnp.dot(hidden_in, full_a, preferred_element_type=jnp.float32)
    query_a = rotate(
        proj_a[:, :first_cols].reshape(num_rows, first_heads, 128), cosine, sine_table
    ).astype(jnp.bfloat16)
    key_rows = rotate(
        proj_a[:, first_cols : first_cols + 128].reshape(num_rows, 1, 128), cosine, sine_table
    )[:, 0, :].astype(jnp.bfloat16)
    value_rows = proj_a[:, first_cols + 128 :].astype(jnp.bfloat16)
    ctx_index, ctx_count = lax.axis_index("ctx"), lax.axis_size("ctx")
    kv_rows = jnp.concatenate([key_rows, value_rows], 1)
    if ctx_count == 2:
        kv_other = lax.ppermute(kv_rows, "ctx", [(0, 1), (1, 0)])
        kv_all = jnp.where(
            ctx_index == 0,
            jnp.concatenate([kv_rows, kv_other], 0),
            jnp.concatenate([kv_other, kv_rows], 0),
        )
    else:
        kv_all = lax.all_gather(kv_rows, "ctx", axis=0, tiled=True)
    key_all, value_all = kv_all[:, :128], kv_all[:, 128:]
    dout_rows = attn_grad.reshape(num_rows, head_count, 128)
    shared = (key_all, value_all)
    masks = (positions, all_pos, seg_own, seg_all)
    out_a, grad_qa, part_k, part_v = attend(query_a, *shared, dout_rows[:, :first_heads], *masks)
    d_query_a = unrotate(grad_qa, cosine, sine_table).astype(jnp.bfloat16).reshape(num_rows, -1)
    out_parts, d_query_parts = [out_a], [d_query_a]
    if first_heads < head_count:
        w_rest = w_query[:, first_cols:]
        full_b = lax.all_gather(w_rest, rows_axes, axis=0, tiled=True)
        d_query_a, full_b, hidden_cols = lax.optimization_barrier((d_query_a, full_b, hidden_cols))
        early_all = lax.all_gather(d_query_a, rows_axes, axis=0, tiled=True)
        proj_b = jnp.dot(hidden_in, full_b, preferred_element_type=jnp.float32)
        query_b = rotate(
            proj_b.reshape(num_rows, head_count - first_heads, 128), cosine, sine_table
        ).astype(jnp.bfloat16)
        out_b, grad_qb, part_kb, part_vb = attend(
            query_b, *shared, dout_rows[:, first_heads:], *masks
        )
        d_query_b = unrotate(grad_qb, cosine, sine_table).astype(jnp.bfloat16).reshape(num_rows, -1)
        part_k, part_v = part_k + part_kb, part_v + part_vb
        out_parts.append(out_b)
    attended = jnp.concatenate(out_parts, 1).reshape(num_rows, query_cols)
    parts_kv = jnp.concatenate([part_k, part_v], 1)
    if ctx_count == 2:
        own_part = lax.dynamic_slice_in_dim(parts_kv, ctx_index * num_rows, num_rows, 0)
        away_part = lax.dynamic_slice_in_dim(parts_kv, (1 - ctx_index) * num_rows, num_rows, 0)
        grad_kv = own_part + lax.ppermute(away_part, "ctx", [(0, 1), (1, 0)])
    else:
        grad_kv = lax.psum_scatter(parts_kv, "ctx", scatter_dimension=0, tiled=True)
    grad_k, grad_v = grad_kv[:, :128], grad_kv[:, 128:]
    d_key = unrotate(grad_k[:, None, :], cosine, sine_table)[:, 0, :].astype(jnp.bfloat16)
    d_value = grad_v.astype(jnp.bfloat16)
    d_proj_a = jnp.concatenate([d_query_a, d_key, d_value], 1)
    input_part = lax.dot_general(
        d_proj_a, full_a, (((1,), (1,)), ((), ())), preferred_element_type=jnp.float32
    )
    if first_heads < head_count:
        input_part = input_part + lax.dot_general(
            d_query_b, full_b, (((1,), (1,)), ((), ())), preferred_element_type=jnp.float32
        )
        late_proj = jnp.concatenate([d_query_b, d_key, d_value], 1)
        early_sum = lax.dot_general(
            hidden_cols, early_all, (((0,), (0,)), ((), ())), preferred_element_type=jnp.float32
        )
    else:
        late_proj = jnp.concatenate([d_key, d_value], 1)
        early_all = lax.all_gather(d_query_a, rows_axes, axis=0, tiled=True)
        early_sum = lax.dot_general(
            hidden_cols, early_all, (((0,), (0,)), ((), ())), preferred_element_type=jnp.float32
        )
    input_cols = input_part.shape[1] // head_groups
    input_split = lax.all_to_all(
        input_part.astype(jnp.bfloat16).reshape(num_rows, head_groups, input_cols),
        "head", 1, 1, tiled=False,
    )
    grad_input = jnp.sum(input_split.astype(jnp.float32), axis=1).astype(jnp.bfloat16)
    late_all = lax.all_gather(late_proj, rows_axes, axis=0, tiled=True)
    late_sum = lax.dot_general(
        hidden_cols, late_all, (((0,), (0,)), ((), ())), preferred_element_type=jnp.float32
    )
    query_w = jnp.concatenate([early_sum, late_sum[:, : query_cols - first_cols]], 1)
    rest = late_sum[:, query_cols - first_cols :]
    return (attended, grad_input, query_w, rest[:, :128], rest[:, 128:])


def solution(mesh):
    placed = (
        P(("dp", "ctx"), None),
        P(("dp", "ctx"), "head"),
        P(("dp", "ctx"), "head"),
        P(("dp", "ctx"), "head"),
        P("dp", None),
        P(("dp", "ctx"), "head"),
    )
    return jax.shard_map(
        local,
        mesh=mesh,
        in_specs=placed,
        out_specs=(
            P(("dp", "ctx"), "head"),
            P(("dp", "ctx"), "head"),
            P(("dp", "ctx"), "head"),
            P(("dp", "ctx"), "head"),
            P(("dp", "ctx"), "head"),
        ),
        check_vma=False,
    )
```

```python
import jax
import jax.numpy as jnp
from jax import lax
from jax.sharding import PartitionSpec as P

scale_factor = 128.0 ** (-0.5)
neg_large = -1e30


def rope_tables(positions):
    inverse = jnp.power(500000.0, -jnp.arange(64, dtype=jnp.float32) / 64.0)
    angles = positions.astype(jnp.float32)[:, None] * inverse[None, :]
    return (jnp.cos(angles)[:, None, :], jnp.sin(angles)[:, None, :])


def rotate(entries, cosine, sine_table):
    first_half = entries[..., :64]
    second_half = entries[..., 64:]
    return jnp.concatenate(
        [
            first_half * cosine - second_half * sine_table,
            second_half * cosine + first_half * sine_table,
        ],
        -1,
    )


def unrotate(entries, cosine, sine_table):
    first_half = entries[..., :64]
    second_half = entries[..., 64:]
    return jnp.concatenate(
        [
            first_half * cosine + second_half * sine_table,
            second_half * cosine - first_half * sine_table,
        ],
        -1,
    )


def segment_ids(length_row, positions):
    ends = jnp.cumsum(length_row)
    return jnp.sum((positions[:, None] >= ends[None, :]).astype(jnp.int32), 1)


def block_scores(query_blk, key_blk, query_pos, key_pos, query_seg, key_seg):
    scores = (
        jnp.einsum("rhd,kd->hrk", query_blk, key_blk, preferred_element_type=jnp.float32)
        * scale_factor
    )
    allowed = (key_pos[None, :] <= query_pos[:, None]) & (key_seg[None, :] == query_seg[:, None])
    return (scores, allowed[None])


def grad_block(
    query_blk,
    dout_blk,
    total_blk,
    delta_blk,
    key_blk,
    value_blk,
    query_pos,
    key_pos,
    query_seg,
    key_seg,
):
    scores, allowed = block_scores(query_blk, key_blk, query_pos, key_pos, query_seg, key_seg)
    prob_rows = jnp.where(
        allowed, jnp.exp(jnp.where(allowed, scores - total_blk[..., None], neg_large)), 0.0
    )
    prob_b = prob_rows.astype(jnp.bfloat16)
    d_prob = jnp.einsum("rhd,kd->hrk", dout_blk, value_blk, preferred_element_type=jnp.float32)
    d_score = (scale_factor * prob_rows * (d_prob - delta_blk[..., None])).astype(jnp.bfloat16)
    return (prob_b, d_score)


def attend_whole(query_rows, key_all, value_all, dout_rows, positions, all_pos, seg_own, seg_all):
    scores, allowed = block_scores(query_rows, key_all, positions, all_pos, seg_own, seg_all)
    masked = jnp.where(allowed, scores, neg_large)
    top_score = jnp.max(masked, -1)
    total = jnp.sum(jnp.where(allowed, jnp.exp(masked - top_score[..., None]), 0.0), -1)
    log_total = top_score + jnp.log(total)
    prob_rows = jnp.where(
        allowed, jnp.exp(jnp.where(allowed, scores - log_total[..., None], neg_large)), 0.0
    )
    prob_b = prob_rows.astype(jnp.bfloat16)
    out_rows = jnp.einsum(
        "hrk,kd->rhd", prob_b, value_all, preferred_element_type=jnp.float32
    ).astype(jnp.bfloat16)
    delta_rows = jnp.einsum("rhd,rhd->hr", dout_rows, out_rows, preferred_element_type=jnp.float32)
    d_prob = jnp.einsum("rhd,kd->hrk", dout_rows, value_all, preferred_element_type=jnp.float32)
    d_score = (scale_factor * prob_rows * (d_prob - delta_rows[..., None])).astype(jnp.bfloat16)
    grad_q = jnp.einsum("hrk,kd->rhd", d_score, key_all, preferred_element_type=jnp.float32)
    part_k = jnp.einsum("hrk,rhd->kd", d_score, query_rows, preferred_element_type=jnp.float32)
    part_v = jnp.einsum("hrk,rhd->kd", prob_b, dout_rows, preferred_element_type=jnp.float32)
    return out_rows, grad_q, part_k, part_v


def attend_blocked(query_rows, key_all, value_all, dout_rows, positions, all_pos, seg_own, seg_all, kblock):
    num_rows, head_count = query_rows.shape[0], query_rows.shape[1]
    seq_len = key_all.shape[0]
    causal_limit = (positions[-1] + kblock) // kblock
    key_first = jnp.int32(0)

    def take_block(block_index):
        first_row = block_index * kblock
        return (
            lax.dynamic_slice_in_dim(key_all, first_row, kblock, 0),
            lax.dynamic_slice_in_dim(value_all, first_row, kblock, 0),
            lax.dynamic_slice_in_dim(all_pos, first_row, kblock, 0),
            lax.dynamic_slice_in_dim(seg_all, first_row, kblock, 0),
        )

    def stats_step(block_index, carried):
        run_max, run_sum = carried
        key_blk, value_blk, key_pos, key_seg = take_block(block_index)
        scores, allowed = block_scores(query_rows, key_blk, positions, key_pos, seg_own, key_seg)
        masked = jnp.where(allowed, scores, neg_large)
        new_max = jnp.maximum(run_max, jnp.max(masked, -1))
        terms = jnp.where(allowed, jnp.exp(masked - new_max[..., None]), 0.0)
        return (new_max, run_sum * jnp.exp(run_max - new_max) + jnp.sum(terms, -1))

    start_stats = (
        jnp.full((head_count, num_rows), neg_large, jnp.float32),
        jnp.zeros((head_count, num_rows), jnp.float32),
    )
    run_max, run_sum = lax.fori_loop(key_first, causal_limit, stats_step, start_stats)
    log_total = run_max + jnp.log(run_sum)

    def output_step(block_index, carried):
        key_blk, value_blk, key_pos, key_seg = take_block(block_index)
        scores, allowed = block_scores(query_rows, key_blk, positions, key_pos, seg_own, key_seg)
        prob_b = jnp.where(
            allowed, jnp.exp(jnp.where(allowed, scores - log_total[..., None], neg_large)), 0.0
        ).astype(jnp.bfloat16)
        return carried + jnp.einsum(
            "hrk,kd->rhd", prob_b, value_blk, preferred_element_type=jnp.float32
        )

    out_sum = lax.fori_loop(
        key_first, causal_limit, output_step, jnp.zeros((num_rows, head_count, 128), jnp.float32)
    )
    out_rows = out_sum.astype(jnp.bfloat16)
    delta_rows = jnp.einsum("rhd,rhd->hr", dout_rows, out_rows, preferred_element_type=jnp.float32)

    def sums_step(block_index, carried):
        grad_q, part_k, part_v = carried
        first_row = block_index * kblock
        key_blk, value_blk, key_pos, key_seg = take_block(block_index)
        prob_b, d_score = grad_block(
            query_rows, dout_rows, log_total, delta_rows, key_blk, value_blk,
            positions, key_pos, seg_own, key_seg,
        )
        grad_q = grad_q + jnp.einsum(
            "hrk,kd->rhd", d_score, key_blk, preferred_element_type=jnp.float32
        )
        block_k = jnp.einsum("hrk,rhd->kd", d_score, query_rows, preferred_element_type=jnp.float32)
        block_v = jnp.einsum("hrk,rhd->kd", prob_b, dout_rows, preferred_element_type=jnp.float32)
        part_k = lax.dynamic_update_slice_in_dim(
            part_k, lax.dynamic_slice_in_dim(part_k, first_row, kblock, 0) + block_k, first_row, 0
        )
        part_v = lax.dynamic_update_slice_in_dim(
            part_v, lax.dynamic_slice_in_dim(part_v, first_row, kblock, 0) + block_v, first_row, 0
        )
        return (grad_q, part_k, part_v)

    start_sums = (
        jnp.zeros((num_rows, head_count, 128), jnp.float32),
        jnp.zeros((seq_len, 128), jnp.float32),
        jnp.zeros((seq_len, 128), jnp.float32),
    )
    grad_q, part_k, part_v = lax.fori_loop(key_first, causal_limit, sums_step, start_sums)
    return out_rows, grad_q, part_k, part_v


def attend(query_rows, key_all, value_all, dout_rows, positions, all_pos, seg_own, seg_all):
    head_count, num_rows, seq_len = query_rows.shape[1], query_rows.shape[0], key_all.shape[0]
    operands = (query_rows, key_all, value_all, dout_rows, positions, all_pos, seg_own, seg_all)
    if head_count * num_rows * seq_len <= (1 << 22):
        return attend_whole(*operands)
    kblock = seq_len
    while head_count * num_rows * kblock > (1 << 21) and kblock % 256 == 0:
        kblock //= 2
    return attend_blocked(*operands, kblock)


def local(hidden_in, w_query, w_key, w_value, lengths, attn_grad):
    num_rows = hidden_in.shape[0]
    head_count = w_query.shape[1] // 128
    first_heads = head_count // 2 if head_count % 2 == 0 else head_count
    first_cols = first_heads * 128
    query_cols = head_count * 128
    start_row = lax.axis_index("ctx") * num_rows
    seq_len = num_rows * lax.axis_size("ctx")
    positions = start_row + jnp.arange(num_rows, dtype=jnp.int32)
    all_pos = jnp.arange(seq_len, dtype=jnp.int32)
    seg_all = segment_ids(lengths[0], all_pos)
    seg_own = lax.dynamic_slice_in_dim(seg_all, start_row, num_rows)
    cosine, sine_table = rope_tables(positions)
    rows_axes = ("dp", "ctx")
    group_count = lax.axis_size(rows_axes)
    head_groups = lax.axis_size("head")
    local_a = jnp.concatenate([w_query[:, :first_cols], w_key, w_value], 1)
    full_a = lax.all_gather(local_a, rows_axes, axis=0, tiled=True)
    split_rows = num_rows % head_groups == 0
    dp_count, ctx_count = lax.axis_size("dp"), lax.axis_size("ctx")
    ctx_index = lax.axis_index("ctx")
    if split_rows:
        quarter = num_rows // head_groups
        own_rows = lax.dynamic_slice_in_dim(hidden_in, lax.axis_index("head") * quarter, quarter, 0)
        cols_part = lax.all_to_all(own_rows, "dp", 1, 0, tiled=True)
    else:
        cols_part = lax.all_to_all(hidden_in, "dp", 1, 0, tiled=True)
    full_a, w_query, cols_part = lax.optimization_barrier((full_a, w_query, cols_part))
    hidden_cols = cols_part
    if split_rows:
        spread = jnp.broadcast_to(cols_part[None], (head_groups,) + cols_part.shape)
        cols_all = lax.all_to_all(spread, "head", 0, 0, tiled=False)
        hidden_cols = (
            cols_all.reshape(head_groups, dp_count, quarter, -1)
            .transpose(1, 0, 2, 3)
            .reshape(dp_count * num_rows, -1)
        )
    weight_rows = w_query.shape[0]

    def weight_grad(d_rows):
        gathered = lax.all_gather(d_rows, "dp", axis=0, tiled=True)
        partial = lax.dot_general(
            hidden_cols, gathered, (((0,), (0,)), ((), ())), preferred_element_type=jnp.float32
        )
        if ctx_count == 2:
            own_part = lax.dynamic_slice_in_dim(partial, ctx_index * weight_rows, weight_rows, 0)
            away_part = lax.dynamic_slice_in_dim(
                partial, (1 - ctx_index) * weight_rows, weight_rows, 0
            )
            return own_part + lax.ppermute(away_part, "ctx", [(0, 1), (1, 0)])
        return lax.psum_scatter(partial, "ctx", scatter_dimension=0, tiled=True)

    proj_a = jnp.dot(hidden_in, full_a, preferred_element_type=jnp.float32)
    query_a = rotate(
        proj_a[:, :first_cols].reshape(num_rows, first_heads, 128), cosine, sine_table
    ).astype(jnp.bfloat16)
    key_rows = rotate(
        proj_a[:, first_cols : first_cols + 128].reshape(num_rows, 1, 128), cosine, sine_table
    )[:, 0, :].astype(jnp.bfloat16)
    value_rows = proj_a[:, first_cols + 128 :].astype(jnp.bfloat16)
    kv_rows = jnp.concatenate([key_rows, value_rows], 1)
    if ctx_count == 2:
        kv_other = lax.ppermute(kv_rows, "ctx", [(0, 1), (1, 0)])
        kv_all = jnp.where(
            ctx_index == 0,
            jnp.concatenate([kv_rows, kv_other], 0),
            jnp.concatenate([kv_other, kv_rows], 0),
        )
    else:
        kv_all = lax.all_gather(kv_rows, "ctx", axis=0, tiled=True)
    key_all, value_all = kv_all[:, :128], kv_all[:, 128:]
    dout_rows = attn_grad.reshape(num_rows, head_count, 128)
    shared = (key_all, value_all)
    masks = (positions, all_pos, seg_own, seg_all)
    out_a, grad_qa, part_k, part_v = attend(query_a, *shared, dout_rows[:, :first_heads], *masks)
    d_query_a = unrotate(grad_qa, cosine, sine_table).astype(jnp.bfloat16).reshape(num_rows, -1)
    out_parts, d_query_parts = [out_a], [d_query_a]
    if first_heads < head_count:
        w_rest = w_query[:, first_cols:]
        full_b = lax.all_gather(w_rest, rows_axes, axis=0, tiled=True)
        d_query_a, full_b, hidden_cols = lax.optimization_barrier((d_query_a, full_b, hidden_cols))
        early_sum = weight_grad(d_query_a)
        proj_b = jnp.dot(hidden_in, full_b, preferred_element_type=jnp.float32)
        query_b = rotate(
            proj_b.reshape(num_rows, head_count - first_heads, 128), cosine, sine_table
        ).astype(jnp.bfloat16)
        out_b, grad_qb, part_kb, part_vb = attend(
            query_b, *shared, dout_rows[:, first_heads:], *masks
        )
        d_query_b = unrotate(grad_qb, cosine, sine_table).astype(jnp.bfloat16).reshape(num_rows, -1)
        part_k, part_v = part_k + part_kb, part_v + part_vb
        out_parts.append(out_b)
    attended = jnp.concatenate(out_parts, 1).reshape(num_rows, query_cols)
    parts_kv = jnp.concatenate([part_k, part_v], 1)
    if ctx_count == 2:
        own_part = lax.dynamic_slice_in_dim(parts_kv, ctx_index * num_rows, num_rows, 0)
        away_part = lax.dynamic_slice_in_dim(parts_kv, (1 - ctx_index) * num_rows, num_rows, 0)
        grad_kv = own_part + lax.ppermute(away_part, "ctx", [(0, 1), (1, 0)])
    else:
        grad_kv = lax.psum_scatter(parts_kv, "ctx", scatter_dimension=0, tiled=True)
    grad_k, grad_v = grad_kv[:, :128], grad_kv[:, 128:]
    d_key = unrotate(grad_k[:, None, :], cosine, sine_table)[:, 0, :].astype(jnp.bfloat16)
    d_value = grad_v.astype(jnp.bfloat16)
    d_proj_a = jnp.concatenate([d_query_a, d_key, d_value], 1)
    input_part = lax.dot_general(
        d_proj_a, full_a, (((1,), (1,)), ((), ())), preferred_element_type=jnp.float32
    )
    if first_heads < head_count:
        input_part = input_part + lax.dot_general(
            d_query_b, full_b, (((1,), (1,)), ((), ())), preferred_element_type=jnp.float32
        )
        late_proj = jnp.concatenate([d_query_b, d_key, d_value], 1)
    else:
        late_proj = jnp.concatenate([d_key, d_value], 1)
        early_sum = weight_grad(d_query_a)
    input_cols = input_part.shape[1] // head_groups
    input_split = lax.all_to_all(
        input_part.astype(jnp.bfloat16).reshape(num_rows, head_groups, input_cols),
        "head", 1, 1, tiled=False,
    )
    grad_input = jnp.sum(input_split.astype(jnp.float32), axis=1).astype(jnp.bfloat16)
    late_sum = weight_grad(late_proj)
    query_w = jnp.concatenate([early_sum, late_sum[:, : query_cols - first_cols]], 1)
    rest = late_sum[:, query_cols - first_cols :]
    return (attended, grad_input, query_w, rest[:, :128], rest[:, 128:])


def solution(mesh):
    placed = (
        P(("dp", "ctx"), None),
        P(("dp", "ctx"), "head"),
        P(("dp", "ctx"), "head"),
        P(("dp", "ctx"), "head"),
        P("dp", None),
        P(("dp", "ctx"), "head"),
    )
    return jax.shard_map(
        local,
        mesh=mesh,
        in_specs=placed,
        out_specs=(
            P(("dp", "ctx"), "head"),
            P(("dp", "ctx"), "head"),
            P(("dp", "ctx"), "head"),
            P(("dp", "ctx"), "head"),
            P(("dp", "ctx"), "head"),
        ),
        check_vma=False,
    )
```

```python
import jax
import jax.numpy as jnp
from jax import lax
from jax.sharding import PartitionSpec as P

scale_factor = 128.0 ** (-0.5)
neg_large = -1e30


def rope_tables(positions):
    inverse = jnp.power(500000.0, -jnp.arange(64, dtype=jnp.float32) / 64.0)
    angles = positions.astype(jnp.float32)[:, None] * inverse[None, :]
    return (jnp.cos(angles)[:, None, :], jnp.sin(angles)[:, None, :])


def rotate(entries, cosine, sine_table):
    first_half = entries[..., :64]
    second_half = entries[..., 64:]
    return jnp.concatenate(
        [
            first_half * cosine - second_half * sine_table,
            second_half * cosine + first_half * sine_table,
        ],
        -1,
    )


def unrotate(entries, cosine, sine_table):
    first_half = entries[..., :64]
    second_half = entries[..., 64:]
    return jnp.concatenate(
        [
            first_half * cosine + second_half * sine_table,
            second_half * cosine - first_half * sine_table,
        ],
        -1,
    )


def segment_ids(length_row, positions):
    ends = jnp.cumsum(length_row)
    return jnp.sum((positions[:, None] >= ends[None, :]).astype(jnp.int32), 1)


def block_scores(query_blk, key_blk, query_pos, key_pos, query_seg, key_seg):
    scores = (
        jnp.einsum("rhd,kd->hrk", query_blk, key_blk, preferred_element_type=jnp.float32)
        * scale_factor
    )
    allowed = (key_pos[None, :] <= query_pos[:, None]) & (key_seg[None, :] == query_seg[:, None])
    return (scores, allowed[None])


def grad_block(
    query_blk,
    dout_blk,
    total_blk,
    delta_blk,
    key_blk,
    value_blk,
    query_pos,
    key_pos,
    query_seg,
    key_seg,
):
    scores, allowed = block_scores(query_blk, key_blk, query_pos, key_pos, query_seg, key_seg)
    prob_rows = jnp.where(
        allowed, jnp.exp(jnp.where(allowed, scores - total_blk[..., None], neg_large)), 0.0
    )
    prob_b = prob_rows.astype(jnp.bfloat16)
    d_prob = jnp.einsum("rhd,kd->hrk", dout_blk, value_blk, preferred_element_type=jnp.float32)
    d_score = (scale_factor * prob_rows * (d_prob - delta_blk[..., None])).astype(jnp.bfloat16)
    return (prob_b, d_score)


def attend_whole(query_rows, key_all, value_all, dout_rows, positions, all_pos, seg_own, seg_all):
    scores, allowed = block_scores(query_rows, key_all, positions, all_pos, seg_own, seg_all)
    masked = jnp.where(allowed, scores, neg_large)
    top_score = jnp.max(masked, -1)
    total = jnp.sum(jnp.where(allowed, jnp.exp(masked - top_score[..., None]), 0.0), -1)
    log_total = top_score + jnp.log(total)
    prob_rows = jnp.where(
        allowed, jnp.exp(jnp.where(allowed, scores - log_total[..., None], neg_large)), 0.0
    )
    prob_b = prob_rows.astype(jnp.bfloat16)
    out_rows = jnp.einsum(
        "hrk,kd->rhd", prob_b, value_all, preferred_element_type=jnp.float32
    ).astype(jnp.bfloat16)
    delta_rows = jnp.einsum("rhd,rhd->hr", dout_rows, out_rows, preferred_element_type=jnp.float32)
    d_prob = jnp.einsum("rhd,kd->hrk", dout_rows, value_all, preferred_element_type=jnp.float32)
    d_score = (scale_factor * prob_rows * (d_prob - delta_rows[..., None])).astype(jnp.bfloat16)
    grad_q = jnp.einsum("hrk,kd->rhd", d_score, key_all, preferred_element_type=jnp.float32)
    part_k = jnp.einsum("hrk,rhd->kd", d_score, query_rows, preferred_element_type=jnp.float32)
    part_v = jnp.einsum("hrk,rhd->kd", prob_b, dout_rows, preferred_element_type=jnp.float32)
    return out_rows, grad_q, part_k, part_v


def attend_blocked(query_rows, key_all, value_all, dout_rows, positions, all_pos, seg_own, seg_all, kblock):
    num_rows, head_count = query_rows.shape[0], query_rows.shape[1]
    seq_len = key_all.shape[0]
    causal_limit = (positions[-1] + kblock) // kblock
    key_first = jnp.int32(0)

    def take_block(block_index):
        first_row = block_index * kblock
        return (
            lax.dynamic_slice_in_dim(key_all, first_row, kblock, 0),
            lax.dynamic_slice_in_dim(value_all, first_row, kblock, 0),
            lax.dynamic_slice_in_dim(all_pos, first_row, kblock, 0),
            lax.dynamic_slice_in_dim(seg_all, first_row, kblock, 0),
        )

    def stats_step(block_index, carried):
        run_max, run_sum = carried
        key_blk, value_blk, key_pos, key_seg = take_block(block_index)
        scores, allowed = block_scores(query_rows, key_blk, positions, key_pos, seg_own, key_seg)
        masked = jnp.where(allowed, scores, neg_large)
        new_max = jnp.maximum(run_max, jnp.max(masked, -1))
        terms = jnp.where(allowed, jnp.exp(masked - new_max[..., None]), 0.0)
        return (new_max, run_sum * jnp.exp(run_max - new_max) + jnp.sum(terms, -1))

    start_stats = (
        jnp.full((head_count, num_rows), neg_large, jnp.float32),
        jnp.zeros((head_count, num_rows), jnp.float32),
    )
    run_max, run_sum = lax.fori_loop(key_first, causal_limit, stats_step, start_stats)
    log_total = run_max + jnp.log(run_sum)

    def output_step(block_index, carried):
        key_blk, value_blk, key_pos, key_seg = take_block(block_index)
        scores, allowed = block_scores(query_rows, key_blk, positions, key_pos, seg_own, key_seg)
        prob_b = jnp.where(
            allowed, jnp.exp(jnp.where(allowed, scores - log_total[..., None], neg_large)), 0.0
        ).astype(jnp.bfloat16)
        return carried + jnp.einsum(
            "hrk,kd->rhd", prob_b, value_blk, preferred_element_type=jnp.float32
        )

    out_sum = lax.fori_loop(
        key_first, causal_limit, output_step, jnp.zeros((num_rows, head_count, 128), jnp.float32)
    )
    out_rows = out_sum.astype(jnp.bfloat16)
    delta_rows = jnp.einsum("rhd,rhd->hr", dout_rows, out_rows, preferred_element_type=jnp.float32)

    def sums_step(block_index, carried):
        grad_q, part_k, part_v = carried
        first_row = block_index * kblock
        key_blk, value_blk, key_pos, key_seg = take_block(block_index)
        prob_b, d_score = grad_block(
            query_rows, dout_rows, log_total, delta_rows, key_blk, value_blk,
            positions, key_pos, seg_own, key_seg,
        )
        grad_q = grad_q + jnp.einsum(
            "hrk,kd->rhd", d_score, key_blk, preferred_element_type=jnp.float32
        )
        block_k = jnp.einsum("hrk,rhd->kd", d_score, query_rows, preferred_element_type=jnp.float32)
        block_v = jnp.einsum("hrk,rhd->kd", prob_b, dout_rows, preferred_element_type=jnp.float32)
        part_k = lax.dynamic_update_slice_in_dim(
            part_k, lax.dynamic_slice_in_dim(part_k, first_row, kblock, 0) + block_k, first_row, 0
        )
        part_v = lax.dynamic_update_slice_in_dim(
            part_v, lax.dynamic_slice_in_dim(part_v, first_row, kblock, 0) + block_v, first_row, 0
        )
        return (grad_q, part_k, part_v)

    start_sums = (
        jnp.zeros((num_rows, head_count, 128), jnp.float32),
        jnp.zeros((seq_len, 128), jnp.float32),
        jnp.zeros((seq_len, 128), jnp.float32),
    )
    grad_q, part_k, part_v = lax.fori_loop(key_first, causal_limit, sums_step, start_sums)
    return out_rows, grad_q, part_k, part_v


def attend(query_rows, key_all, value_all, dout_rows, positions, all_pos, seg_own, seg_all):
    head_count, num_rows, seq_len = query_rows.shape[1], query_rows.shape[0], key_all.shape[0]
    operands = (query_rows, key_all, value_all, dout_rows, positions, all_pos, seg_own, seg_all)
    if head_count * num_rows * seq_len <= (1 << 22):
        return attend_whole(*operands)
    kblock = seq_len
    while head_count * num_rows * kblock > (1 << 21) and kblock % 256 == 0:
        kblock //= 2
    return attend_blocked(*operands, kblock)


def local(hidden_in, w_query, w_key, w_value, lengths, attn_grad):
    num_rows = hidden_in.shape[0]
    head_count = w_query.shape[1] // 128
    first_heads = head_count // 2 if head_count % 2 == 0 else head_count
    first_cols = first_heads * 128
    query_cols = head_count * 128
    start_row = lax.axis_index("ctx") * num_rows
    seq_len = num_rows * lax.axis_size("ctx")
    positions = start_row + jnp.arange(num_rows, dtype=jnp.int32)
    all_pos = jnp.arange(seq_len, dtype=jnp.int32)
    seg_all = segment_ids(lengths[0], all_pos)
    seg_own = lax.dynamic_slice_in_dim(seg_all, start_row, num_rows)
    cosine, sine_table = rope_tables(positions)
    rows_axes = ("dp", "ctx")
    group_count = lax.axis_size(rows_axes)
    head_groups = lax.axis_size("head")
    local_a = jnp.concatenate([w_query[:, :first_cols], w_key, w_value], 1)
    full_a = lax.all_gather(local_a, rows_axes, axis=0, tiled=True)
    split_rows = num_rows % head_groups == 0
    dp_count, ctx_count = lax.axis_size("dp"), lax.axis_size("ctx")
    ctx_index = lax.axis_index("ctx")
    if split_rows:
        quarter = num_rows // head_groups
        own_rows = lax.dynamic_slice_in_dim(hidden_in, lax.axis_index("head") * quarter, quarter, 0)
        cols_part = lax.all_to_all(own_rows, "dp", 1, 0, tiled=True)
    else:
        cols_part = lax.all_to_all(hidden_in, "dp", 1, 0, tiled=True)
    full_a, w_query, cols_part = lax.optimization_barrier((full_a, w_query, cols_part))
    hidden_cols = cols_part
    if split_rows:
        spread = jnp.broadcast_to(cols_part[None], (head_groups,) + cols_part.shape)
        cols_all = lax.all_to_all(spread, "head", 0, 0, tiled=False)
        hidden_cols = (
            cols_all.reshape(head_groups, dp_count, quarter, -1)
            .transpose(1, 0, 2, 3)
            .reshape(dp_count * num_rows, -1)
        )
    weight_rows = w_query.shape[0]

    def weight_grad(d_rows, gathered=None):
        if gathered is None:
            gathered = lax.all_gather(d_rows, "dp", axis=0, tiled=True)
        partial = lax.dot_general(
            hidden_cols, gathered, (((0,), (0,)), ((), ())), preferred_element_type=jnp.float32
        )
        if ctx_count == 2:
            own_part = lax.dynamic_slice_in_dim(partial, ctx_index * weight_rows, weight_rows, 0)
            away_part = lax.dynamic_slice_in_dim(
                partial, (1 - ctx_index) * weight_rows, weight_rows, 0
            )
            return own_part + lax.ppermute(away_part, "ctx", [(0, 1), (1, 0)])
        return lax.psum_scatter(partial, "ctx", scatter_dimension=0, tiled=True)

    proj_a = jnp.dot(hidden_in, full_a, preferred_element_type=jnp.float32)
    query_a = rotate(
        proj_a[:, :first_cols].reshape(num_rows, first_heads, 128), cosine, sine_table
    ).astype(jnp.bfloat16)
    key_rows = rotate(
        proj_a[:, first_cols : first_cols + 128].reshape(num_rows, 1, 128), cosine, sine_table
    )[:, 0, :].astype(jnp.bfloat16)
    value_rows = proj_a[:, first_cols + 128 :].astype(jnp.bfloat16)
    kv_rows = jnp.concatenate([key_rows, value_rows], 1)
    if ctx_count == 2:
        kv_other = lax.ppermute(kv_rows, "ctx", [(0, 1), (1, 0)])
        kv_all = jnp.where(
            ctx_index == 0,
            jnp.concatenate([kv_rows, kv_other], 0),
            jnp.concatenate([kv_other, kv_rows], 0),
        )
    else:
        kv_all = lax.all_gather(kv_rows, "ctx", axis=0, tiled=True)
    key_all, value_all = kv_all[:, :128], kv_all[:, 128:]
    dout_rows = attn_grad.reshape(num_rows, head_count, 128)
    shared = (key_all, value_all)
    masks = (positions, all_pos, seg_own, seg_all)
    out_a, grad_qa, part_k, part_v = attend(query_a, *shared, dout_rows[:, :first_heads], *masks)
    d_query_a = unrotate(grad_qa, cosine, sine_table).astype(jnp.bfloat16).reshape(num_rows, -1)
    out_parts, d_query_parts = [out_a], [d_query_a]
    if first_heads < head_count:
        w_rest = w_query[:, first_cols:]
        full_b = lax.all_gather(w_rest, rows_axes, axis=0, tiled=True)
        d_query_a, full_b, hidden_cols = lax.optimization_barrier((d_query_a, full_b, hidden_cols))
        early_all = lax.all_gather(d_query_a, "dp", axis=0, tiled=True)
        proj_b = jnp.dot(hidden_in, full_b, preferred_element_type=jnp.float32)
        query_b = rotate(
            proj_b.reshape(num_rows, head_count - first_heads, 128), cosine, sine_table
        ).astype(jnp.bfloat16)
        out_b, grad_qb, part_kb, part_vb = attend(
            query_b, *shared, dout_rows[:, first_heads:], *masks
        )
        early_all, grad_qb = lax.optimization_barrier((early_all, grad_qb))
        early_sum = weight_grad(d_query_a, early_all)
        d_query_b = unrotate(grad_qb, cosine, sine_table).astype(jnp.bfloat16).reshape(num_rows, -1)
        part_k, part_v = part_k + part_kb, part_v + part_vb
        out_parts.append(out_b)
    attended = jnp.concatenate(out_parts, 1).reshape(num_rows, query_cols)
    parts_kv = jnp.concatenate([part_k, part_v], 1)
    if ctx_count == 2:
        own_part = lax.dynamic_slice_in_dim(parts_kv, ctx_index * num_rows, num_rows, 0)
        away_part = lax.dynamic_slice_in_dim(parts_kv, (1 - ctx_index) * num_rows, num_rows, 0)
        grad_kv = own_part + lax.ppermute(away_part, "ctx", [(0, 1), (1, 0)])
    else:
        grad_kv = lax.psum_scatter(parts_kv, "ctx", scatter_dimension=0, tiled=True)
    grad_k, grad_v = grad_kv[:, :128], grad_kv[:, 128:]
    d_key = unrotate(grad_k[:, None, :], cosine, sine_table)[:, 0, :].astype(jnp.bfloat16)
    d_value = grad_v.astype(jnp.bfloat16)
    d_proj_a = jnp.concatenate([d_query_a, d_key, d_value], 1)
    input_part = lax.dot_general(
        d_proj_a, full_a, (((1,), (1,)), ((), ())), preferred_element_type=jnp.float32
    )
    if first_heads < head_count:
        input_part = input_part + lax.dot_general(
            d_query_b, full_b, (((1,), (1,)), ((), ())), preferred_element_type=jnp.float32
        )
        late_proj = jnp.concatenate([d_query_b, d_key, d_value], 1)
    else:
        late_proj = jnp.concatenate([d_key, d_value], 1)
        early_sum = weight_grad(d_query_a)
    early_sum, input_part = lax.optimization_barrier((early_sum, input_part))
    input_cols = input_part.shape[1] // head_groups
    input_split = lax.all_to_all(
        input_part.astype(jnp.bfloat16).reshape(num_rows, head_groups, input_cols),
        "head", 1, 1, tiled=False,
    )
    grad_input = jnp.sum(input_split.astype(jnp.float32), axis=1).astype(jnp.bfloat16)
    late_sum = weight_grad(late_proj)
    query_w = jnp.concatenate([early_sum, late_sum[:, : query_cols - first_cols]], 1)
    rest = late_sum[:, query_cols - first_cols :]
    return (attended, grad_input, query_w, rest[:, :128], rest[:, 128:])


def solution(mesh):
    placed = (
        P(("dp", "ctx"), None),
        P(("dp", "ctx"), "head"),
        P(("dp", "ctx"), "head"),
        P(("dp", "ctx"), "head"),
        P("dp", None),
        P(("dp", "ctx"), "head"),
    )
    return jax.shard_map(
        local,
        mesh=mesh,
        in_specs=placed,
        out_specs=(
            P(("dp", "ctx"), "head"),
            P(("dp", "ctx"), "head"),
            P(("dp", "ctx"), "head"),
            P(("dp", "ctx"), "head"),
            P(("dp", "ctx"), "head"),
        ),
        check_vma=False,
    )
```

```python
import jax
import jax.numpy as jnp
from jax import lax
from jax.sharding import PartitionSpec as P

scale_factor = 128.0 ** (-0.5)
neg_large = -1e30


def rope_tables(positions):
    inverse = jnp.power(500000.0, -jnp.arange(64, dtype=jnp.float32) / 64.0)
    angles = positions.astype(jnp.float32)[:, None] * inverse[None, :]
    return (jnp.cos(angles)[:, None, :], jnp.sin(angles)[:, None, :])


def rotate(entries, cosine, sine_table):
    first_half = entries[..., :64]
    second_half = entries[..., 64:]
    return jnp.concatenate(
        [
            first_half * cosine - second_half * sine_table,
            second_half * cosine + first_half * sine_table,
        ],
        -1,
    )


def unrotate(entries, cosine, sine_table):
    first_half = entries[..., :64]
    second_half = entries[..., 64:]
    return jnp.concatenate(
        [
            first_half * cosine + second_half * sine_table,
            second_half * cosine - first_half * sine_table,
        ],
        -1,
    )


def segment_ids(length_row, positions):
    ends = jnp.cumsum(length_row)
    return jnp.sum((positions[:, None] >= ends[None, :]).astype(jnp.int32), 1)


def block_scores(query_blk, key_blk, query_pos, key_pos, query_seg, key_seg):
    scores = (
        jnp.einsum("rhd,kd->hrk", query_blk, key_blk, preferred_element_type=jnp.float32)
        * scale_factor
    )
    allowed = (key_pos[None, :] <= query_pos[:, None]) & (key_seg[None, :] == query_seg[:, None])
    return (scores, allowed[None])


def grad_block(
    query_blk,
    dout_blk,
    total_blk,
    delta_blk,
    key_blk,
    value_blk,
    query_pos,
    key_pos,
    query_seg,
    key_seg,
):
    scores, allowed = block_scores(query_blk, key_blk, query_pos, key_pos, query_seg, key_seg)
    prob_rows = jnp.where(
        allowed, jnp.exp(jnp.where(allowed, scores - total_blk[..., None], neg_large)), 0.0
    )
    prob_b = prob_rows.astype(jnp.bfloat16)
    d_prob = jnp.einsum("rhd,kd->hrk", dout_blk, value_blk, preferred_element_type=jnp.float32)
    d_score = (scale_factor * prob_rows * (d_prob - delta_blk[..., None])).astype(jnp.bfloat16)
    return (prob_b, d_score)


def attend_whole(query_rows, key_all, value_all, dout_rows, positions, all_pos, seg_own, seg_all):
    scores, allowed = block_scores(query_rows, key_all, positions, all_pos, seg_own, seg_all)
    masked = jnp.where(allowed, scores, neg_large)
    top_score = jnp.max(masked, -1)
    total = jnp.sum(jnp.where(allowed, jnp.exp(masked - top_score[..., None]), 0.0), -1)
    log_total = top_score + jnp.log(total)
    prob_rows = jnp.where(
        allowed, jnp.exp(jnp.where(allowed, scores - log_total[..., None], neg_large)), 0.0
    )
    prob_b = prob_rows.astype(jnp.bfloat16)
    out_rows = jnp.einsum(
        "hrk,kd->rhd", prob_b, value_all, preferred_element_type=jnp.float32
    ).astype(jnp.bfloat16)
    delta_rows = jnp.einsum("rhd,rhd->hr", dout_rows, out_rows, preferred_element_type=jnp.float32)
    d_prob = jnp.einsum("rhd,kd->hrk", dout_rows, value_all, preferred_element_type=jnp.float32)
    d_score = (scale_factor * prob_rows * (d_prob - delta_rows[..., None])).astype(jnp.bfloat16)
    grad_q = jnp.einsum("hrk,kd->rhd", d_score, key_all, preferred_element_type=jnp.float32)
    part_k = jnp.einsum("hrk,rhd->kd", d_score, query_rows, preferred_element_type=jnp.float32)
    part_v = jnp.einsum("hrk,rhd->kd", prob_b, dout_rows, preferred_element_type=jnp.float32)
    return out_rows, grad_q, part_k, part_v


def attend_blocked(query_rows, key_all, value_all, dout_rows, positions, all_pos, seg_own, seg_all, kblock):
    num_rows, head_count = query_rows.shape[0], query_rows.shape[1]
    seq_len = key_all.shape[0]
    causal_limit = (positions[-1] + kblock) // kblock
    key_first = jnp.int32(0)

    def take_block(block_index):
        first_row = block_index * kblock
        return (
            lax.dynamic_slice_in_dim(key_all, first_row, kblock, 0),
            lax.dynamic_slice_in_dim(value_all, first_row, kblock, 0),
            lax.dynamic_slice_in_dim(all_pos, first_row, kblock, 0),
            lax.dynamic_slice_in_dim(seg_all, first_row, kblock, 0),
        )

    def stats_step(block_index, carried):
        run_max, run_sum = carried
        key_blk, value_blk, key_pos, key_seg = take_block(block_index)
        scores, allowed = block_scores(query_rows, key_blk, positions, key_pos, seg_own, key_seg)
        masked = jnp.where(allowed, scores, neg_large)
        new_max = jnp.maximum(run_max, jnp.max(masked, -1))
        terms = jnp.where(allowed, jnp.exp(masked - new_max[..., None]), 0.0)
        return (new_max, run_sum * jnp.exp(run_max - new_max) + jnp.sum(terms, -1))

    start_stats = (
        jnp.full((head_count, num_rows), neg_large, jnp.float32),
        jnp.zeros((head_count, num_rows), jnp.float32),
    )
    run_max, run_sum = lax.fori_loop(key_first, causal_limit, stats_step, start_stats)
    log_total = run_max + jnp.log(run_sum)

    def output_step(block_index, carried):
        key_blk, value_blk, key_pos, key_seg = take_block(block_index)
        scores, allowed = block_scores(query_rows, key_blk, positions, key_pos, seg_own, key_seg)
        prob_b = jnp.where(
            allowed, jnp.exp(jnp.where(allowed, scores - log_total[..., None], neg_large)), 0.0
        ).astype(jnp.bfloat16)
        return carried + jnp.einsum(
            "hrk,kd->rhd", prob_b, value_blk, preferred_element_type=jnp.float32
        )

    out_sum = lax.fori_loop(
        key_first, causal_limit, output_step, jnp.zeros((num_rows, head_count, 128), jnp.float32)
    )
    out_rows = out_sum.astype(jnp.bfloat16)
    delta_rows = jnp.einsum("rhd,rhd->hr", dout_rows, out_rows, preferred_element_type=jnp.float32)

    def sums_step(block_index, carried):
        grad_q, part_k, part_v = carried
        first_row = block_index * kblock
        key_blk, value_blk, key_pos, key_seg = take_block(block_index)
        prob_b, d_score = grad_block(
            query_rows, dout_rows, log_total, delta_rows, key_blk, value_blk,
            positions, key_pos, seg_own, key_seg,
        )
        grad_q = grad_q + jnp.einsum(
            "hrk,kd->rhd", d_score, key_blk, preferred_element_type=jnp.float32
        )
        block_k = jnp.einsum("hrk,rhd->kd", d_score, query_rows, preferred_element_type=jnp.float32)
        block_v = jnp.einsum("hrk,rhd->kd", prob_b, dout_rows, preferred_element_type=jnp.float32)
        part_k = lax.dynamic_update_slice_in_dim(
            part_k, lax.dynamic_slice_in_dim(part_k, first_row, kblock, 0) + block_k, first_row, 0
        )
        part_v = lax.dynamic_update_slice_in_dim(
            part_v, lax.dynamic_slice_in_dim(part_v, first_row, kblock, 0) + block_v, first_row, 0
        )
        return (grad_q, part_k, part_v)

    start_sums = (
        jnp.zeros((num_rows, head_count, 128), jnp.float32),
        jnp.zeros((seq_len, 128), jnp.float32),
        jnp.zeros((seq_len, 128), jnp.float32),
    )
    grad_q, part_k, part_v = lax.fori_loop(key_first, causal_limit, sums_step, start_sums)
    return out_rows, grad_q, part_k, part_v


def attend(query_rows, key_all, value_all, dout_rows, positions, all_pos, seg_own, seg_all):
    head_count, num_rows, seq_len = query_rows.shape[1], query_rows.shape[0], key_all.shape[0]
    operands = (query_rows, key_all, value_all, dout_rows, positions, all_pos, seg_own, seg_all)
    if head_count * num_rows * seq_len <= (1 << 22):
        return attend_whole(*operands)
    kblock = seq_len
    while head_count * num_rows * kblock > (1 << 21) and kblock % 256 == 0:
        kblock //= 2
    return attend_blocked(*operands, kblock)


def local(hidden_in, w_query, w_key, w_value, lengths, attn_grad):
    num_rows = hidden_in.shape[0]
    head_count = w_query.shape[1] // 128
    first_heads = head_count // 2 if head_count % 2 == 0 else head_count
    first_cols = first_heads * 128
    query_cols = head_count * 128
    start_row = lax.axis_index("ctx") * num_rows
    seq_len = num_rows * lax.axis_size("ctx")
    positions = start_row + jnp.arange(num_rows, dtype=jnp.int32)
    all_pos = jnp.arange(seq_len, dtype=jnp.int32)
    seg_all = segment_ids(lengths[0], all_pos)
    seg_own = lax.dynamic_slice_in_dim(seg_all, start_row, num_rows)
    cosine, sine_table = rope_tables(positions)
    rows_axes = ("dp", "ctx")
    group_count = lax.axis_size(rows_axes)
    head_groups = lax.axis_size("head")
    local_a = jnp.concatenate([w_query[:, :first_cols], w_key, w_value], 1)
    full_a = lax.all_gather(local_a, rows_axes, axis=0, tiled=True)
    split_rows = num_rows % head_groups == 0
    dp_count, ctx_count = lax.axis_size("dp"), lax.axis_size("ctx")
    ctx_index = lax.axis_index("ctx")
    if split_rows:
        quarter = num_rows // head_groups
        own_rows = lax.dynamic_slice_in_dim(hidden_in, lax.axis_index("head") * quarter, quarter, 0)
        cols_part = lax.all_to_all(own_rows, "dp", 1, 0, tiled=True)
    else:
        cols_part = lax.all_to_all(hidden_in, "dp", 1, 0, tiled=True)
    full_a, w_query, cols_part = lax.optimization_barrier((full_a, w_query, cols_part))
    hidden_cols = cols_part
    if split_rows:
        spread = jnp.broadcast_to(cols_part[None], (head_groups,) + cols_part.shape)
        cols_all = lax.all_to_all(spread, "head", 0, 0, tiled=False)
        hidden_cols = (
            cols_all.reshape(head_groups, dp_count, quarter, -1)
            .transpose(1, 0, 2, 3)
            .reshape(dp_count * num_rows, -1)
        )
    weight_rows = w_query.shape[0]

    def weight_grad(d_rows, gathered=None):
        if gathered is None:
            gathered = lax.all_gather(d_rows, "dp", axis=0, tiled=True)
        partial = lax.dot_general(
            hidden_cols, gathered, (((0,), (0,)), ((), ())), preferred_element_type=jnp.float32
        )
        if ctx_count == 2:
            own_part = lax.dynamic_slice_in_dim(partial, ctx_index * weight_rows, weight_rows, 0)
            away_part = lax.dynamic_slice_in_dim(
                partial, (1 - ctx_index) * weight_rows, weight_rows, 0
            )
            return own_part + lax.ppermute(away_part, "ctx", [(0, 1), (1, 0)])
        return lax.psum_scatter(partial, "ctx", scatter_dimension=0, tiled=True)

    proj_a = jnp.dot(hidden_in, full_a, preferred_element_type=jnp.float32)
    query_a = rotate(
        proj_a[:, :first_cols].reshape(num_rows, first_heads, 128), cosine, sine_table
    ).astype(jnp.bfloat16)
    key_rows = rotate(
        proj_a[:, first_cols : first_cols + 128].reshape(num_rows, 1, 128), cosine, sine_table
    )[:, 0, :].astype(jnp.bfloat16)
    value_rows = proj_a[:, first_cols + 128 :].astype(jnp.bfloat16)
    kv_rows = jnp.concatenate([key_rows, value_rows], 1)
    if ctx_count == 2:
        kv_other = lax.ppermute(kv_rows, "ctx", [(0, 1), (1, 0)])
        kv_all = jnp.where(
            ctx_index == 0,
            jnp.concatenate([kv_rows, kv_other], 0),
            jnp.concatenate([kv_other, kv_rows], 0),
        )
    else:
        kv_all = lax.all_gather(kv_rows, "ctx", axis=0, tiled=True)
    key_all, value_all = kv_all[:, :128], kv_all[:, 128:]
    dout_rows = attn_grad.reshape(num_rows, head_count, 128)
    shared = (key_all, value_all)
    masks = (positions, all_pos, seg_own, seg_all)
    out_a, grad_qa, part_k, part_v = attend(query_a, *shared, dout_rows[:, :first_heads], *masks)
    d_query_a = unrotate(grad_qa, cosine, sine_table).astype(jnp.bfloat16).reshape(num_rows, -1)
    out_parts, d_query_parts = [out_a], [d_query_a]
    if first_heads < head_count:
        w_rest = w_query[:, first_cols:]
        full_b = lax.all_gather(w_rest, rows_axes, axis=0, tiled=True)
        d_query_a, full_b, hidden_cols = lax.optimization_barrier((d_query_a, full_b, hidden_cols))
        early_all = lax.all_gather(d_query_a, "dp", axis=0, tiled=True)
        proj_b = jnp.dot(hidden_in, full_b, preferred_element_type=jnp.float32)
        query_b = rotate(
            proj_b.reshape(num_rows, head_count - first_heads, 128), cosine, sine_table
        ).astype(jnp.bfloat16)
        out_b, grad_qb, part_kb, part_vb = attend(
            query_b, *shared, dout_rows[:, first_heads:], *masks
        )
        early_all, grad_qb = lax.optimization_barrier((early_all, grad_qb))
        early_sum = weight_grad(d_query_a, early_all)
        d_query_b = unrotate(grad_qb, cosine, sine_table).astype(jnp.bfloat16).reshape(num_rows, -1)
        mid_all = lax.all_gather(d_query_b, "dp", axis=0, tiled=True)
        part_k, part_v = part_k + part_kb, part_v + part_vb
        out_parts.append(out_b)
    attended = jnp.concatenate(out_parts, 1).reshape(num_rows, query_cols)
    parts_kv = jnp.concatenate([part_k, part_v], 1)
    if ctx_count == 2:
        own_part = lax.dynamic_slice_in_dim(parts_kv, ctx_index * num_rows, num_rows, 0)
        away_part = lax.dynamic_slice_in_dim(parts_kv, (1 - ctx_index) * num_rows, num_rows, 0)
        grad_kv = own_part + lax.ppermute(away_part, "ctx", [(0, 1), (1, 0)])
    else:
        grad_kv = lax.psum_scatter(parts_kv, "ctx", scatter_dimension=0, tiled=True)
    grad_k, grad_v = grad_kv[:, :128], grad_kv[:, 128:]
    d_key = unrotate(grad_k[:, None, :], cosine, sine_table)[:, 0, :].astype(jnp.bfloat16)
    d_value = grad_v.astype(jnp.bfloat16)
    d_proj_a = jnp.concatenate([d_query_a, d_key, d_value], 1)
    input_part = lax.dot_general(
        d_proj_a, full_a, (((1,), (1,)), ((), ())), preferred_element_type=jnp.float32
    )
    if first_heads < head_count:
        input_part = input_part + lax.dot_general(
            d_query_b, full_b, (((1,), (1,)), ((), ())), preferred_element_type=jnp.float32
        )
        late_proj = jnp.concatenate([d_key, d_value], 1)
        mid_sum = weight_grad(d_query_b, mid_all)
        early_sum = jnp.concatenate([early_sum, mid_sum], 1)
    else:
        late_proj = jnp.concatenate([d_key, d_value], 1)
        early_sum = weight_grad(d_query_a)
    early_sum, input_part = lax.optimization_barrier((early_sum, input_part))
    input_cols = input_part.shape[1] // head_groups
    input_split = lax.all_to_all(
        input_part.astype(jnp.bfloat16).reshape(num_rows, head_groups, input_cols),
        "head", 1, 1, tiled=False,
    )
    grad_input = jnp.sum(input_split.astype(jnp.float32), axis=1).astype(jnp.bfloat16)
    late_sum = weight_grad(late_proj)
    query_w = early_sum
    rest = late_sum
    return (attended, grad_input, query_w, rest[:, :128], rest[:, 128:])


def solution(mesh):
    placed = (
        P(("dp", "ctx"), None),
        P(("dp", "ctx"), "head"),
        P(("dp", "ctx"), "head"),
        P(("dp", "ctx"), "head"),
        P("dp", None),
        P(("dp", "ctx"), "head"),
    )
    return jax.shard_map(
        local,
        mesh=mesh,
        in_specs=placed,
        out_specs=(
            P(("dp", "ctx"), "head"),
            P(("dp", "ctx"), "head"),
            P(("dp", "ctx"), "head"),
            P(("dp", "ctx"), "head"),
            P(("dp", "ctx"), "head"),
        ),
        check_vma=False,
    )
```

```python
import jax
import jax.numpy as jnp
from jax import lax
from jax.sharding import PartitionSpec as P

scale_factor = 128.0 ** (-0.5)
neg_large = -1e30


def rope_tables(positions):
    inverse = jnp.power(500000.0, -jnp.arange(64, dtype=jnp.float32) / 64.0)
    angles = positions.astype(jnp.float32)[:, None] * inverse[None, :]
    return (jnp.cos(angles)[:, None, :], jnp.sin(angles)[:, None, :])


def rotate(entries, cosine, sine_table):
    first_half = entries[..., :64]
    second_half = entries[..., 64:]
    return jnp.concatenate(
        [
            first_half * cosine - second_half * sine_table,
            second_half * cosine + first_half * sine_table,
        ],
        -1,
    )


def unrotate(entries, cosine, sine_table):
    first_half = entries[..., :64]
    second_half = entries[..., 64:]
    return jnp.concatenate(
        [
            first_half * cosine + second_half * sine_table,
            second_half * cosine - first_half * sine_table,
        ],
        -1,
    )


def segment_ids(length_row, positions):
    ends = jnp.cumsum(length_row)
    return jnp.sum((positions[:, None] >= ends[None, :]).astype(jnp.int32), 1)


def block_scores(query_blk, key_blk, query_pos, key_pos, query_seg, key_seg):
    scores = (
        jnp.einsum("rhd,kd->hrk", query_blk, key_blk, preferred_element_type=jnp.float32)
        * scale_factor
    )
    allowed = (key_pos[None, :] <= query_pos[:, None]) & (key_seg[None, :] == query_seg[:, None])
    return (scores, allowed[None])


def grad_block(
    query_blk,
    dout_blk,
    total_blk,
    delta_blk,
    key_blk,
    value_blk,
    query_pos,
    key_pos,
    query_seg,
    key_seg,
):
    scores, allowed = block_scores(query_blk, key_blk, query_pos, key_pos, query_seg, key_seg)
    prob_rows = jnp.where(
        allowed, jnp.exp(jnp.where(allowed, scores - total_blk[..., None], neg_large)), 0.0
    )
    prob_b = prob_rows.astype(jnp.bfloat16)
    d_prob = jnp.einsum("rhd,kd->hrk", dout_blk, value_blk, preferred_element_type=jnp.float32)
    d_score = (scale_factor * prob_rows * (d_prob - delta_blk[..., None])).astype(jnp.bfloat16)
    return (prob_b, d_score)


def attend_whole(query_rows, key_all, value_all, dout_rows, positions, all_pos, seg_own, seg_all):
    scores, allowed = block_scores(query_rows, key_all, positions, all_pos, seg_own, seg_all)
    masked = jnp.where(allowed, scores, neg_large)
    top_score = jnp.max(masked, -1)
    total = jnp.sum(jnp.where(allowed, jnp.exp(masked - top_score[..., None]), 0.0), -1)
    log_total = top_score + jnp.log(total)
    prob_rows = jnp.where(
        allowed, jnp.exp(jnp.where(allowed, scores - log_total[..., None], neg_large)), 0.0
    )
    prob_b = prob_rows.astype(jnp.bfloat16)
    out_rows = jnp.einsum(
        "hrk,kd->rhd", prob_b, value_all, preferred_element_type=jnp.float32
    ).astype(jnp.bfloat16)
    delta_rows = jnp.einsum("rhd,rhd->hr", dout_rows, out_rows, preferred_element_type=jnp.float32)
    d_prob = jnp.einsum("rhd,kd->hrk", dout_rows, value_all, preferred_element_type=jnp.float32)
    d_score = (scale_factor * prob_rows * (d_prob - delta_rows[..., None])).astype(jnp.bfloat16)
    grad_q = jnp.einsum("hrk,kd->rhd", d_score, key_all, preferred_element_type=jnp.float32)
    part_k = jnp.einsum("hrk,rhd->kd", d_score, query_rows, preferred_element_type=jnp.float32)
    part_v = jnp.einsum("hrk,rhd->kd", prob_b, dout_rows, preferred_element_type=jnp.float32)
    return out_rows, grad_q, part_k, part_v


def attend_blocked(query_rows, key_all, value_all, dout_rows, positions, all_pos, seg_own, seg_all, kblock):
    num_rows, head_count = query_rows.shape[0], query_rows.shape[1]
    seq_len = key_all.shape[0]
    causal_limit = (positions[-1] + kblock) // kblock
    key_first = jnp.int32(0)

    def take_block(block_index):
        first_row = block_index * kblock
        return (
            lax.dynamic_slice_in_dim(key_all, first_row, kblock, 0),
            lax.dynamic_slice_in_dim(value_all, first_row, kblock, 0),
            lax.dynamic_slice_in_dim(all_pos, first_row, kblock, 0),
            lax.dynamic_slice_in_dim(seg_all, first_row, kblock, 0),
        )

    def stats_step(block_index, carried):
        run_max, run_sum = carried
        key_blk, value_blk, key_pos, key_seg = take_block(block_index)
        scores, allowed = block_scores(query_rows, key_blk, positions, key_pos, seg_own, key_seg)
        masked = jnp.where(allowed, scores, neg_large)
        new_max = jnp.maximum(run_max, jnp.max(masked, -1))
        terms = jnp.where(allowed, jnp.exp(masked - new_max[..., None]), 0.0)
        return (new_max, run_sum * jnp.exp(run_max - new_max) + jnp.sum(terms, -1))

    start_stats = (
        jnp.full((head_count, num_rows), neg_large, jnp.float32),
        jnp.zeros((head_count, num_rows), jnp.float32),
    )
    run_max, run_sum = lax.fori_loop(key_first, causal_limit, stats_step, start_stats)
    log_total = run_max + jnp.log(run_sum)

    def output_step(block_index, carried):
        key_blk, value_blk, key_pos, key_seg = take_block(block_index)
        scores, allowed = block_scores(query_rows, key_blk, positions, key_pos, seg_own, key_seg)
        prob_b = jnp.where(
            allowed, jnp.exp(jnp.where(allowed, scores - log_total[..., None], neg_large)), 0.0
        ).astype(jnp.bfloat16)
        return carried + jnp.einsum(
            "hrk,kd->rhd", prob_b, value_blk, preferred_element_type=jnp.float32
        )

    out_sum = lax.fori_loop(
        key_first, causal_limit, output_step, jnp.zeros((num_rows, head_count, 128), jnp.float32)
    )
    out_rows = out_sum.astype(jnp.bfloat16)
    delta_rows = jnp.einsum("rhd,rhd->hr", dout_rows, out_rows, preferred_element_type=jnp.float32)

    def sums_step(block_index, carried):
        grad_q, part_k, part_v = carried
        first_row = block_index * kblock
        key_blk, value_blk, key_pos, key_seg = take_block(block_index)
        prob_b, d_score = grad_block(
            query_rows, dout_rows, log_total, delta_rows, key_blk, value_blk,
            positions, key_pos, seg_own, key_seg,
        )
        grad_q = grad_q + jnp.einsum(
            "hrk,kd->rhd", d_score, key_blk, preferred_element_type=jnp.float32
        )
        block_k = jnp.einsum("hrk,rhd->kd", d_score, query_rows, preferred_element_type=jnp.float32)
        block_v = jnp.einsum("hrk,rhd->kd", prob_b, dout_rows, preferred_element_type=jnp.float32)
        part_k = lax.dynamic_update_slice_in_dim(
            part_k, lax.dynamic_slice_in_dim(part_k, first_row, kblock, 0) + block_k, first_row, 0
        )
        part_v = lax.dynamic_update_slice_in_dim(
            part_v, lax.dynamic_slice_in_dim(part_v, first_row, kblock, 0) + block_v, first_row, 0
        )
        return (grad_q, part_k, part_v)

    start_sums = (
        jnp.zeros((num_rows, head_count, 128), jnp.float32),
        jnp.zeros((seq_len, 128), jnp.float32),
        jnp.zeros((seq_len, 128), jnp.float32),
    )
    grad_q, part_k, part_v = lax.fori_loop(key_first, causal_limit, sums_step, start_sums)
    return out_rows, grad_q, part_k, part_v


def attend(query_rows, key_all, value_all, dout_rows, positions, all_pos, seg_own, seg_all):
    head_count, num_rows, seq_len = query_rows.shape[1], query_rows.shape[0], key_all.shape[0]
    operands = (query_rows, key_all, value_all, dout_rows, positions, all_pos, seg_own, seg_all)
    if head_count * num_rows * seq_len <= (1 << 22):
        return attend_whole(*operands)
    kblock = seq_len
    while head_count * num_rows * kblock > (1 << 21) and kblock % 256 == 0:
        kblock //= 2
    return attend_blocked(*operands, kblock)


def local(hidden_in, w_query, w_key, w_value, lengths, attn_grad):
    num_rows = hidden_in.shape[0]
    head_count = w_query.shape[1] // 128
    first_heads = head_count // 2 if head_count % 2 == 0 else head_count
    first_cols = first_heads * 128
    query_cols = head_count * 128
    start_row = lax.axis_index("ctx") * num_rows
    seq_len = num_rows * lax.axis_size("ctx")
    positions = start_row + jnp.arange(num_rows, dtype=jnp.int32)
    all_pos = jnp.arange(seq_len, dtype=jnp.int32)
    seg_all = segment_ids(lengths[0], all_pos)
    seg_own = lax.dynamic_slice_in_dim(seg_all, start_row, num_rows)
    cosine, sine_table = rope_tables(positions)
    rows_axes = ("dp", "ctx")
    group_count = lax.axis_size(rows_axes)
    head_groups = lax.axis_size("head")
    local_a = jnp.concatenate([w_query[:, :first_cols], w_key, w_value], 1)
    full_a = lax.all_gather(local_a, rows_axes, axis=0, tiled=True)
    split_rows = num_rows % head_groups == 0
    dp_count, ctx_count = lax.axis_size("dp"), lax.axis_size("ctx")
    ctx_index = lax.axis_index("ctx")
    if split_rows:
        quarter = num_rows // head_groups
        own_rows = lax.dynamic_slice_in_dim(hidden_in, lax.axis_index("head") * quarter, quarter, 0)
        cols_part = lax.all_to_all(own_rows, "dp", 1, 0, tiled=True)
    else:
        cols_part = lax.all_to_all(hidden_in, "dp", 1, 0, tiled=True)
    full_a, w_query, cols_part = lax.optimization_barrier((full_a, w_query, cols_part))
    hidden_cols = cols_part
    if split_rows:
        spread = jnp.broadcast_to(cols_part[None], (head_groups,) + cols_part.shape)
        cols_all = lax.all_to_all(spread, "head", 0, 0, tiled=False)
        hidden_cols = (
            cols_all.reshape(head_groups, dp_count, quarter, -1)
            .transpose(1, 0, 2, 3)
            .reshape(dp_count * num_rows, -1)
        )
    weight_rows = w_query.shape[0]

    def weight_grad(d_rows, gathered=None):
        if gathered is None:
            gathered = lax.all_gather(d_rows, "dp", axis=0, tiled=True)
        partial = lax.dot_general(
            hidden_cols, gathered, (((0,), (0,)), ((), ())), preferred_element_type=jnp.float32
        )
        if ctx_count == 2:
            own_part = lax.dynamic_slice_in_dim(partial, ctx_index * weight_rows, weight_rows, 0)
            away_part = lax.dynamic_slice_in_dim(
                partial, (1 - ctx_index) * weight_rows, weight_rows, 0
            )
            sent = lax.ppermute(away_part.astype(jnp.bfloat16), "ctx", [(0, 1), (1, 0)])
            return own_part + sent.astype(jnp.float32)
        return lax.psum_scatter(partial, "ctx", scatter_dimension=0, tiled=True)

    proj_a = jnp.dot(hidden_in, full_a, preferred_element_type=jnp.float32)
    query_a = rotate(
        proj_a[:, :first_cols].reshape(num_rows, first_heads, 128), cosine, sine_table
    ).astype(jnp.bfloat16)
    key_rows = rotate(
        proj_a[:, first_cols : first_cols + 128].reshape(num_rows, 1, 128), cosine, sine_table
    )[:, 0, :].astype(jnp.bfloat16)
    value_rows = proj_a[:, first_cols + 128 :].astype(jnp.bfloat16)
    kv_rows = jnp.concatenate([key_rows, value_rows], 1)
    if ctx_count == 2:
        kv_other = lax.ppermute(kv_rows, "ctx", [(0, 1), (1, 0)])
        kv_all = jnp.where(
            ctx_index == 0,
            jnp.concatenate([kv_rows, kv_other], 0),
            jnp.concatenate([kv_other, kv_rows], 0),
        )
    else:
        kv_all = lax.all_gather(kv_rows, "ctx", axis=0, tiled=True)
    key_all, value_all = kv_all[:, :128], kv_all[:, 128:]
    dout_rows = attn_grad.reshape(num_rows, head_count, 128)
    shared = (key_all, value_all)
    masks = (positions, all_pos, seg_own, seg_all)
    out_a, grad_qa, part_k, part_v = attend(query_a, *shared, dout_rows[:, :first_heads], *masks)
    d_query_a = unrotate(grad_qa, cosine, sine_table).astype(jnp.bfloat16).reshape(num_rows, -1)
    out_parts, d_query_parts = [out_a], [d_query_a]
    if first_heads < head_count:
        w_rest = w_query[:, first_cols:]
        full_b = lax.all_gather(w_rest, rows_axes, axis=0, tiled=True)
        d_query_a, full_b, hidden_cols = lax.optimization_barrier((d_query_a, full_b, hidden_cols))
        early_all = lax.all_gather(d_query_a, "dp", axis=0, tiled=True)
        proj_b = jnp.dot(hidden_in, full_b, preferred_element_type=jnp.float32)
        query_b = rotate(
            proj_b.reshape(num_rows, head_count - first_heads, 128), cosine, sine_table
        ).astype(jnp.bfloat16)
        out_b, grad_qb, part_kb, part_vb = attend(
            query_b, *shared, dout_rows[:, first_heads:], *masks
        )
        early_all, grad_qb = lax.optimization_barrier((early_all, grad_qb))
        early_sum = weight_grad(d_query_a, early_all)
        d_query_b = unrotate(grad_qb, cosine, sine_table).astype(jnp.bfloat16).reshape(num_rows, -1)
        part_k, part_v = part_k + part_kb, part_v + part_vb
        out_parts.append(out_b)
    attended = jnp.concatenate(out_parts, 1).reshape(num_rows, query_cols)
    parts_kv = jnp.concatenate([part_k, part_v], 1)
    if ctx_count == 2:
        own_part = lax.dynamic_slice_in_dim(parts_kv, ctx_index * num_rows, num_rows, 0)
        away_part = lax.dynamic_slice_in_dim(parts_kv, (1 - ctx_index) * num_rows, num_rows, 0)
        grad_kv = own_part + lax.ppermute(away_part, "ctx", [(0, 1), (1, 0)])
    else:
        grad_kv = lax.psum_scatter(parts_kv, "ctx", scatter_dimension=0, tiled=True)
    grad_k, grad_v = grad_kv[:, :128], grad_kv[:, 128:]
    d_key = unrotate(grad_k[:, None, :], cosine, sine_table)[:, 0, :].astype(jnp.bfloat16)
    d_value = grad_v.astype(jnp.bfloat16)
    d_proj_a = jnp.concatenate([d_query_a, d_key, d_value], 1)
    input_part = lax.dot_general(
        d_proj_a, full_a, (((1,), (1,)), ((), ())), preferred_element_type=jnp.float32
    )
    if first_heads < head_count:
        input_part = input_part + lax.dot_general(
            d_query_b, full_b, (((1,), (1,)), ((), ())), preferred_element_type=jnp.float32
        )
        late_proj = jnp.concatenate([d_query_b, d_key, d_value], 1)
    else:
        late_proj = jnp.concatenate([d_key, d_value], 1)
        early_sum = weight_grad(d_query_a)
    early_sum, input_part = lax.optimization_barrier((early_sum, input_part))
    input_cols = input_part.shape[1] // head_groups
    input_split = lax.all_to_all(
        input_part.astype(jnp.bfloat16).reshape(num_rows, head_groups, input_cols),
        "head", 1, 1, tiled=False,
    )
    grad_input = jnp.sum(input_split.astype(jnp.float32), axis=1).astype(jnp.bfloat16)
    late_sum = weight_grad(late_proj)
    query_w = jnp.concatenate([early_sum, late_sum[:, : query_cols - first_cols]], 1)
    rest = late_sum[:, query_cols - first_cols :]
    return (attended, grad_input, query_w, rest[:, :128], rest[:, 128:])


def solution(mesh):
    placed = (
        P(("dp", "ctx"), None),
        P(("dp", "ctx"), "head"),
        P(("dp", "ctx"), "head"),
        P(("dp", "ctx"), "head"),
        P("dp", None),
        P(("dp", "ctx"), "head"),
    )
    return jax.shard_map(
        local,
        mesh=mesh,
        in_specs=placed,
        out_specs=(
            P(("dp", "ctx"), "head"),
            P(("dp", "ctx"), "head"),
            P(("dp", "ctx"), "head"),
            P(("dp", "ctx"), "head"),
            P(("dp", "ctx"), "head"),
        ),
        check_vma=False,
    )
```

```python
import jax
import jax.numpy as jnp
from jax import lax
from jax.sharding import PartitionSpec as P

scale_factor = 128.0 ** (-0.5)
neg_large = -1e30


def rope_tables(positions):
    inverse = jnp.power(500000.0, -jnp.arange(64, dtype=jnp.float32) / 64.0)
    angles = positions.astype(jnp.float32)[:, None] * inverse[None, :]
    return (jnp.cos(angles)[:, None, :], jnp.sin(angles)[:, None, :])


def rotate(entries, cosine, sine_table):
    first_half = entries[..., :64]
    second_half = entries[..., 64:]
    return jnp.concatenate(
        [
            first_half * cosine - second_half * sine_table,
            second_half * cosine + first_half * sine_table,
        ],
        -1,
    )


def unrotate(entries, cosine, sine_table):
    first_half = entries[..., :64]
    second_half = entries[..., 64:]
    return jnp.concatenate(
        [
            first_half * cosine + second_half * sine_table,
            second_half * cosine - first_half * sine_table,
        ],
        -1,
    )


def segment_ids(length_row, positions):
    ends = jnp.cumsum(length_row)
    return jnp.sum((positions[:, None] >= ends[None, :]).astype(jnp.int32), 1)


def block_scores(query_blk, key_blk, query_pos, key_pos, query_seg, key_seg):
    scores = (
        jnp.einsum("rhd,kd->hrk", query_blk, key_blk, preferred_element_type=jnp.float32)
        * scale_factor
    )
    allowed = (key_pos[None, :] <= query_pos[:, None]) & (key_seg[None, :] == query_seg[:, None])
    return (scores, allowed[None])


def grad_block(
    query_blk,
    dout_blk,
    total_blk,
    delta_blk,
    key_blk,
    value_blk,
    query_pos,
    key_pos,
    query_seg,
    key_seg,
):
    scores, allowed = block_scores(query_blk, key_blk, query_pos, key_pos, query_seg, key_seg)
    prob_rows = jnp.where(
        allowed, jnp.exp(jnp.where(allowed, scores - total_blk[..., None], neg_large)), 0.0
    )
    prob_b = prob_rows.astype(jnp.bfloat16)
    d_prob = jnp.einsum("rhd,kd->hrk", dout_blk, value_blk, preferred_element_type=jnp.float32)
    d_score = (scale_factor * prob_rows * (d_prob - delta_blk[..., None])).astype(jnp.bfloat16)
    return (prob_b, d_score)


def attend_whole(query_rows, key_all, value_all, dout_rows, positions, all_pos, seg_own, seg_all):
    scores, allowed = block_scores(query_rows, key_all, positions, all_pos, seg_own, seg_all)
    masked = jnp.where(allowed, scores, neg_large)
    top_score = jnp.max(masked, -1)
    total = jnp.sum(jnp.where(allowed, jnp.exp(masked - top_score[..., None]), 0.0), -1)
    log_total = top_score + jnp.log(total)
    prob_rows = jnp.where(
        allowed, jnp.exp(jnp.where(allowed, scores - log_total[..., None], neg_large)), 0.0
    )
    prob_b = prob_rows.astype(jnp.bfloat16)
    out_rows = jnp.einsum(
        "hrk,kd->rhd", prob_b, value_all, preferred_element_type=jnp.float32
    ).astype(jnp.bfloat16)
    delta_rows = jnp.einsum("rhd,rhd->hr", dout_rows, out_rows, preferred_element_type=jnp.float32)
    d_prob = jnp.einsum("rhd,kd->hrk", dout_rows, value_all, preferred_element_type=jnp.float32)
    d_score = (scale_factor * prob_rows * (d_prob - delta_rows[..., None])).astype(jnp.bfloat16)
    grad_q = jnp.einsum("hrk,kd->rhd", d_score, key_all, preferred_element_type=jnp.float32)
    part_k = jnp.einsum("hrk,rhd->kd", d_score, query_rows, preferred_element_type=jnp.float32)
    part_v = jnp.einsum("hrk,rhd->kd", prob_b, dout_rows, preferred_element_type=jnp.float32)
    return out_rows, grad_q, part_k, part_v


def attend_blocked(query_rows, key_all, value_all, dout_rows, positions, all_pos, seg_own, seg_all, kblock):
    num_rows, head_count = query_rows.shape[0], query_rows.shape[1]
    seq_len = key_all.shape[0]
    causal_limit = (positions[-1] + kblock) // kblock
    key_first = jnp.int32(0)

    def take_block(block_index):
        first_row = block_index * kblock
        return (
            lax.dynamic_slice_in_dim(key_all, first_row, kblock, 0),
            lax.dynamic_slice_in_dim(value_all, first_row, kblock, 0),
            lax.dynamic_slice_in_dim(all_pos, first_row, kblock, 0),
            lax.dynamic_slice_in_dim(seg_all, first_row, kblock, 0),
        )

    def stats_step(block_index, carried):
        run_max, run_sum = carried
        key_blk, value_blk, key_pos, key_seg = take_block(block_index)
        scores, allowed = block_scores(query_rows, key_blk, positions, key_pos, seg_own, key_seg)
        masked = jnp.where(allowed, scores, neg_large)
        new_max = jnp.maximum(run_max, jnp.max(masked, -1))
        terms = jnp.where(allowed, jnp.exp(masked - new_max[..., None]), 0.0)
        return (new_max, run_sum * jnp.exp(run_max - new_max) + jnp.sum(terms, -1))

    start_stats = (
        jnp.full((head_count, num_rows), neg_large, jnp.float32),
        jnp.zeros((head_count, num_rows), jnp.float32),
    )
    run_max, run_sum = lax.fori_loop(key_first, causal_limit, stats_step, start_stats)
    log_total = run_max + jnp.log(run_sum)

    def output_step(block_index, carried):
        key_blk, value_blk, key_pos, key_seg = take_block(block_index)
        scores, allowed = block_scores(query_rows, key_blk, positions, key_pos, seg_own, key_seg)
        prob_b = jnp.where(
            allowed, jnp.exp(jnp.where(allowed, scores - log_total[..., None], neg_large)), 0.0
        ).astype(jnp.bfloat16)
        return carried + jnp.einsum(
            "hrk,kd->rhd", prob_b, value_blk, preferred_element_type=jnp.float32
        )

    out_sum = lax.fori_loop(
        key_first, causal_limit, output_step, jnp.zeros((num_rows, head_count, 128), jnp.float32)
    )
    out_rows = out_sum.astype(jnp.bfloat16)
    delta_rows = jnp.einsum("rhd,rhd->hr", dout_rows, out_rows, preferred_element_type=jnp.float32)

    def sums_step(block_index, carried):
        grad_q, part_k, part_v = carried
        first_row = block_index * kblock
        key_blk, value_blk, key_pos, key_seg = take_block(block_index)
        prob_b, d_score = grad_block(
            query_rows, dout_rows, log_total, delta_rows, key_blk, value_blk,
            positions, key_pos, seg_own, key_seg,
        )
        grad_q = grad_q + jnp.einsum(
            "hrk,kd->rhd", d_score, key_blk, preferred_element_type=jnp.float32
        )
        block_k = jnp.einsum("hrk,rhd->kd", d_score, query_rows, preferred_element_type=jnp.float32)
        block_v = jnp.einsum("hrk,rhd->kd", prob_b, dout_rows, preferred_element_type=jnp.float32)
        part_k = lax.dynamic_update_slice_in_dim(
            part_k, lax.dynamic_slice_in_dim(part_k, first_row, kblock, 0) + block_k, first_row, 0
        )
        part_v = lax.dynamic_update_slice_in_dim(
            part_v, lax.dynamic_slice_in_dim(part_v, first_row, kblock, 0) + block_v, first_row, 0
        )
        return (grad_q, part_k, part_v)

    start_sums = (
        jnp.zeros((num_rows, head_count, 128), jnp.float32),
        jnp.zeros((seq_len, 128), jnp.float32),
        jnp.zeros((seq_len, 128), jnp.float32),
    )
    grad_q, part_k, part_v = lax.fori_loop(key_first, causal_limit, sums_step, start_sums)
    return out_rows, grad_q, part_k, part_v


def attend(query_rows, key_all, value_all, dout_rows, positions, all_pos, seg_own, seg_all):
    head_count, num_rows, seq_len = query_rows.shape[1], query_rows.shape[0], key_all.shape[0]
    operands = (query_rows, key_all, value_all, dout_rows, positions, all_pos, seg_own, seg_all)
    if head_count * num_rows * seq_len <= (1 << 22):
        return attend_whole(*operands)
    kblock = seq_len
    while head_count * num_rows * kblock > (1 << 21) and kblock % 256 == 0:
        kblock //= 2
    return attend_blocked(*operands, kblock)


def local(hidden_in, w_query, w_key, w_value, lengths, attn_grad):
    num_rows = hidden_in.shape[0]
    head_count = w_query.shape[1] // 128
    first_heads = head_count // 2 if head_count % 2 == 0 else head_count
    first_cols = first_heads * 128
    query_cols = head_count * 128
    start_row = lax.axis_index("ctx") * num_rows
    seq_len = num_rows * lax.axis_size("ctx")
    positions = start_row + jnp.arange(num_rows, dtype=jnp.int32)
    all_pos = jnp.arange(seq_len, dtype=jnp.int32)
    seg_all = segment_ids(lengths[0], all_pos)
    seg_own = lax.dynamic_slice_in_dim(seg_all, start_row, num_rows)
    cosine, sine_table = rope_tables(positions)
    rows_axes = ("dp", "ctx")
    group_count = lax.axis_size(rows_axes)
    head_groups = lax.axis_size("head")
    local_a = jnp.concatenate([w_query[:, :first_cols], w_key, w_value], 1)
    full_a = lax.all_gather(local_a, rows_axes, axis=0, tiled=True)
    split_rows = num_rows % head_groups == 0
    dp_count, ctx_count = lax.axis_size("dp"), lax.axis_size("ctx")
    ctx_index = lax.axis_index("ctx")
    if split_rows:
        quarter = num_rows // head_groups
        own_rows = lax.dynamic_slice_in_dim(hidden_in, lax.axis_index("head") * quarter, quarter, 0)
        cols_part = lax.all_to_all(own_rows, "dp", 1, 0, tiled=True)
    else:
        cols_part = lax.all_to_all(hidden_in, "dp", 1, 0, tiled=True)
    full_a, w_query, cols_part = lax.optimization_barrier((full_a, w_query, cols_part))
    hidden_cols = cols_part
    if split_rows:
        spread = jnp.broadcast_to(cols_part[None], (head_groups,) + cols_part.shape)
        cols_all = lax.all_to_all(spread, "head", 0, 0, tiled=False)
        hidden_cols = (
            cols_all.reshape(head_groups, dp_count, quarter, -1)
            .transpose(1, 0, 2, 3)
            .reshape(dp_count * num_rows, -1)
        )
    weight_rows = w_query.shape[0]

    def weight_grad(d_rows, gathered=None):
        if gathered is None:
            gathered = lax.all_gather(d_rows, "dp", axis=0, tiled=True)
        partial = lax.dot_general(
            hidden_cols, gathered, (((0,), (0,)), ((), ())), preferred_element_type=jnp.float32
        )
        if ctx_count == 2:
            own_part = lax.dynamic_slice_in_dim(partial, ctx_index * weight_rows, weight_rows, 0)
            away_part = lax.dynamic_slice_in_dim(
                partial, (1 - ctx_index) * weight_rows, weight_rows, 0
            )
            sent = lax.ppermute(away_part.astype(jnp.bfloat16), "ctx", [(0, 1), (1, 0)])
            return own_part + sent.astype(jnp.float32)
        return lax.psum_scatter(partial, "ctx", scatter_dimension=0, tiled=True)

    proj_a = jnp.dot(hidden_in, full_a, preferred_element_type=jnp.float32)
    query_a = rotate(
        proj_a[:, :first_cols].reshape(num_rows, first_heads, 128), cosine, sine_table
    ).astype(jnp.bfloat16)
    key_rows = rotate(
        proj_a[:, first_cols : first_cols + 128].reshape(num_rows, 1, 128), cosine, sine_table
    )[:, 0, :].astype(jnp.bfloat16)
    value_rows = proj_a[:, first_cols + 128 :].astype(jnp.bfloat16)
    kv_rows = jnp.concatenate([key_rows, value_rows], 1)
    if ctx_count == 2:
        kv_other = lax.ppermute(kv_rows, "ctx", [(0, 1), (1, 0)])
        kv_all = jnp.where(
            ctx_index == 0,
            jnp.concatenate([kv_rows, kv_other], 0),
            jnp.concatenate([kv_other, kv_rows], 0),
        )
    else:
        kv_all = lax.all_gather(kv_rows, "ctx", axis=0, tiled=True)
    key_all, value_all = kv_all[:, :128], kv_all[:, 128:]
    dout_rows = attn_grad.reshape(num_rows, head_count, 128)
    shared = (key_all, value_all)
    masks = (positions, all_pos, seg_own, seg_all)
    out_a, grad_qa, part_k, part_v = attend(query_a, *shared, dout_rows[:, :first_heads], *masks)
    d_query_a = unrotate(grad_qa, cosine, sine_table).astype(jnp.bfloat16).reshape(num_rows, -1)
    out_parts, d_query_parts = [out_a], [d_query_a]
    if first_heads < head_count:
        w_rest = w_query[:, first_cols:]
        full_b = lax.all_gather(w_rest, rows_axes, axis=0, tiled=True)
        d_query_a, full_b = lax.optimization_barrier((d_query_a, full_b))
        early_all = lax.all_gather(d_query_a, "dp", axis=0, tiled=True)
        proj_b = jnp.dot(hidden_in, full_b, preferred_element_type=jnp.float32)
        query_b = rotate(
            proj_b.reshape(num_rows, head_count - first_heads, 128), cosine, sine_table
        ).astype(jnp.bfloat16)
        out_b, grad_qb, part_kb, part_vb = attend(
            query_b, *shared, dout_rows[:, first_heads:], *masks
        )
        early_all, grad_qb = lax.optimization_barrier((early_all, grad_qb))
        early_sum = weight_grad(d_query_a, early_all)
        d_query_b = unrotate(grad_qb, cosine, sine_table).astype(jnp.bfloat16).reshape(num_rows, -1)
        part_k, part_v = part_k + part_kb, part_v + part_vb
        out_parts.append(out_b)
    attended = jnp.concatenate(out_parts, 1).reshape(num_rows, query_cols)
    parts_kv = jnp.concatenate([part_k, part_v], 1)
    if ctx_count == 2:
        own_part = lax.dynamic_slice_in_dim(parts_kv, ctx_index * num_rows, num_rows, 0)
        away_part = lax.dynamic_slice_in_dim(parts_kv, (1 - ctx_index) * num_rows, num_rows, 0)
        grad_kv = own_part + lax.ppermute(away_part, "ctx", [(0, 1), (1, 0)])
    else:
        grad_kv = lax.psum_scatter(parts_kv, "ctx", scatter_dimension=0, tiled=True)
    grad_k, grad_v = grad_kv[:, :128], grad_kv[:, 128:]
    d_key = unrotate(grad_k[:, None, :], cosine, sine_table)[:, 0, :].astype(jnp.bfloat16)
    d_value = grad_v.astype(jnp.bfloat16)
    d_proj_a = jnp.concatenate([d_query_a, d_key, d_value], 1)
    input_part = lax.dot_general(
        d_proj_a, full_a, (((1,), (1,)), ((), ())), preferred_element_type=jnp.float32
    )
    if first_heads < head_count:
        input_part = input_part + lax.dot_general(
            d_query_b, full_b, (((1,), (1,)), ((), ())), preferred_element_type=jnp.float32
        )
        late_proj = jnp.concatenate([d_query_b, d_key, d_value], 1)
    else:
        late_proj = jnp.concatenate([d_key, d_value], 1)
        early_sum = weight_grad(d_query_a)
    early_sum, input_part = lax.optimization_barrier((early_sum, input_part))
    input_cols = input_part.shape[1] // head_groups
    input_split = lax.all_to_all(
        input_part.astype(jnp.bfloat16).reshape(num_rows, head_groups, input_cols),
        "head", 1, 1, tiled=False,
    )
    grad_input = jnp.sum(input_split.astype(jnp.float32), axis=1).astype(jnp.bfloat16)
    late_sum = weight_grad(late_proj)
    query_w = jnp.concatenate([early_sum, late_sum[:, : query_cols - first_cols]], 1)
    rest = late_sum[:, query_cols - first_cols :]
    return (attended, grad_input, query_w, rest[:, :128], rest[:, 128:])


def solution(mesh):
    placed = (
        P(("dp", "ctx"), None),
        P(("dp", "ctx"), "head"),
        P(("dp", "ctx"), "head"),
        P(("dp", "ctx"), "head"),
        P("dp", None),
        P(("dp", "ctx"), "head"),
    )
    return jax.shard_map(
        local,
        mesh=mesh,
        in_specs=placed,
        out_specs=(
            P(("dp", "ctx"), "head"),
            P(("dp", "ctx"), "head"),
            P(("dp", "ctx"), "head"),
            P(("dp", "ctx"), "head"),
            P(("dp", "ctx"), "head"),
        ),
        check_vma=False,
    )
```

```python
import jax
import jax.numpy as jnp
from jax import lax
from jax.sharding import PartitionSpec as P

scale_factor = 128.0 ** (-0.5)
neg_large = -1e30


def rope_tables(positions):
    inverse = jnp.power(500000.0, -jnp.arange(64, dtype=jnp.float32) / 64.0)
    angles = positions.astype(jnp.float32)[:, None] * inverse[None, :]
    return (jnp.cos(angles)[:, None, :], jnp.sin(angles)[:, None, :])


def rotate(entries, cosine, sine_table):
    first_half = entries[..., :64]
    second_half = entries[..., 64:]
    return jnp.concatenate(
        [
            first_half * cosine - second_half * sine_table,
            second_half * cosine + first_half * sine_table,
        ],
        -1,
    )


def unrotate(entries, cosine, sine_table):
    first_half = entries[..., :64]
    second_half = entries[..., 64:]
    return jnp.concatenate(
        [
            first_half * cosine + second_half * sine_table,
            second_half * cosine - first_half * sine_table,
        ],
        -1,
    )


def segment_ids(length_row, positions):
    ends = jnp.cumsum(length_row)
    return jnp.sum((positions[:, None] >= ends[None, :]).astype(jnp.int32), 1)


def block_scores(query_blk, key_blk, query_pos, key_pos, query_seg, key_seg):
    scores = (
        jnp.einsum("rhd,kd->hrk", query_blk, key_blk, preferred_element_type=jnp.float32)
        * scale_factor
    )
    allowed = (key_pos[None, :] <= query_pos[:, None]) & (key_seg[None, :] == query_seg[:, None])
    return (scores, allowed[None])


def grad_block(
    query_blk,
    dout_blk,
    total_blk,
    delta_blk,
    key_blk,
    value_blk,
    query_pos,
    key_pos,
    query_seg,
    key_seg,
):
    scores, allowed = block_scores(query_blk, key_blk, query_pos, key_pos, query_seg, key_seg)
    prob_rows = jnp.where(
        allowed, jnp.exp(jnp.where(allowed, scores - total_blk[..., None], neg_large)), 0.0
    )
    prob_b = prob_rows.astype(jnp.bfloat16)
    d_prob = jnp.einsum("rhd,kd->hrk", dout_blk, value_blk, preferred_element_type=jnp.float32)
    d_score = (scale_factor * prob_rows * (d_prob - delta_blk[..., None])).astype(jnp.bfloat16)
    return (prob_b, d_score)


def attend_whole(query_rows, key_all, value_all, dout_rows, positions, all_pos, seg_own, seg_all):
    scores, allowed = block_scores(query_rows, key_all, positions, all_pos, seg_own, seg_all)
    masked = jnp.where(allowed, scores, neg_large)
    top_score = jnp.max(masked, -1)
    total = jnp.sum(jnp.where(allowed, jnp.exp(masked - top_score[..., None]), 0.0), -1)
    log_total = top_score + jnp.log(total)
    prob_rows = jnp.where(
        allowed, jnp.exp(jnp.where(allowed, scores - log_total[..., None], neg_large)), 0.0
    )
    prob_b = prob_rows.astype(jnp.bfloat16)
    out_rows = jnp.einsum(
        "hrk,kd->rhd", prob_b, value_all, preferred_element_type=jnp.float32
    ).astype(jnp.bfloat16)
    delta_rows = jnp.einsum("rhd,rhd->hr", dout_rows, out_rows, preferred_element_type=jnp.float32)
    d_prob = jnp.einsum("rhd,kd->hrk", dout_rows, value_all, preferred_element_type=jnp.float32)
    d_score = (scale_factor * prob_rows * (d_prob - delta_rows[..., None])).astype(jnp.bfloat16)
    grad_q = jnp.einsum("hrk,kd->rhd", d_score, key_all, preferred_element_type=jnp.float32)
    part_k = jnp.einsum("hrk,rhd->kd", d_score, query_rows, preferred_element_type=jnp.float32)
    part_v = jnp.einsum("hrk,rhd->kd", prob_b, dout_rows, preferred_element_type=jnp.float32)
    return out_rows, grad_q, part_k, part_v


def attend_blocked(query_rows, key_all, value_all, dout_rows, positions, all_pos, seg_own, seg_all, kblock):
    num_rows, head_count = query_rows.shape[0], query_rows.shape[1]
    seq_len = key_all.shape[0]
    causal_limit = (positions[-1] + kblock) // kblock
    key_first = jnp.int32(0)

    def take_block(block_index):
        first_row = block_index * kblock
        return (
            lax.dynamic_slice_in_dim(key_all, first_row, kblock, 0),
            lax.dynamic_slice_in_dim(value_all, first_row, kblock, 0),
            lax.dynamic_slice_in_dim(all_pos, first_row, kblock, 0),
            lax.dynamic_slice_in_dim(seg_all, first_row, kblock, 0),
        )

    def stats_step(block_index, carried):
        run_max, run_sum = carried
        key_blk, value_blk, key_pos, key_seg = take_block(block_index)
        scores, allowed = block_scores(query_rows, key_blk, positions, key_pos, seg_own, key_seg)
        masked = jnp.where(allowed, scores, neg_large)
        new_max = jnp.maximum(run_max, jnp.max(masked, -1))
        terms = jnp.where(allowed, jnp.exp(masked - new_max[..., None]), 0.0)
        return (new_max, run_sum * jnp.exp(run_max - new_max) + jnp.sum(terms, -1))

    start_stats = (
        jnp.full((head_count, num_rows), neg_large, jnp.float32),
        jnp.zeros((head_count, num_rows), jnp.float32),
    )
    run_max, run_sum = lax.fori_loop(key_first, causal_limit, stats_step, start_stats)
    log_total = run_max + jnp.log(run_sum)

    def output_step(block_index, carried):
        key_blk, value_blk, key_pos, key_seg = take_block(block_index)
        scores, allowed = block_scores(query_rows, key_blk, positions, key_pos, seg_own, key_seg)
        prob_b = jnp.where(
            allowed, jnp.exp(jnp.where(allowed, scores - log_total[..., None], neg_large)), 0.0
        ).astype(jnp.bfloat16)
        return carried + jnp.einsum(
            "hrk,kd->rhd", prob_b, value_blk, preferred_element_type=jnp.float32
        )

    out_sum = lax.fori_loop(
        key_first, causal_limit, output_step, jnp.zeros((num_rows, head_count, 128), jnp.float32)
    )
    out_rows = out_sum.astype(jnp.bfloat16)
    delta_rows = jnp.einsum("rhd,rhd->hr", dout_rows, out_rows, preferred_element_type=jnp.float32)

    def sums_step(block_index, carried):
        grad_q, part_k, part_v = carried
        first_row = block_index * kblock
        key_blk, value_blk, key_pos, key_seg = take_block(block_index)
        prob_b, d_score = grad_block(
            query_rows, dout_rows, log_total, delta_rows, key_blk, value_blk,
            positions, key_pos, seg_own, key_seg,
        )
        grad_q = grad_q + jnp.einsum(
            "hrk,kd->rhd", d_score, key_blk, preferred_element_type=jnp.float32
        )
        block_k = jnp.einsum("hrk,rhd->kd", d_score, query_rows, preferred_element_type=jnp.float32)
        block_v = jnp.einsum("hrk,rhd->kd", prob_b, dout_rows, preferred_element_type=jnp.float32)
        part_k = lax.dynamic_update_slice_in_dim(
            part_k, lax.dynamic_slice_in_dim(part_k, first_row, kblock, 0) + block_k, first_row, 0
        )
        part_v = lax.dynamic_update_slice_in_dim(
            part_v, lax.dynamic_slice_in_dim(part_v, first_row, kblock, 0) + block_v, first_row, 0
        )
        return (grad_q, part_k, part_v)

    start_sums = (
        jnp.zeros((num_rows, head_count, 128), jnp.float32),
        jnp.zeros((seq_len, 128), jnp.float32),
        jnp.zeros((seq_len, 128), jnp.float32),
    )
    grad_q, part_k, part_v = lax.fori_loop(key_first, causal_limit, sums_step, start_sums)
    return out_rows, grad_q, part_k, part_v


def attend(query_rows, key_all, value_all, dout_rows, positions, all_pos, seg_own, seg_all):
    head_count, num_rows, seq_len = query_rows.shape[1], query_rows.shape[0], key_all.shape[0]
    operands = (query_rows, key_all, value_all, dout_rows, positions, all_pos, seg_own, seg_all)
    if head_count * num_rows * seq_len <= (1 << 22):
        return attend_whole(*operands)
    kblock = seq_len
    while head_count * num_rows * kblock > (1 << 21) and kblock % 256 == 0:
        kblock //= 2
    return attend_blocked(*operands, kblock)


def local(hidden_in, w_query, w_key, w_value, lengths, attn_grad):
    num_rows = hidden_in.shape[0]
    head_count = w_query.shape[1] // 128
    first_heads = head_count // 2 if head_count % 2 == 0 else head_count
    first_cols = first_heads * 128
    query_cols = head_count * 128
    start_row = lax.axis_index("ctx") * num_rows
    seq_len = num_rows * lax.axis_size("ctx")
    positions = start_row + jnp.arange(num_rows, dtype=jnp.int32)
    all_pos = jnp.arange(seq_len, dtype=jnp.int32)
    seg_all = segment_ids(lengths[0], all_pos)
    seg_own = lax.dynamic_slice_in_dim(seg_all, start_row, num_rows)
    cosine, sine_table = rope_tables(positions)
    rows_axes = ("dp", "ctx")
    group_count = lax.axis_size(rows_axes)
    head_groups = lax.axis_size("head")
    local_a = jnp.concatenate([w_query[:, :first_cols], w_key, w_value], 1)
    full_a = lax.all_gather(local_a, rows_axes, axis=0, tiled=True)
    split_rows = num_rows % head_groups == 0
    dp_count, ctx_count = lax.axis_size("dp"), lax.axis_size("ctx")
    ctx_index = lax.axis_index("ctx")
    if split_rows:
        quarter = num_rows // head_groups
        own_rows = lax.dynamic_slice_in_dim(hidden_in, lax.axis_index("head") * quarter, quarter, 0)
        own_rows, full_a = lax.optimization_barrier((own_rows, full_a))
        cols_part = lax.all_to_all(own_rows, "dp", 1, 0, tiled=True)
    else:
        cols_part = lax.all_to_all(hidden_in, "dp", 1, 0, tiled=True)
    full_a, w_query = lax.optimization_barrier((full_a, w_query))
    hidden_cols = cols_part
    if split_rows:
        spread = jnp.broadcast_to(cols_part[None], (head_groups,) + cols_part.shape)
        cols_all = lax.all_to_all(spread, "head", 0, 0, tiled=False)
        hidden_cols = (
            cols_all.reshape(head_groups, dp_count, quarter, -1)
            .transpose(1, 0, 2, 3)
            .reshape(dp_count * num_rows, -1)
        )
    weight_rows = w_query.shape[0]

    def weight_grad(d_rows, gathered=None):
        if gathered is None:
            gathered = lax.all_gather(d_rows, "dp", axis=0, tiled=True)
        partial = lax.dot_general(
            hidden_cols, gathered, (((0,), (0,)), ((), ())), preferred_element_type=jnp.float32
        )
        if ctx_count == 2:
            own_part = lax.dynamic_slice_in_dim(partial, ctx_index * weight_rows, weight_rows, 0)
            away_part = lax.dynamic_slice_in_dim(
                partial, (1 - ctx_index) * weight_rows, weight_rows, 0
            )
            sent = lax.ppermute(away_part.astype(jnp.bfloat16), "ctx", [(0, 1), (1, 0)])
            return own_part + sent.astype(jnp.float32)
        return lax.psum_scatter(partial, "ctx", scatter_dimension=0, tiled=True)

    proj_a = jnp.dot(hidden_in, full_a, preferred_element_type=jnp.float32)
    query_a = rotate(
        proj_a[:, :first_cols].reshape(num_rows, first_heads, 128), cosine, sine_table
    ).astype(jnp.bfloat16)
    key_rows = rotate(
        proj_a[:, first_cols : first_cols + 128].reshape(num_rows, 1, 128), cosine, sine_table
    )[:, 0, :].astype(jnp.bfloat16)
    value_rows = proj_a[:, first_cols + 128 :].astype(jnp.bfloat16)
    kv_rows = jnp.concatenate([key_rows, value_rows], 1)
    if ctx_count == 2:
        kv_other = lax.ppermute(kv_rows, "ctx", [(0, 1), (1, 0)])
        kv_all = jnp.where(
            ctx_index == 0,
            jnp.concatenate([kv_rows, kv_other], 0),
            jnp.concatenate([kv_other, kv_rows], 0),
        )
    else:
        kv_all = lax.all_gather(kv_rows, "ctx", axis=0, tiled=True)
    key_all, value_all = kv_all[:, :128], kv_all[:, 128:]
    dout_rows = attn_grad.reshape(num_rows, head_count, 128)
    shared = (key_all, value_all)
    masks = (positions, all_pos, seg_own, seg_all)
    out_a, grad_qa, part_k, part_v = attend(query_a, *shared, dout_rows[:, :first_heads], *masks)
    d_query_a = unrotate(grad_qa, cosine, sine_table).astype(jnp.bfloat16).reshape(num_rows, -1)
    out_parts, d_query_parts = [out_a], [d_query_a]
    if first_heads < head_count:
        w_rest = w_query[:, first_cols:]
        full_b = lax.all_gather(w_rest, rows_axes, axis=0, tiled=True)
        d_query_a, full_b = lax.optimization_barrier((d_query_a, full_b))
        early_all = lax.all_gather(d_query_a, "dp", axis=0, tiled=True)
        proj_b = jnp.dot(hidden_in, full_b, preferred_element_type=jnp.float32)
        query_b = rotate(
            proj_b.reshape(num_rows, head_count - first_heads, 128), cosine, sine_table
        ).astype(jnp.bfloat16)
        out_b, grad_qb, part_kb, part_vb = attend(
            query_b, *shared, dout_rows[:, first_heads:], *masks
        )
        early_all, grad_qb = lax.optimization_barrier((early_all, grad_qb))
        early_sum = weight_grad(d_query_a, early_all)
        d_query_b = unrotate(grad_qb, cosine, sine_table).astype(jnp.bfloat16).reshape(num_rows, -1)
        part_k, part_v = part_k + part_kb, part_v + part_vb
        out_parts.append(out_b)
    attended = jnp.concatenate(out_parts, 1).reshape(num_rows, query_cols)
    parts_kv = jnp.concatenate([part_k, part_v], 1)
    if ctx_count == 2:
        own_part = lax.dynamic_slice_in_dim(parts_kv, ctx_index * num_rows, num_rows, 0)
        away_part = lax.dynamic_slice_in_dim(parts_kv, (1 - ctx_index) * num_rows, num_rows, 0)
        grad_kv = own_part + lax.ppermute(away_part, "ctx", [(0, 1), (1, 0)])
    else:
        grad_kv = lax.psum_scatter(parts_kv, "ctx", scatter_dimension=0, tiled=True)
    grad_k, grad_v = grad_kv[:, :128], grad_kv[:, 128:]
    d_key = unrotate(grad_k[:, None, :], cosine, sine_table)[:, 0, :].astype(jnp.bfloat16)
    d_value = grad_v.astype(jnp.bfloat16)
    d_proj_a = jnp.concatenate([d_query_a, d_key, d_value], 1)
    input_part = lax.dot_general(
        d_proj_a, full_a, (((1,), (1,)), ((), ())), preferred_element_type=jnp.float32
    )
    if first_heads < head_count:
        input_part = input_part + lax.dot_general(
            d_query_b, full_b, (((1,), (1,)), ((), ())), preferred_element_type=jnp.float32
        )
        late_proj = jnp.concatenate([d_query_b, d_key, d_value], 1)
    else:
        late_proj = jnp.concatenate([d_key, d_value], 1)
        early_sum = weight_grad(d_query_a)
    early_sum, input_part = lax.optimization_barrier((early_sum, input_part))
    input_cols = input_part.shape[1] // head_groups
    input_split = lax.all_to_all(
        input_part.astype(jnp.bfloat16).reshape(num_rows, head_groups, input_cols),
        "head", 1, 1, tiled=False,
    )
    grad_input = jnp.sum(input_split.astype(jnp.float32), axis=1).astype(jnp.bfloat16)
    late_sum = weight_grad(late_proj)
    query_w = jnp.concatenate([early_sum, late_sum[:, : query_cols - first_cols]], 1)
    rest = late_sum[:, query_cols - first_cols :]
    return (attended, grad_input, query_w, rest[:, :128], rest[:, 128:])


def solution(mesh):
    placed = (
        P(("dp", "ctx"), None),
        P(("dp", "ctx"), "head"),
        P(("dp", "ctx"), "head"),
        P(("dp", "ctx"), "head"),
        P("dp", None),
        P(("dp", "ctx"), "head"),
    )
    return jax.shard_map(
        local,
        mesh=mesh,
        in_specs=placed,
        out_specs=(
            P(("dp", "ctx"), "head"),
            P(("dp", "ctx"), "head"),
            P(("dp", "ctx"), "head"),
            P(("dp", "ctx"), "head"),
            P(("dp", "ctx"), "head"),
        ),
        check_vma=False,
    )
```

```python
import jax
import jax.numpy as jnp
from jax import lax
from jax.sharding import PartitionSpec as P

scale_factor = 128.0 ** (-0.5)
neg_large = -1e30


def rope_tables(positions):
    inverse = jnp.power(500000.0, -jnp.arange(64, dtype=jnp.float32) / 64.0)
    angles = positions.astype(jnp.float32)[:, None] * inverse[None, :]
    return (jnp.cos(angles)[:, None, :], jnp.sin(angles)[:, None, :])


def rotate(entries, cosine, sine_table):
    first_half = entries[..., :64]
    second_half = entries[..., 64:]
    return jnp.concatenate(
        [
            first_half * cosine - second_half * sine_table,
            second_half * cosine + first_half * sine_table,
        ],
        -1,
    )


def unrotate(entries, cosine, sine_table):
    first_half = entries[..., :64]
    second_half = entries[..., 64:]
    return jnp.concatenate(
        [
            first_half * cosine + second_half * sine_table,
            second_half * cosine - first_half * sine_table,
        ],
        -1,
    )


def segment_ids(length_row, positions):
    ends = jnp.cumsum(length_row)
    return jnp.sum((positions[:, None] >= ends[None, :]).astype(jnp.int32), 1)


def block_scores(query_blk, key_blk, query_pos, key_pos, query_seg, key_seg):
    scores = (
        jnp.einsum("rhd,kd->hrk", query_blk, key_blk, preferred_element_type=jnp.float32)
        * scale_factor
    )
    allowed = (key_pos[None, :] <= query_pos[:, None]) & (key_seg[None, :] == query_seg[:, None])
    return (scores, allowed[None])


def grad_block(
    query_blk,
    dout_blk,
    total_blk,
    delta_blk,
    key_blk,
    value_blk,
    query_pos,
    key_pos,
    query_seg,
    key_seg,
):
    scores, allowed = block_scores(query_blk, key_blk, query_pos, key_pos, query_seg, key_seg)
    prob_rows = jnp.where(
        allowed, jnp.exp(jnp.where(allowed, scores - total_blk[..., None], neg_large)), 0.0
    )
    prob_b = prob_rows.astype(jnp.bfloat16)
    d_prob = jnp.einsum("rhd,kd->hrk", dout_blk, value_blk, preferred_element_type=jnp.float32)
    d_score = (scale_factor * prob_rows * (d_prob - delta_blk[..., None])).astype(jnp.bfloat16)
    return (prob_b, d_score)


def attend_whole(query_rows, key_all, value_all, dout_rows, positions, all_pos, seg_own, seg_all):
    scores, allowed = block_scores(query_rows, key_all, positions, all_pos, seg_own, seg_all)
    masked = jnp.where(allowed, scores, neg_large)
    top_score = jnp.max(masked, -1)
    total = jnp.sum(jnp.where(allowed, jnp.exp(masked - top_score[..., None]), 0.0), -1)
    log_total = top_score + jnp.log(total)
    prob_rows = jnp.where(
        allowed, jnp.exp(jnp.where(allowed, scores - log_total[..., None], neg_large)), 0.0
    )
    prob_b = prob_rows.astype(jnp.bfloat16)
    out_rows = jnp.einsum(
        "hrk,kd->rhd", prob_b, value_all, preferred_element_type=jnp.float32
    ).astype(jnp.bfloat16)
    delta_rows = jnp.einsum("rhd,rhd->hr", dout_rows, out_rows, preferred_element_type=jnp.float32)
    d_prob = jnp.einsum("rhd,kd->hrk", dout_rows, value_all, preferred_element_type=jnp.float32)
    d_score = (scale_factor * prob_rows * (d_prob - delta_rows[..., None])).astype(jnp.bfloat16)
    grad_q = jnp.einsum("hrk,kd->rhd", d_score, key_all, preferred_element_type=jnp.float32)
    part_k = jnp.einsum("hrk,rhd->kd", d_score, query_rows, preferred_element_type=jnp.float32)
    part_v = jnp.einsum("hrk,rhd->kd", prob_b, dout_rows, preferred_element_type=jnp.float32)
    return out_rows, grad_q, part_k, part_v


def attend_blocked(query_rows, key_all, value_all, dout_rows, positions, all_pos, seg_own, seg_all, kblock):
    num_rows, head_count = query_rows.shape[0], query_rows.shape[1]
    seq_len = key_all.shape[0]
    causal_limit = (positions[-1] + kblock) // kblock
    key_first = jnp.int32(0)

    def take_block(block_index):
        first_row = block_index * kblock
        return (
            lax.dynamic_slice_in_dim(key_all, first_row, kblock, 0),
            lax.dynamic_slice_in_dim(value_all, first_row, kblock, 0),
            lax.dynamic_slice_in_dim(all_pos, first_row, kblock, 0),
            lax.dynamic_slice_in_dim(seg_all, first_row, kblock, 0),
        )

    def stats_step(block_index, carried):
        run_max, run_sum = carried
        key_blk, value_blk, key_pos, key_seg = take_block(block_index)
        scores, allowed = block_scores(query_rows, key_blk, positions, key_pos, seg_own, key_seg)
        masked = jnp.where(allowed, scores, neg_large)
        new_max = jnp.maximum(run_max, jnp.max(masked, -1))
        terms = jnp.where(allowed, jnp.exp(masked - new_max[..., None]), 0.0)
        return (new_max, run_sum * jnp.exp(run_max - new_max) + jnp.sum(terms, -1))

    start_stats = (
        jnp.full((head_count, num_rows), neg_large, jnp.float32),
        jnp.zeros((head_count, num_rows), jnp.float32),
    )
    run_max, run_sum = lax.fori_loop(key_first, causal_limit, stats_step, start_stats)
    log_total = run_max + jnp.log(run_sum)

    def output_step(block_index, carried):
        key_blk, value_blk, key_pos, key_seg = take_block(block_index)
        scores, allowed = block_scores(query_rows, key_blk, positions, key_pos, seg_own, key_seg)
        prob_b = jnp.where(
            allowed, jnp.exp(jnp.where(allowed, scores - log_total[..., None], neg_large)), 0.0
        ).astype(jnp.bfloat16)
        return carried + jnp.einsum(
            "hrk,kd->rhd", prob_b, value_blk, preferred_element_type=jnp.float32
        )

    out_sum = lax.fori_loop(
        key_first, causal_limit, output_step, jnp.zeros((num_rows, head_count, 128), jnp.float32)
    )
    out_rows = out_sum.astype(jnp.bfloat16)
    delta_rows = jnp.einsum("rhd,rhd->hr", dout_rows, out_rows, preferred_element_type=jnp.float32)

    def sums_step(block_index, carried):
        grad_q, part_k, part_v = carried
        first_row = block_index * kblock
        key_blk, value_blk, key_pos, key_seg = take_block(block_index)
        prob_b, d_score = grad_block(
            query_rows, dout_rows, log_total, delta_rows, key_blk, value_blk,
            positions, key_pos, seg_own, key_seg,
        )
        grad_q = grad_q + jnp.einsum(
            "hrk,kd->rhd", d_score, key_blk, preferred_element_type=jnp.float32
        )
        block_k = jnp.einsum("hrk,rhd->kd", d_score, query_rows, preferred_element_type=jnp.float32)
        block_v = jnp.einsum("hrk,rhd->kd", prob_b, dout_rows, preferred_element_type=jnp.float32)
        part_k = lax.dynamic_update_slice_in_dim(
            part_k, lax.dynamic_slice_in_dim(part_k, first_row, kblock, 0) + block_k, first_row, 0
        )
        part_v = lax.dynamic_update_slice_in_dim(
            part_v, lax.dynamic_slice_in_dim(part_v, first_row, kblock, 0) + block_v, first_row, 0
        )
        return (grad_q, part_k, part_v)

    start_sums = (
        jnp.zeros((num_rows, head_count, 128), jnp.float32),
        jnp.zeros((seq_len, 128), jnp.float32),
        jnp.zeros((seq_len, 128), jnp.float32),
    )
    grad_q, part_k, part_v = lax.fori_loop(key_first, causal_limit, sums_step, start_sums)
    return out_rows, grad_q, part_k, part_v


def attend(query_rows, key_all, value_all, dout_rows, positions, all_pos, seg_own, seg_all):
    head_count, num_rows, seq_len = query_rows.shape[1], query_rows.shape[0], key_all.shape[0]
    operands = (query_rows, key_all, value_all, dout_rows, positions, all_pos, seg_own, seg_all)
    if head_count * num_rows * seq_len <= (1 << 22):
        return attend_whole(*operands)
    kblock = seq_len
    while head_count * num_rows * kblock > (1 << 21) and kblock % 256 == 0:
        kblock //= 2
    return attend_blocked(*operands, kblock)


def local(hidden_in, w_query, w_key, w_value, lengths, attn_grad):
    num_rows = hidden_in.shape[0]
    head_count = w_query.shape[1] // 128
    first_heads = head_count // 2 if head_count % 2 == 0 else head_count
    first_cols = first_heads * 128
    query_cols = head_count * 128
    start_row = lax.axis_index("ctx") * num_rows
    seq_len = num_rows * lax.axis_size("ctx")
    positions = start_row + jnp.arange(num_rows, dtype=jnp.int32)
    all_pos = jnp.arange(seq_len, dtype=jnp.int32)
    seg_all = segment_ids(lengths[0], all_pos)
    seg_own = lax.dynamic_slice_in_dim(seg_all, start_row, num_rows)
    cosine, sine_table = rope_tables(positions)
    rows_axes = ("dp", "ctx")
    group_count = lax.axis_size(rows_axes)
    head_groups = lax.axis_size("head")
    local_a = jnp.concatenate([w_query[:, :first_cols], w_key, w_value], 1)
    full_a = lax.all_gather(local_a, rows_axes, axis=0, tiled=True)
    split_rows = num_rows % head_groups == 0
    dp_count, ctx_count = lax.axis_size("dp"), lax.axis_size("ctx")
    ctx_index = lax.axis_index("ctx")
    if split_rows:
        quarter = num_rows // head_groups
        own_rows = lax.dynamic_slice_in_dim(hidden_in, lax.axis_index("head") * quarter, quarter, 0)
        own_rows, full_a = lax.optimization_barrier((own_rows, full_a))
        cols_part = lax.all_to_all(own_rows, "dp", 1, 0, tiled=True)
    else:
        cols_part = lax.all_to_all(hidden_in, "dp", 1, 0, tiled=True)
    full_a, w_query = lax.optimization_barrier((full_a, w_query))
    hidden_cols = cols_part
    if split_rows:
        spread = jnp.broadcast_to(cols_part[None], (head_groups,) + cols_part.shape)
        cols_all = lax.all_to_all(spread, "head", 0, 0, tiled=False)
        hidden_cols = (
            cols_all.reshape(head_groups, dp_count, quarter, -1)
            .transpose(1, 0, 2, 3)
            .reshape(dp_count * num_rows, -1)
        )
    weight_rows = w_query.shape[0]

    def weight_grad(d_rows, gathered=None):
        if gathered is None:
            gathered = lax.all_gather(d_rows, "dp", axis=0, tiled=True)
        partial = lax.dot_general(
            hidden_cols, gathered, (((0,), (0,)), ((), ())), preferred_element_type=jnp.float32
        )
        if ctx_count == 2:
            own_part = lax.dynamic_slice_in_dim(partial, ctx_index * weight_rows, weight_rows, 0)
            away_part = lax.dynamic_slice_in_dim(
                partial, (1 - ctx_index) * weight_rows, weight_rows, 0
            )
            sent = lax.ppermute(away_part.astype(jnp.bfloat16), "ctx", [(0, 1), (1, 0)])
            return own_part + sent.astype(jnp.float32)
        return lax.psum_scatter(partial, "ctx", scatter_dimension=0, tiled=True)

    proj_a = jnp.dot(hidden_in, full_a, preferred_element_type=jnp.float32)
    query_a = rotate(
        proj_a[:, :first_cols].reshape(num_rows, first_heads, 128), cosine, sine_table
    ).astype(jnp.bfloat16)
    key_rows = rotate(
        proj_a[:, first_cols : first_cols + 128].reshape(num_rows, 1, 128), cosine, sine_table
    )[:, 0, :].astype(jnp.bfloat16)
    value_rows = proj_a[:, first_cols + 128 :].astype(jnp.bfloat16)
    kv_rows = jnp.concatenate([key_rows, value_rows], 1)
    if ctx_count == 2:
        kv_other = lax.ppermute(kv_rows, "ctx", [(0, 1), (1, 0)])
        kv_all = jnp.where(
            ctx_index == 0,
            jnp.concatenate([kv_rows, kv_other], 0),
            jnp.concatenate([kv_other, kv_rows], 0),
        )
    else:
        kv_all = lax.all_gather(kv_rows, "ctx", axis=0, tiled=True)
    key_all, value_all = kv_all[:, :128], kv_all[:, 128:]
    dout_rows = attn_grad.reshape(num_rows, head_count, 128)
    shared = (key_all, value_all)
    masks = (positions, all_pos, seg_own, seg_all)
    out_a, grad_qa, part_k, part_v = attend(query_a, *shared, dout_rows[:, :first_heads], *masks)
    d_query_a = unrotate(grad_qa, cosine, sine_table).astype(jnp.bfloat16).reshape(num_rows, -1)
    out_parts, d_query_parts = [out_a], [d_query_a]
    if first_heads < head_count:
        w_rest = w_query[:, first_cols:]
        full_b = lax.all_gather(w_rest, rows_axes, axis=0, tiled=True)
        d_query_a, full_b = lax.optimization_barrier((d_query_a, full_b))
        early_all = lax.all_gather(d_query_a, "dp", axis=0, tiled=True)
        proj_b = jnp.dot(hidden_in, full_b, preferred_element_type=jnp.float32)
        query_b = rotate(
            proj_b.reshape(num_rows, head_count - first_heads, 128), cosine, sine_table
        ).astype(jnp.bfloat16)
        out_b, grad_qb, part_kb, part_vb = attend(
            query_b, *shared, dout_rows[:, first_heads:], *masks
        )
        early_all, grad_qb = lax.optimization_barrier((early_all, grad_qb))
        early_sum = weight_grad(d_query_a, early_all)
        d_query_b = unrotate(grad_qb, cosine, sine_table).astype(jnp.bfloat16).reshape(num_rows, -1)
        part_k, part_v = part_k + part_kb, part_v + part_vb
        out_parts.append(out_b)
    attended = jnp.concatenate(out_parts, 1).reshape(num_rows, query_cols)
    parts_kv = jnp.concatenate([part_k, part_v], 1)
    if ctx_count == 2:
        own_part = lax.dynamic_slice_in_dim(parts_kv, ctx_index * num_rows, num_rows, 0)
        away_part = lax.dynamic_slice_in_dim(parts_kv, (1 - ctx_index) * num_rows, num_rows, 0)
        grad_kv = own_part + lax.ppermute(away_part, "ctx", [(0, 1), (1, 0)])
    else:
        grad_kv = lax.psum_scatter(parts_kv, "ctx", scatter_dimension=0, tiled=True)
    grad_k, grad_v = grad_kv[:, :128], grad_kv[:, 128:]
    d_key = unrotate(grad_k[:, None, :], cosine, sine_table)[:, 0, :].astype(jnp.bfloat16)
    d_value = grad_v.astype(jnp.bfloat16)
    d_proj_a = jnp.concatenate([d_query_a, d_key, d_value], 1)
    input_part = lax.dot_general(
        d_proj_a, full_a, (((1,), (1,)), ((), ())), preferred_element_type=jnp.float32
    )
    if first_heads < head_count:
        input_part = input_part + lax.dot_general(
            d_query_b, full_b, (((1,), (1,)), ((), ())), preferred_element_type=jnp.float32
        )
        late_proj = jnp.concatenate([d_query_b, d_key, d_value], 1)
    else:
        late_proj = jnp.concatenate([d_key, d_value], 1)
        early_sum = weight_grad(d_query_a)
    input_cols = input_part.shape[1] // head_groups
    input_split = lax.all_to_all(
        input_part.astype(jnp.bfloat16).reshape(num_rows, head_groups, input_cols),
        "head", 1, 1, tiled=False,
    )
    grad_input = jnp.sum(input_split.astype(jnp.float32), axis=1).astype(jnp.bfloat16)
    late_all = lax.all_gather(late_proj, "dp", axis=0, tiled=True)
    early_sum, late_all = lax.optimization_barrier((early_sum, late_all))
    late_sum = weight_grad(late_proj, late_all)
    query_w = jnp.concatenate([early_sum, late_sum[:, : query_cols - first_cols]], 1)
    rest = late_sum[:, query_cols - first_cols :]
    return (attended, grad_input, query_w, rest[:, :128], rest[:, 128:])


def solution(mesh):
    placed = (
        P(("dp", "ctx"), None),
        P(("dp", "ctx"), "head"),
        P(("dp", "ctx"), "head"),
        P(("dp", "ctx"), "head"),
        P("dp", None),
        P(("dp", "ctx"), "head"),
    )
    return jax.shard_map(
        local,
        mesh=mesh,
        in_specs=placed,
        out_specs=(
            P(("dp", "ctx"), "head"),
            P(("dp", "ctx"), "head"),
            P(("dp", "ctx"), "head"),
            P(("dp", "ctx"), "head"),
            P(("dp", "ctx"), "head"),
        ),
        check_vma=False,
    )
```

```python
import jax
import jax.numpy as jnp
from jax import lax
from jax.sharding import PartitionSpec as P

scale_factor = 128.0 ** (-0.5)
neg_large = -1e30


def rope_tables(positions):
    inverse = jnp.power(500000.0, -jnp.arange(64, dtype=jnp.float32) / 64.0)
    angles = positions.astype(jnp.float32)[:, None] * inverse[None, :]
    return (jnp.cos(angles)[:, None, :], jnp.sin(angles)[:, None, :])


def rotate(entries, cosine, sine_table):
    first_half = entries[..., :64]
    second_half = entries[..., 64:]
    return jnp.concatenate(
        [
            first_half * cosine - second_half * sine_table,
            second_half * cosine + first_half * sine_table,
        ],
        -1,
    )


def unrotate(entries, cosine, sine_table):
    first_half = entries[..., :64]
    second_half = entries[..., 64:]
    return jnp.concatenate(
        [
            first_half * cosine + second_half * sine_table,
            second_half * cosine - first_half * sine_table,
        ],
        -1,
    )


def segment_ids(length_row, positions):
    ends = jnp.cumsum(length_row)
    return jnp.sum((positions[:, None] >= ends[None, :]).astype(jnp.int32), 1)


def block_scores(query_blk, key_blk, query_pos, key_pos, query_seg, key_seg):
    scores = (
        jnp.einsum("rhd,kd->hrk", query_blk, key_blk, preferred_element_type=jnp.float32)
        * scale_factor
    )
    allowed = (key_pos[None, :] <= query_pos[:, None]) & (key_seg[None, :] == query_seg[:, None])
    return (scores, allowed[None])


def grad_block(
    query_blk,
    dout_blk,
    total_blk,
    delta_blk,
    key_blk,
    value_blk,
    query_pos,
    key_pos,
    query_seg,
    key_seg,
):
    scores, allowed = block_scores(query_blk, key_blk, query_pos, key_pos, query_seg, key_seg)
    prob_rows = jnp.where(
        allowed, jnp.exp(jnp.where(allowed, scores - total_blk[..., None], neg_large)), 0.0
    )
    prob_b = prob_rows.astype(jnp.bfloat16)
    d_prob = jnp.einsum("rhd,kd->hrk", dout_blk, value_blk, preferred_element_type=jnp.float32)
    d_score = (scale_factor * prob_rows * (d_prob - delta_blk[..., None])).astype(jnp.bfloat16)
    return (prob_b, d_score)


def attend_whole(query_rows, key_all, value_all, dout_rows, positions, all_pos, seg_own, seg_all):
    scores, allowed = block_scores(query_rows, key_all, positions, all_pos, seg_own, seg_all)
    masked = jnp.where(allowed, scores, neg_large)
    top_score = jnp.max(masked, -1)
    total = jnp.sum(jnp.where(allowed, jnp.exp(masked - top_score[..., None]), 0.0), -1)
    log_total = top_score + jnp.log(total)
    prob_rows = jnp.where(
        allowed, jnp.exp(jnp.where(allowed, scores - log_total[..., None], neg_large)), 0.0
    )
    prob_b = prob_rows.astype(jnp.bfloat16)
    out_rows = jnp.einsum(
        "hrk,kd->rhd", prob_b, value_all, preferred_element_type=jnp.float32
    ).astype(jnp.bfloat16)
    delta_rows = jnp.einsum("rhd,rhd->hr", dout_rows, out_rows, preferred_element_type=jnp.float32)
    d_prob = jnp.einsum("rhd,kd->hrk", dout_rows, value_all, preferred_element_type=jnp.float32)
    d_score = (scale_factor * prob_rows * (d_prob - delta_rows[..., None])).astype(jnp.bfloat16)
    grad_q = jnp.einsum("hrk,kd->rhd", d_score, key_all, preferred_element_type=jnp.float32)
    part_k = jnp.einsum("hrk,rhd->kd", d_score, query_rows, preferred_element_type=jnp.float32)
    part_v = jnp.einsum("hrk,rhd->kd", prob_b, dout_rows, preferred_element_type=jnp.float32)
    return out_rows, grad_q, part_k, part_v


def attend_blocked(query_rows, key_all, value_all, dout_rows, positions, all_pos, seg_own, seg_all, kblock):
    num_rows, head_count = query_rows.shape[0], query_rows.shape[1]
    seq_len = key_all.shape[0]
    causal_limit = (positions[-1] + kblock) // kblock
    key_first = jnp.int32(0)

    def take_block(block_index):
        first_row = block_index * kblock
        return (
            lax.dynamic_slice_in_dim(key_all, first_row, kblock, 0),
            lax.dynamic_slice_in_dim(value_all, first_row, kblock, 0),
            lax.dynamic_slice_in_dim(all_pos, first_row, kblock, 0),
            lax.dynamic_slice_in_dim(seg_all, first_row, kblock, 0),
        )

    def stats_step(block_index, carried):
        run_max, run_sum = carried
        key_blk, value_blk, key_pos, key_seg = take_block(block_index)
        scores, allowed = block_scores(query_rows, key_blk, positions, key_pos, seg_own, key_seg)
        masked = jnp.where(allowed, scores, neg_large)
        new_max = jnp.maximum(run_max, jnp.max(masked, -1))
        terms = jnp.where(allowed, jnp.exp(masked - new_max[..., None]), 0.0)
        return (new_max, run_sum * jnp.exp(run_max - new_max) + jnp.sum(terms, -1))

    start_stats = (
        jnp.full((head_count, num_rows), neg_large, jnp.float32),
        jnp.zeros((head_count, num_rows), jnp.float32),
    )
    run_max, run_sum = lax.fori_loop(key_first, causal_limit, stats_step, start_stats)
    log_total = run_max + jnp.log(run_sum)

    def output_step(block_index, carried):
        key_blk, value_blk, key_pos, key_seg = take_block(block_index)
        scores, allowed = block_scores(query_rows, key_blk, positions, key_pos, seg_own, key_seg)
        prob_b = jnp.where(
            allowed, jnp.exp(jnp.where(allowed, scores - log_total[..., None], neg_large)), 0.0
        ).astype(jnp.bfloat16)
        return carried + jnp.einsum(
            "hrk,kd->rhd", prob_b, value_blk, preferred_element_type=jnp.float32
        )

    out_sum = lax.fori_loop(
        key_first, causal_limit, output_step, jnp.zeros((num_rows, head_count, 128), jnp.float32)
    )
    out_rows = out_sum.astype(jnp.bfloat16)
    delta_rows = jnp.einsum("rhd,rhd->hr", dout_rows, out_rows, preferred_element_type=jnp.float32)

    def sums_step(block_index, carried):
        grad_q, part_k, part_v = carried
        first_row = block_index * kblock
        key_blk, value_blk, key_pos, key_seg = take_block(block_index)
        prob_b, d_score = grad_block(
            query_rows, dout_rows, log_total, delta_rows, key_blk, value_blk,
            positions, key_pos, seg_own, key_seg,
        )
        grad_q = grad_q + jnp.einsum(
            "hrk,kd->rhd", d_score, key_blk, preferred_element_type=jnp.float32
        )
        block_k = jnp.einsum("hrk,rhd->kd", d_score, query_rows, preferred_element_type=jnp.float32)
        block_v = jnp.einsum("hrk,rhd->kd", prob_b, dout_rows, preferred_element_type=jnp.float32)
        part_k = lax.dynamic_update_slice_in_dim(
            part_k, lax.dynamic_slice_in_dim(part_k, first_row, kblock, 0) + block_k, first_row, 0
        )
        part_v = lax.dynamic_update_slice_in_dim(
            part_v, lax.dynamic_slice_in_dim(part_v, first_row, kblock, 0) + block_v, first_row, 0
        )
        return (grad_q, part_k, part_v)

    start_sums = (
        jnp.zeros((num_rows, head_count, 128), jnp.float32),
        jnp.zeros((seq_len, 128), jnp.float32),
        jnp.zeros((seq_len, 128), jnp.float32),
    )
    grad_q, part_k, part_v = lax.fori_loop(key_first, causal_limit, sums_step, start_sums)
    return out_rows, grad_q, part_k, part_v


def attend(query_rows, key_all, value_all, dout_rows, positions, all_pos, seg_own, seg_all):
    head_count, num_rows, seq_len = query_rows.shape[1], query_rows.shape[0], key_all.shape[0]
    operands = (query_rows, key_all, value_all, dout_rows, positions, all_pos, seg_own, seg_all)
    if head_count * num_rows * seq_len <= (1 << 22):
        return attend_whole(*operands)
    kblock = seq_len
    while head_count * num_rows * kblock > (1 << 21) and kblock % 256 == 0:
        kblock //= 2
    return attend_blocked(*operands, kblock)


def local(hidden_in, w_query, w_key, w_value, lengths, attn_grad):
    num_rows = hidden_in.shape[0]
    head_count = w_query.shape[1] // 128
    first_heads = (head_count * 5) // 8 if head_count >= 2 else head_count
    first_cols = first_heads * 128
    query_cols = head_count * 128
    start_row = lax.axis_index("ctx") * num_rows
    seq_len = num_rows * lax.axis_size("ctx")
    positions = start_row + jnp.arange(num_rows, dtype=jnp.int32)
    all_pos = jnp.arange(seq_len, dtype=jnp.int32)
    seg_all = segment_ids(lengths[0], all_pos)
    seg_own = lax.dynamic_slice_in_dim(seg_all, start_row, num_rows)
    cosine, sine_table = rope_tables(positions)
    rows_axes = ("dp", "ctx")
    group_count = lax.axis_size(rows_axes)
    head_groups = lax.axis_size("head")
    local_a = jnp.concatenate([w_query[:, :first_cols], w_key, w_value], 1)
    full_a = lax.all_gather(local_a, rows_axes, axis=0, tiled=True)
    split_rows = num_rows % head_groups == 0
    dp_count, ctx_count = lax.axis_size("dp"), lax.axis_size("ctx")
    ctx_index = lax.axis_index("ctx")
    if split_rows:
        quarter = num_rows // head_groups
        own_rows = lax.dynamic_slice_in_dim(hidden_in, lax.axis_index("head") * quarter, quarter, 0)
        own_rows, full_a = lax.optimization_barrier((own_rows, full_a))
        cols_part = lax.all_to_all(own_rows, "dp", 1, 0, tiled=True)
    else:
        cols_part = lax.all_to_all(hidden_in, "dp", 1, 0, tiled=True)
    full_a, w_query = lax.optimization_barrier((full_a, w_query))
    hidden_cols = cols_part
    if split_rows:
        spread = jnp.broadcast_to(cols_part[None], (head_groups,) + cols_part.shape)
        cols_all = lax.all_to_all(spread, "head", 0, 0, tiled=False)
        hidden_cols = (
            cols_all.reshape(head_groups, dp_count, quarter, -1)
            .transpose(1, 0, 2, 3)
            .reshape(dp_count * num_rows, -1)
        )
    weight_rows = w_query.shape[0]

    def weight_grad(d_rows, gathered=None):
        if gathered is None:
            gathered = lax.all_gather(d_rows, "dp", axis=0, tiled=True)
        partial = lax.dot_general(
            hidden_cols, gathered, (((0,), (0,)), ((), ())), preferred_element_type=jnp.float32
        )
        if ctx_count == 2:
            own_part = lax.dynamic_slice_in_dim(partial, ctx_index * weight_rows, weight_rows, 0)
            away_part = lax.dynamic_slice_in_dim(
                partial, (1 - ctx_index) * weight_rows, weight_rows, 0
            )
            sent = lax.ppermute(away_part.astype(jnp.bfloat16), "ctx", [(0, 1), (1, 0)])
            return own_part + sent.astype(jnp.float32)
        return lax.psum_scatter(partial, "ctx", scatter_dimension=0, tiled=True)

    proj_a = jnp.dot(hidden_in, full_a, preferred_element_type=jnp.float32)
    query_a = rotate(
        proj_a[:, :first_cols].reshape(num_rows, first_heads, 128), cosine, sine_table
    ).astype(jnp.bfloat16)
    key_rows = rotate(
        proj_a[:, first_cols : first_cols + 128].reshape(num_rows, 1, 128), cosine, sine_table
    )[:, 0, :].astype(jnp.bfloat16)
    value_rows = proj_a[:, first_cols + 128 :].astype(jnp.bfloat16)
    kv_rows = jnp.concatenate([key_rows, value_rows], 1)
    if ctx_count == 2:
        kv_other = lax.ppermute(kv_rows, "ctx", [(0, 1), (1, 0)])
        kv_all = jnp.where(
            ctx_index == 0,
            jnp.concatenate([kv_rows, kv_other], 0),
            jnp.concatenate([kv_other, kv_rows], 0),
        )
    else:
        kv_all = lax.all_gather(kv_rows, "ctx", axis=0, tiled=True)
    key_all, value_all = kv_all[:, :128], kv_all[:, 128:]
    dout_rows = attn_grad.reshape(num_rows, head_count, 128)
    shared = (key_all, value_all)
    masks = (positions, all_pos, seg_own, seg_all)
    out_a, grad_qa, part_k, part_v = attend(query_a, *shared, dout_rows[:, :first_heads], *masks)
    d_query_a = unrotate(grad_qa, cosine, sine_table).astype(jnp.bfloat16).reshape(num_rows, -1)
    out_parts, d_query_parts = [out_a], [d_query_a]
    if first_heads < head_count:
        w_rest = w_query[:, first_cols:]
        full_b = lax.all_gather(w_rest, rows_axes, axis=0, tiled=True)
        d_query_a, full_b = lax.optimization_barrier((d_query_a, full_b))
        early_all = lax.all_gather(d_query_a, "dp", axis=0, tiled=True)
        proj_b = jnp.dot(hidden_in, full_b, preferred_element_type=jnp.float32)
        query_b = rotate(
            proj_b.reshape(num_rows, head_count - first_heads, 128), cosine, sine_table
        ).astype(jnp.bfloat16)
        out_b, grad_qb, part_kb, part_vb = attend(
            query_b, *shared, dout_rows[:, first_heads:], *masks
        )
        early_all, grad_qb = lax.optimization_barrier((early_all, grad_qb))
        early_sum = weight_grad(d_query_a, early_all)
        d_query_b = unrotate(grad_qb, cosine, sine_table).astype(jnp.bfloat16).reshape(num_rows, -1)
        part_k, part_v = part_k + part_kb, part_v + part_vb
        out_parts.append(out_b)
    attended = jnp.concatenate(out_parts, 1).reshape(num_rows, query_cols)
    parts_kv = jnp.concatenate([part_k, part_v], 1)
    if ctx_count == 2:
        own_part = lax.dynamic_slice_in_dim(parts_kv, ctx_index * num_rows, num_rows, 0)
        away_part = lax.dynamic_slice_in_dim(parts_kv, (1 - ctx_index) * num_rows, num_rows, 0)
        grad_kv = own_part + lax.ppermute(away_part, "ctx", [(0, 1), (1, 0)])
    else:
        grad_kv = lax.psum_scatter(parts_kv, "ctx", scatter_dimension=0, tiled=True)
    grad_k, grad_v = grad_kv[:, :128], grad_kv[:, 128:]
    d_key = unrotate(grad_k[:, None, :], cosine, sine_table)[:, 0, :].astype(jnp.bfloat16)
    d_value = grad_v.astype(jnp.bfloat16)
    d_proj_a = jnp.concatenate([d_query_a, d_key, d_value], 1)
    input_part = lax.dot_general(
        d_proj_a, full_a, (((1,), (1,)), ((), ())), preferred_element_type=jnp.float32
    )
    if first_heads < head_count:
        input_part = input_part + lax.dot_general(
            d_query_b, full_b, (((1,), (1,)), ((), ())), preferred_element_type=jnp.float32
        )
        late_proj = jnp.concatenate([d_query_b, d_key, d_value], 1)
    else:
        late_proj = jnp.concatenate([d_key, d_value], 1)
        early_sum = weight_grad(d_query_a)
    early_sum, input_part = lax.optimization_barrier((early_sum, input_part))
    input_cols = input_part.shape[1] // head_groups
    input_split = lax.all_to_all(
        input_part.astype(jnp.bfloat16).reshape(num_rows, head_groups, input_cols),
        "head", 1, 1, tiled=False,
    )
    grad_input = jnp.sum(input_split.astype(jnp.float32), axis=1).astype(jnp.bfloat16)
    late_sum = weight_grad(late_proj)
    query_w = jnp.concatenate([early_sum, late_sum[:, : query_cols - first_cols]], 1)
    rest = late_sum[:, query_cols - first_cols :]
    return (attended, grad_input, query_w, rest[:, :128], rest[:, 128:])


def solution(mesh):
    placed = (
        P(("dp", "ctx"), None),
        P(("dp", "ctx"), "head"),
        P(("dp", "ctx"), "head"),
        P(("dp", "ctx"), "head"),
        P("dp", None),
        P(("dp", "ctx"), "head"),
    )
    return jax.shard_map(
        local,
        mesh=mesh,
        in_specs=placed,
        out_specs=(
            P(("dp", "ctx"), "head"),
            P(("dp", "ctx"), "head"),
            P(("dp", "ctx"), "head"),
            P(("dp", "ctx"), "head"),
            P(("dp", "ctx"), "head"),
        ),
        check_vma=False,
    )
```

```python
import jax
import jax.numpy as jnp
from jax import lax
from jax.sharding import PartitionSpec as P

scale_factor = 128.0 ** (-0.5)
neg_large = -1e30


def rope_tables(positions):
    inverse = jnp.power(500000.0, -jnp.arange(64, dtype=jnp.float32) / 64.0)
    angles = positions.astype(jnp.float32)[:, None] * inverse[None, :]
    return (jnp.cos(angles)[:, None, :], jnp.sin(angles)[:, None, :])


def rotate(entries, cosine, sine_table):
    first_half = entries[..., :64]
    second_half = entries[..., 64:]
    return jnp.concatenate(
        [
            first_half * cosine - second_half * sine_table,
            second_half * cosine + first_half * sine_table,
        ],
        -1,
    )


def unrotate(entries, cosine, sine_table):
    first_half = entries[..., :64]
    second_half = entries[..., 64:]
    return jnp.concatenate(
        [
            first_half * cosine + second_half * sine_table,
            second_half * cosine - first_half * sine_table,
        ],
        -1,
    )


def segment_ids(length_row, positions):
    ends = jnp.cumsum(length_row)
    return jnp.sum((positions[:, None] >= ends[None, :]).astype(jnp.int32), 1)


def block_scores(query_blk, key_blk, query_pos, key_pos, query_seg, key_seg):
    scores = (
        jnp.einsum("rhd,kd->hrk", query_blk, key_blk, preferred_element_type=jnp.float32)
        * scale_factor
    )
    allowed = (key_pos[None, :] <= query_pos[:, None]) & (key_seg[None, :] == query_seg[:, None])
    return (scores, allowed[None])


def grad_block(
    query_blk,
    dout_blk,
    total_blk,
    delta_blk,
    key_blk,
    value_blk,
    query_pos,
    key_pos,
    query_seg,
    key_seg,
):
    scores, allowed = block_scores(query_blk, key_blk, query_pos, key_pos, query_seg, key_seg)
    prob_rows = jnp.where(
        allowed, jnp.exp(jnp.where(allowed, scores - total_blk[..., None], neg_large)), 0.0
    )
    prob_b = prob_rows.astype(jnp.bfloat16)
    d_prob = jnp.einsum("rhd,kd->hrk", dout_blk, value_blk, preferred_element_type=jnp.float32)
    d_score = (scale_factor * prob_rows * (d_prob - delta_blk[..., None])).astype(jnp.bfloat16)
    return (prob_b, d_score)


def attend_whole(query_rows, key_all, value_all, dout_rows, positions, all_pos, seg_own, seg_all):
    scores, allowed = block_scores(query_rows, key_all, positions, all_pos, seg_own, seg_all)
    masked = jnp.where(allowed, scores, neg_large)
    top_score = jnp.max(masked, -1)
    total = jnp.sum(jnp.where(allowed, jnp.exp(masked - top_score[..., None]), 0.0), -1)
    log_total = top_score + jnp.log(total)
    prob_rows = jnp.where(
        allowed, jnp.exp(jnp.where(allowed, scores - log_total[..., None], neg_large)), 0.0
    )
    prob_b = prob_rows.astype(jnp.bfloat16)
    out_rows = jnp.einsum(
        "hrk,kd->rhd", prob_b, value_all, preferred_element_type=jnp.float32
    ).astype(jnp.bfloat16)
    delta_rows = jnp.einsum("rhd,rhd->hr", dout_rows, out_rows, preferred_element_type=jnp.float32)
    d_prob = jnp.einsum("rhd,kd->hrk", dout_rows, value_all, preferred_element_type=jnp.float32)
    d_score = (scale_factor * prob_rows * (d_prob - delta_rows[..., None])).astype(jnp.bfloat16)
    grad_q = jnp.einsum("hrk,kd->rhd", d_score, key_all, preferred_element_type=jnp.float32)
    part_k = jnp.einsum("hrk,rhd->kd", d_score, query_rows, preferred_element_type=jnp.float32)
    part_v = jnp.einsum("hrk,rhd->kd", prob_b, dout_rows, preferred_element_type=jnp.float32)
    return out_rows, grad_q, part_k, part_v


def attend_blocked(query_rows, key_all, value_all, dout_rows, positions, all_pos, seg_own, seg_all, kblock):
    num_rows, head_count = query_rows.shape[0], query_rows.shape[1]
    seq_len = key_all.shape[0]
    causal_limit = (positions[-1] + kblock) // kblock
    key_first = jnp.int32(0)

    def take_block(block_index):
        first_row = block_index * kblock
        return (
            lax.dynamic_slice_in_dim(key_all, first_row, kblock, 0),
            lax.dynamic_slice_in_dim(value_all, first_row, kblock, 0),
            lax.dynamic_slice_in_dim(all_pos, first_row, kblock, 0),
            lax.dynamic_slice_in_dim(seg_all, first_row, kblock, 0),
        )

    def stats_step(block_index, carried):
        run_max, run_sum = carried
        key_blk, value_blk, key_pos, key_seg = take_block(block_index)
        scores, allowed = block_scores(query_rows, key_blk, positions, key_pos, seg_own, key_seg)
        masked = jnp.where(allowed, scores, neg_large)
        new_max = jnp.maximum(run_max, jnp.max(masked, -1))
        terms = jnp.where(allowed, jnp.exp(masked - new_max[..., None]), 0.0)
        return (new_max, run_sum * jnp.exp(run_max - new_max) + jnp.sum(terms, -1))

    start_stats = (
        jnp.full((head_count, num_rows), neg_large, jnp.float32),
        jnp.zeros((head_count, num_rows), jnp.float32),
    )
    run_max, run_sum = lax.fori_loop(key_first, causal_limit, stats_step, start_stats)
    log_total = run_max + jnp.log(run_sum)

    def output_step(block_index, carried):
        key_blk, value_blk, key_pos, key_seg = take_block(block_index)
        scores, allowed = block_scores(query_rows, key_blk, positions, key_pos, seg_own, key_seg)
        prob_b = jnp.where(
            allowed, jnp.exp(jnp.where(allowed, scores - log_total[..., None], neg_large)), 0.0
        ).astype(jnp.bfloat16)
        return carried + jnp.einsum(
            "hrk,kd->rhd", prob_b, value_blk, preferred_element_type=jnp.float32
        )

    out_sum = lax.fori_loop(
        key_first, causal_limit, output_step, jnp.zeros((num_rows, head_count, 128), jnp.float32)
    )
    out_rows = out_sum.astype(jnp.bfloat16)
    delta_rows = jnp.einsum("rhd,rhd->hr", dout_rows, out_rows, preferred_element_type=jnp.float32)

    def sums_step(block_index, carried):
        grad_q, part_k, part_v = carried
        first_row = block_index * kblock
        key_blk, value_blk, key_pos, key_seg = take_block(block_index)
        prob_b, d_score = grad_block(
            query_rows, dout_rows, log_total, delta_rows, key_blk, value_blk,
            positions, key_pos, seg_own, key_seg,
        )
        grad_q = grad_q + jnp.einsum(
            "hrk,kd->rhd", d_score, key_blk, preferred_element_type=jnp.float32
        )
        block_k = jnp.einsum("hrk,rhd->kd", d_score, query_rows, preferred_element_type=jnp.float32)
        block_v = jnp.einsum("hrk,rhd->kd", prob_b, dout_rows, preferred_element_type=jnp.float32)
        part_k = lax.dynamic_update_slice_in_dim(
            part_k, lax.dynamic_slice_in_dim(part_k, first_row, kblock, 0) + block_k, first_row, 0
        )
        part_v = lax.dynamic_update_slice_in_dim(
            part_v, lax.dynamic_slice_in_dim(part_v, first_row, kblock, 0) + block_v, first_row, 0
        )
        return (grad_q, part_k, part_v)

    start_sums = (
        jnp.zeros((num_rows, head_count, 128), jnp.float32),
        jnp.zeros((seq_len, 128), jnp.float32),
        jnp.zeros((seq_len, 128), jnp.float32),
    )
    grad_q, part_k, part_v = lax.fori_loop(key_first, causal_limit, sums_step, start_sums)
    return out_rows, grad_q, part_k, part_v


def attend(query_rows, key_all, value_all, dout_rows, positions, all_pos, seg_own, seg_all):
    head_count, num_rows, seq_len = query_rows.shape[1], query_rows.shape[0], key_all.shape[0]
    operands = (query_rows, key_all, value_all, dout_rows, positions, all_pos, seg_own, seg_all)
    if head_count * num_rows * seq_len <= (1 << 22):
        return attend_whole(*operands)
    kblock = seq_len
    while head_count * num_rows * kblock > (1 << 21) and kblock % 256 == 0:
        kblock //= 2
    return attend_blocked(*operands, kblock)


def local(hidden_in, w_query, w_key, w_value, lengths, attn_grad):
    num_rows = hidden_in.shape[0]
    head_count = w_query.shape[1] // 128
    first_heads = (head_count * 3) // 8 if head_count >= 3 else head_count
    first_cols = first_heads * 128
    query_cols = head_count * 128
    start_row = lax.axis_index("ctx") * num_rows
    seq_len = num_rows * lax.axis_size("ctx")
    positions = start_row + jnp.arange(num_rows, dtype=jnp.int32)
    all_pos = jnp.arange(seq_len, dtype=jnp.int32)
    seg_all = segment_ids(lengths[0], all_pos)
    seg_own = lax.dynamic_slice_in_dim(seg_all, start_row, num_rows)
    cosine, sine_table = rope_tables(positions)
    rows_axes = ("dp", "ctx")
    group_count = lax.axis_size(rows_axes)
    head_groups = lax.axis_size("head")
    local_a = jnp.concatenate([w_query[:, :first_cols], w_key, w_value], 1)
    full_a = lax.all_gather(local_a, rows_axes, axis=0, tiled=True)
    split_rows = num_rows % head_groups == 0
    dp_count, ctx_count = lax.axis_size("dp"), lax.axis_size("ctx")
    ctx_index = lax.axis_index("ctx")
    if split_rows:
        quarter = num_rows // head_groups
        own_rows = lax.dynamic_slice_in_dim(hidden_in, lax.axis_index("head") * quarter, quarter, 0)
        own_rows, full_a = lax.optimization_barrier((own_rows, full_a))
        cols_part = lax.all_to_all(own_rows, "dp", 1, 0, tiled=True)
    else:
        cols_part = lax.all_to_all(hidden_in, "dp", 1, 0, tiled=True)
    full_a, w_query = lax.optimization_barrier((full_a, w_query))
    hidden_cols = cols_part
    if split_rows:
        spread = jnp.broadcast_to(cols_part[None], (head_groups,) + cols_part.shape)
        cols_all = lax.all_to_all(spread, "head", 0, 0, tiled=False)
        hidden_cols = (
            cols_all.reshape(head_groups, dp_count, quarter, -1)
            .transpose(1, 0, 2, 3)
            .reshape(dp_count * num_rows, -1)
        )
    weight_rows = w_query.shape[0]

    def weight_grad(d_rows, gathered=None):
        if gathered is None:
            gathered = lax.all_gather(d_rows, "dp", axis=0, tiled=True)
        partial = lax.dot_general(
            hidden_cols, gathered, (((0,), (0,)), ((), ())), preferred_element_type=jnp.float32
        )
        if ctx_count == 2:
            own_part = lax.dynamic_slice_in_dim(partial, ctx_index * weight_rows, weight_rows, 0)
            away_part = lax.dynamic_slice_in_dim(
                partial, (1 - ctx_index) * weight_rows, weight_rows, 0
            )
            sent = lax.ppermute(away_part.astype(jnp.bfloat16), "ctx", [(0, 1), (1, 0)])
            return own_part + sent.astype(jnp.float32)
        return lax.psum_scatter(partial, "ctx", scatter_dimension=0, tiled=True)

    proj_a = jnp.dot(hidden_in, full_a, preferred_element_type=jnp.float32)
    query_a = rotate(
        proj_a[:, :first_cols].reshape(num_rows, first_heads, 128), cosine, sine_table
    ).astype(jnp.bfloat16)
    key_rows = rotate(
        proj_a[:, first_cols : first_cols + 128].reshape(num_rows, 1, 128), cosine, sine_table
    )[:, 0, :].astype(jnp.bfloat16)
    value_rows = proj_a[:, first_cols + 128 :].astype(jnp.bfloat16)
    kv_rows = jnp.concatenate([key_rows, value_rows], 1)
    if ctx_count == 2:
        kv_other = lax.ppermute(kv_rows, "ctx", [(0, 1), (1, 0)])
        kv_all = jnp.where(
            ctx_index == 0,
            jnp.concatenate([kv_rows, kv_other], 0),
            jnp.concatenate([kv_other, kv_rows], 0),
        )
    else:
        kv_all = lax.all_gather(kv_rows, "ctx", axis=0, tiled=True)
    key_all, value_all = kv_all[:, :128], kv_all[:, 128:]
    dout_rows = attn_grad.reshape(num_rows, head_count, 128)
    shared = (key_all, value_all)
    masks = (positions, all_pos, seg_own, seg_all)
    out_a, grad_qa, part_k, part_v = attend(query_a, *shared, dout_rows[:, :first_heads], *masks)
    d_query_a = unrotate(grad_qa, cosine, sine_table).astype(jnp.bfloat16).reshape(num_rows, -1)
    out_parts, d_query_parts = [out_a], [d_query_a]
    if first_heads < head_count:
        w_rest = w_query[:, first_cols:]
        full_b = lax.all_gather(w_rest, rows_axes, axis=0, tiled=True)
        d_query_a, full_b = lax.optimization_barrier((d_query_a, full_b))
        early_all = lax.all_gather(d_query_a, "dp", axis=0, tiled=True)
        proj_b = jnp.dot(hidden_in, full_b, preferred_element_type=jnp.float32)
        query_b = rotate(
            proj_b.reshape(num_rows, head_count - first_heads, 128), cosine, sine_table
        ).astype(jnp.bfloat16)
        out_b, grad_qb, part_kb, part_vb = attend(
            query_b, *shared, dout_rows[:, first_heads:], *masks
        )
        early_all, grad_qb = lax.optimization_barrier((early_all, grad_qb))
        early_sum = weight_grad(d_query_a, early_all)
        d_query_b = unrotate(grad_qb, cosine, sine_table).astype(jnp.bfloat16).reshape(num_rows, -1)
        part_k, part_v = part_k + part_kb, part_v + part_vb
        out_parts.append(out_b)
    attended = jnp.concatenate(out_parts, 1).reshape(num_rows, query_cols)
    parts_kv = jnp.concatenate([part_k, part_v], 1)
    if ctx_count == 2:
        own_part = lax.dynamic_slice_in_dim(parts_kv, ctx_index * num_rows, num_rows, 0)
        away_part = lax.dynamic_slice_in_dim(parts_kv, (1 - ctx_index) * num_rows, num_rows, 0)
        grad_kv = own_part + lax.ppermute(away_part, "ctx", [(0, 1), (1, 0)])
    else:
        grad_kv = lax.psum_scatter(parts_kv, "ctx", scatter_dimension=0, tiled=True)
    grad_k, grad_v = grad_kv[:, :128], grad_kv[:, 128:]
    d_key = unrotate(grad_k[:, None, :], cosine, sine_table)[:, 0, :].astype(jnp.bfloat16)
    d_value = grad_v.astype(jnp.bfloat16)
    d_proj_a = jnp.concatenate([d_query_a, d_key, d_value], 1)
    input_part = lax.dot_general(
        d_proj_a, full_a, (((1,), (1,)), ((), ())), preferred_element_type=jnp.float32
    )
    if first_heads < head_count:
        input_part = input_part + lax.dot_general(
            d_query_b, full_b, (((1,), (1,)), ((), ())), preferred_element_type=jnp.float32
        )
        late_proj = jnp.concatenate([d_query_b, d_key, d_value], 1)
    else:
        late_proj = jnp.concatenate([d_key, d_value], 1)
        early_sum = weight_grad(d_query_a)
    early_sum, input_part = lax.optimization_barrier((early_sum, input_part))
    input_cols = input_part.shape[1] // head_groups
    input_split = lax.all_to_all(
        input_part.astype(jnp.bfloat16).reshape(num_rows, head_groups, input_cols),
        "head", 1, 1, tiled=False,
    )
    grad_input = jnp.sum(input_split.astype(jnp.float32), axis=1).astype(jnp.bfloat16)
    late_sum = weight_grad(late_proj)
    query_w = jnp.concatenate([early_sum, late_sum[:, : query_cols - first_cols]], 1)
    rest = late_sum[:, query_cols - first_cols :]
    return (attended, grad_input, query_w, rest[:, :128], rest[:, 128:])


def solution(mesh):
    placed = (
        P(("dp", "ctx"), None),
        P(("dp", "ctx"), "head"),
        P(("dp", "ctx"), "head"),
        P(("dp", "ctx"), "head"),
        P("dp", None),
        P(("dp", "ctx"), "head"),
    )
    return jax.shard_map(
        local,
        mesh=mesh,
        in_specs=placed,
        out_specs=(
            P(("dp", "ctx"), "head"),
            P(("dp", "ctx"), "head"),
            P(("dp", "ctx"), "head"),
            P(("dp", "ctx"), "head"),
            P(("dp", "ctx"), "head"),
        ),
        check_vma=False,
    )
```

```python
import jax
import jax.numpy as jnp
from jax import lax
from jax.sharding import PartitionSpec as P

scale_factor = 128.0 ** (-0.5)
neg_large = -1e30


def rope_tables(positions):
    inverse = jnp.power(500000.0, -jnp.arange(64, dtype=jnp.float32) / 64.0)
    angles = positions.astype(jnp.float32)[:, None] * inverse[None, :]
    return (jnp.cos(angles)[:, None, :], jnp.sin(angles)[:, None, :])


def rotate(entries, cosine, sine_table):
    first_half = entries[..., :64]
    second_half = entries[..., 64:]
    return jnp.concatenate(
        [
            first_half * cosine - second_half * sine_table,
            second_half * cosine + first_half * sine_table,
        ],
        -1,
    )


def unrotate(entries, cosine, sine_table):
    first_half = entries[..., :64]
    second_half = entries[..., 64:]
    return jnp.concatenate(
        [
            first_half * cosine + second_half * sine_table,
            second_half * cosine - first_half * sine_table,
        ],
        -1,
    )


def segment_ids(length_row, positions):
    ends = jnp.cumsum(length_row)
    return jnp.sum((positions[:, None] >= ends[None, :]).astype(jnp.int32), 1)


def block_scores(query_blk, key_blk, query_pos, key_pos, query_seg, key_seg):
    scores = (
        jnp.einsum("rhd,kd->hrk", query_blk, key_blk, preferred_element_type=jnp.float32)
        * scale_factor
    )
    allowed = (key_pos[None, :] <= query_pos[:, None]) & (key_seg[None, :] == query_seg[:, None])
    return (scores, allowed[None])


def grad_block(
    query_blk,
    dout_blk,
    total_blk,
    delta_blk,
    key_blk,
    value_blk,
    query_pos,
    key_pos,
    query_seg,
    key_seg,
):
    scores, allowed = block_scores(query_blk, key_blk, query_pos, key_pos, query_seg, key_seg)
    prob_rows = jnp.where(
        allowed, jnp.exp(jnp.where(allowed, scores - total_blk[..., None], neg_large)), 0.0
    )
    prob_b = prob_rows.astype(jnp.bfloat16)
    d_prob = jnp.einsum("rhd,kd->hrk", dout_blk, value_blk, preferred_element_type=jnp.float32)
    d_score = (scale_factor * prob_rows * (d_prob - delta_blk[..., None])).astype(jnp.bfloat16)
    return (prob_b, d_score)


def attend_whole(query_rows, key_all, value_all, dout_rows, positions, all_pos, seg_own, seg_all):
    scores, allowed = block_scores(query_rows, key_all, positions, all_pos, seg_own, seg_all)
    masked = jnp.where(allowed, scores, neg_large)
    top_score = jnp.max(masked, -1)
    total = jnp.sum(jnp.where(allowed, jnp.exp(masked - top_score[..., None]), 0.0), -1)
    log_total = top_score + jnp.log(total)
    prob_rows = jnp.where(
        allowed, jnp.exp(jnp.where(allowed, scores - log_total[..., None], neg_large)), 0.0
    )
    prob_b = prob_rows.astype(jnp.bfloat16)
    out_rows = jnp.einsum(
        "hrk,kd->rhd", prob_b, value_all, preferred_element_type=jnp.float32
    ).astype(jnp.bfloat16)
    delta_rows = jnp.einsum("rhd,rhd->hr", dout_rows, out_rows, preferred_element_type=jnp.float32)
    d_prob = jnp.einsum("rhd,kd->hrk", dout_rows, value_all, preferred_element_type=jnp.float32)
    d_score = (scale_factor * prob_rows * (d_prob - delta_rows[..., None])).astype(jnp.bfloat16)
    grad_q = jnp.einsum("hrk,kd->rhd", d_score, key_all, preferred_element_type=jnp.float32)
    part_k = jnp.einsum("hrk,rhd->kd", d_score, query_rows, preferred_element_type=jnp.float32)
    part_v = jnp.einsum("hrk,rhd->kd", prob_b, dout_rows, preferred_element_type=jnp.float32)
    return out_rows, grad_q, part_k, part_v


def attend_blocked(query_rows, key_all, value_all, dout_rows, positions, all_pos, seg_own, seg_all, kblock):
    num_rows, head_count = query_rows.shape[0], query_rows.shape[1]
    seq_len = key_all.shape[0]
    causal_limit = (positions[-1] + kblock) // kblock
    key_first = jnp.int32(0)

    def take_block(block_index):
        first_row = block_index * kblock
        return (
            lax.dynamic_slice_in_dim(key_all, first_row, kblock, 0),
            lax.dynamic_slice_in_dim(value_all, first_row, kblock, 0),
            lax.dynamic_slice_in_dim(all_pos, first_row, kblock, 0),
            lax.dynamic_slice_in_dim(seg_all, first_row, kblock, 0),
        )

    def stats_step(block_index, carried):
        run_max, run_sum = carried
        key_blk, value_blk, key_pos, key_seg = take_block(block_index)
        scores, allowed = block_scores(query_rows, key_blk, positions, key_pos, seg_own, key_seg)
        masked = jnp.where(allowed, scores, neg_large)
        new_max = jnp.maximum(run_max, jnp.max(masked, -1))
        terms = jnp.where(allowed, jnp.exp(masked - new_max[..., None]), 0.0)
        return (new_max, run_sum * jnp.exp(run_max - new_max) + jnp.sum(terms, -1))

    start_stats = (
        jnp.full((head_count, num_rows), neg_large, jnp.float32),
        jnp.zeros((head_count, num_rows), jnp.float32),
    )
    run_max, run_sum = lax.fori_loop(key_first, causal_limit, stats_step, start_stats)
    log_total = run_max + jnp.log(run_sum)

    def output_step(block_index, carried):
        key_blk, value_blk, key_pos, key_seg = take_block(block_index)
        scores, allowed = block_scores(query_rows, key_blk, positions, key_pos, seg_own, key_seg)
        prob_b = jnp.where(
            allowed, jnp.exp(jnp.where(allowed, scores - log_total[..., None], neg_large)), 0.0
        ).astype(jnp.bfloat16)
        return carried + jnp.einsum(
            "hrk,kd->rhd", prob_b, value_blk, preferred_element_type=jnp.float32
        )

    out_sum = lax.fori_loop(
        key_first, causal_limit, output_step, jnp.zeros((num_rows, head_count, 128), jnp.float32)
    )
    out_rows = out_sum.astype(jnp.bfloat16)
    delta_rows = jnp.einsum("rhd,rhd->hr", dout_rows, out_rows, preferred_element_type=jnp.float32)

    def sums_step(block_index, carried):
        grad_q, part_k, part_v = carried
        first_row = block_index * kblock
        key_blk, value_blk, key_pos, key_seg = take_block(block_index)
        prob_b, d_score = grad_block(
            query_rows, dout_rows, log_total, delta_rows, key_blk, value_blk,
            positions, key_pos, seg_own, key_seg,
        )
        grad_q = grad_q + jnp.einsum(
            "hrk,kd->rhd", d_score, key_blk, preferred_element_type=jnp.float32
        )
        block_k = jnp.einsum("hrk,rhd->kd", d_score, query_rows, preferred_element_type=jnp.float32)
        block_v = jnp.einsum("hrk,rhd->kd", prob_b, dout_rows, preferred_element_type=jnp.float32)
        part_k = lax.dynamic_update_slice_in_dim(
            part_k, lax.dynamic_slice_in_dim(part_k, first_row, kblock, 0) + block_k, first_row, 0
        )
        part_v = lax.dynamic_update_slice_in_dim(
            part_v, lax.dynamic_slice_in_dim(part_v, first_row, kblock, 0) + block_v, first_row, 0
        )
        return (grad_q, part_k, part_v)

    start_sums = (
        jnp.zeros((num_rows, head_count, 128), jnp.float32),
        jnp.zeros((seq_len, 128), jnp.float32),
        jnp.zeros((seq_len, 128), jnp.float32),
    )
    grad_q, part_k, part_v = lax.fori_loop(key_first, causal_limit, sums_step, start_sums)
    return out_rows, grad_q, part_k, part_v


def attend(query_rows, key_all, value_all, dout_rows, positions, all_pos, seg_own, seg_all):
    head_count, num_rows, seq_len = query_rows.shape[1], query_rows.shape[0], key_all.shape[0]
    operands = (query_rows, key_all, value_all, dout_rows, positions, all_pos, seg_own, seg_all)
    if head_count * num_rows * seq_len <= (1 << 22):
        return attend_whole(*operands)
    kblock = seq_len
    while head_count * num_rows * kblock > (1 << 21) and kblock % 256 == 0:
        kblock //= 2
    return attend_blocked(*operands, kblock)


def local(hidden_in, w_query, w_key, w_value, lengths, attn_grad):
    num_rows = hidden_in.shape[0]
    head_count = w_query.shape[1] // 128
    first_heads = head_count // 2 if head_count % 2 == 0 else head_count
    first_cols = first_heads * 128
    query_cols = head_count * 128
    start_row = lax.axis_index("ctx") * num_rows
    seq_len = num_rows * lax.axis_size("ctx")
    positions = start_row + jnp.arange(num_rows, dtype=jnp.int32)
    all_pos = jnp.arange(seq_len, dtype=jnp.int32)
    seg_all = segment_ids(lengths[0], all_pos)
    seg_own = lax.dynamic_slice_in_dim(seg_all, start_row, num_rows)
    cosine, sine_table = rope_tables(positions)
    rows_axes = ("dp", "ctx")
    group_count = lax.axis_size(rows_axes)
    head_groups = lax.axis_size("head")
    local_a = jnp.concatenate([w_query[:, :first_cols], w_key, w_value], 1)
    full_a = lax.all_gather(local_a, rows_axes, axis=0, tiled=True)
    split_rows = num_rows % head_groups == 0
    dp_count, ctx_count = lax.axis_size("dp"), lax.axis_size("ctx")
    ctx_index = lax.axis_index("ctx")
    if split_rows:
        quarter = num_rows // head_groups
        own_rows = lax.dynamic_slice_in_dim(hidden_in, lax.axis_index("head") * quarter, quarter, 0)
        own_rows, full_a = lax.optimization_barrier((own_rows, full_a))
        cols_part = lax.all_to_all(own_rows, "dp", 1, 0, tiled=True)
    else:
        cols_part = lax.all_to_all(hidden_in, "dp", 1, 0, tiled=True)
    full_a, w_query = lax.optimization_barrier((full_a, w_query))
    hidden_cols = cols_part
    if split_rows:
        spread = jnp.broadcast_to(cols_part[None], (head_groups,) + cols_part.shape)
        cols_all = lax.all_to_all(spread, "head", 0, 0, tiled=False)
        hidden_cols = (
            cols_all.reshape(head_groups, dp_count, quarter, -1)
            .transpose(1, 0, 2, 3)
            .reshape(dp_count * num_rows, -1)
        )
    weight_rows = w_query.shape[0]

    def weight_grad(d_rows, gathered=None):
        if gathered is None:
            gathered = lax.all_gather(d_rows, "dp", axis=0, tiled=True)
        partial = lax.dot_general(
            hidden_cols, gathered, (((0,), (0,)), ((), ())), preferred_element_type=jnp.float32
        )
        if ctx_count == 2:
            own_part = lax.dynamic_slice_in_dim(partial, ctx_index * weight_rows, weight_rows, 0)
            away_part = lax.dynamic_slice_in_dim(
                partial, (1 - ctx_index) * weight_rows, weight_rows, 0
            )
            sent = lax.ppermute(away_part.astype(jnp.bfloat16), "ctx", [(0, 1), (1, 0)])
            return own_part + sent.astype(jnp.float32)
        return lax.psum_scatter(partial, "ctx", scatter_dimension=0, tiled=True)

    proj_a = jnp.dot(hidden_in, full_a, preferred_element_type=jnp.float32)
    query_a = rotate(
        proj_a[:, :first_cols].reshape(num_rows, first_heads, 128), cosine, sine_table
    ).astype(jnp.bfloat16)
    key_rows = rotate(
        proj_a[:, first_cols : first_cols + 128].reshape(num_rows, 1, 128), cosine, sine_table
    )[:, 0, :].astype(jnp.bfloat16)
    value_rows = proj_a[:, first_cols + 128 :].astype(jnp.bfloat16)
    kv_rows = jnp.concatenate([key_rows, value_rows], 1)
    if ctx_count == 2:
        kv_other = lax.ppermute(kv_rows, "ctx", [(0, 1), (1, 0)])
        kv_all = jnp.where(
            ctx_index == 0,
            jnp.concatenate([kv_rows, kv_other], 0),
            jnp.concatenate([kv_other, kv_rows], 0),
        )
    else:
        kv_all = lax.all_gather(kv_rows, "ctx", axis=0, tiled=True)
    key_all, value_all = kv_all[:, :128], kv_all[:, 128:]
    dout_rows = attn_grad.reshape(num_rows, head_count, 128)
    shared = (key_all, value_all)
    masks = (positions, all_pos, seg_own, seg_all)
    out_a, grad_qa, part_k, part_v = attend(query_a, *shared, dout_rows[:, :first_heads], *masks)
    d_query_a = unrotate(grad_qa, cosine, sine_table).astype(jnp.bfloat16).reshape(num_rows, -1)
    out_parts, d_query_parts = [out_a], [d_query_a]
    if first_heads < head_count:
        w_rest = w_query[:, first_cols:]
        full_b = lax.all_gather(w_rest, rows_axes, axis=0, tiled=True)
        d_query_a, full_b = lax.optimization_barrier((d_query_a, full_b))
        early_all = lax.all_gather(d_query_a, "dp", axis=0, tiled=True)
        proj_b = jnp.dot(hidden_in, full_b, preferred_element_type=jnp.float32)
        query_b = rotate(
            proj_b.reshape(num_rows, head_count - first_heads, 128), cosine, sine_table
        ).astype(jnp.bfloat16)
        out_b, grad_qb, part_kb, part_vb = attend(
            query_b, *shared, dout_rows[:, first_heads:], *masks
        )
        early_all, grad_qb = lax.optimization_barrier((early_all, grad_qb))
        early_sum = weight_grad(d_query_a, early_all)
        d_query_b = unrotate(grad_qb, cosine, sine_table).astype(jnp.bfloat16).reshape(num_rows, -1)
        part_k, part_v = part_k + part_kb, part_v + part_vb
        out_parts.append(out_b)
    attended = jnp.concatenate(out_parts, 1).reshape(num_rows, query_cols)
    parts_kv = jnp.concatenate([part_k, part_v], 1)
    if ctx_count == 2:
        own_part = lax.dynamic_slice_in_dim(parts_kv, ctx_index * num_rows, num_rows, 0)
        away_part = lax.dynamic_slice_in_dim(parts_kv, (1 - ctx_index) * num_rows, num_rows, 0)
        got_part = lax.ppermute(away_part.astype(jnp.bfloat16), "ctx", [(0, 1), (1, 0)])
        grad_kv = own_part + got_part.astype(jnp.float32)
    else:
        grad_kv = lax.psum_scatter(parts_kv, "ctx", scatter_dimension=0, tiled=True)
    grad_k, grad_v = grad_kv[:, :128], grad_kv[:, 128:]
    d_key = unrotate(grad_k[:, None, :], cosine, sine_table)[:, 0, :].astype(jnp.bfloat16)
    d_value = grad_v.astype(jnp.bfloat16)
    d_proj_a = jnp.concatenate([d_query_a, d_key, d_value], 1)
    input_part = lax.dot_general(
        d_proj_a, full_a, (((1,), (1,)), ((), ())), preferred_element_type=jnp.float32
    )
    if first_heads < head_count:
        input_part = input_part + lax.dot_general(
            d_query_b, full_b, (((1,), (1,)), ((), ())), preferred_element_type=jnp.float32
        )
        late_proj = jnp.concatenate([d_query_b, d_key, d_value], 1)
    else:
        late_proj = jnp.concatenate([d_key, d_value], 1)
        early_sum = weight_grad(d_query_a)
    early_sum, input_part = lax.optimization_barrier((early_sum, input_part))
    input_cols = input_part.shape[1] // head_groups
    input_split = lax.all_to_all(
        input_part.astype(jnp.bfloat16).reshape(num_rows, head_groups, input_cols),
        "head", 1, 1, tiled=False,
    )
    grad_input = jnp.sum(input_split.astype(jnp.float32), axis=1).astype(jnp.bfloat16)
    late_sum = weight_grad(late_proj)
    query_w = jnp.concatenate([early_sum, late_sum[:, : query_cols - first_cols]], 1)
    rest = late_sum[:, query_cols - first_cols :]
    return (attended, grad_input, query_w, rest[:, :128], rest[:, 128:])


def solution(mesh):
    placed = (
        P(("dp", "ctx"), None),
        P(("dp", "ctx"), "head"),
        P(("dp", "ctx"), "head"),
        P(("dp", "ctx"), "head"),
        P("dp", None),
        P(("dp", "ctx"), "head"),
    )
    return jax.shard_map(
        local,
        mesh=mesh,
        in_specs=placed,
        out_specs=(
            P(("dp", "ctx"), "head"),
            P(("dp", "ctx"), "head"),
            P(("dp", "ctx"), "head"),
            P(("dp", "ctx"), "head"),
            P(("dp", "ctx"), "head"),
        ),
        check_vma=False,
    )
```
